512 devices in a mesh: seq: 128 (over y_hi, z, x), head: 4 (over y_lo, core).
Axes of the slice: x: 4, y: 4 (y_hi: 2, y_lo: 2; y = y_hi * 2 + y_lo), z: 16, core: 2. Of those that a mesh axis runs over, the one named last changes fastest.
Arguments:
- single: bfloat16 [16384, 384], P('seq'), may hold values from -6 to 6
- atoms: bfloat16 [131072, 128], P('seq'), may hold values from -6 to 6
- gain_single: float32 [384], replicated, may hold values from 0.25 to 1.75
- gain_atom: float32 [128], replicated, may hold values from 0.25 to 1.75
- w_token: bfloat16 [4, 384, 384], P(None, None, 'head'), may hold values from -0.3125 to 0.3125
- w_token_out: bfloat16 [384, 384], P('head'), may hold values from -0.3125 to 0.3125
- w_cond: bfloat16 [384, 128], replicated, may hold values from -0.3125 to 0.3125
- w_atom: bfloat16 [4, 128, 128], P(None, None, 'head'), may hold values from -0.5 to 0.5
- w_atom_out: bfloat16 [128, 128], P('head'), may hold values from -0.5 to 0.5
- pair_bias: bfloat16 [16, 16384, 512], P('head', 'seq'), may hold values from -6 to 300
- atom_bias: bfloat16 [4, 131072, 128], P('head', 'seq'), may hold values from -6 to 300
- used_blocks: int32 [128, 4], P('seq'), may hold values from 0 to 127, as said below
- used_count: int32 [128], P('seq'), may hold values from 1 to 4, as said below
- atom_counts: int32 [128, 128], P('seq'), may hold values from 1 to 24, 1024 in all within a row
- key_offset: int32 [4096], P('seq'), may hold values from -64 to -32
- grad_token: bfloat16 [16384, 384], P('seq'), may hold values from -6 to 6
- grad_atom: bfloat16 [131072, 128], P('seq'), may hold values from -6 to 6
Outputs:
- token_out: bfloat16 [16384, 384], P('seq')
- atom_out: bfloat16 [131072, 128], P('seq')
- grad_single: bfloat16 [16384, 384], P('seq')
- grad_atoms: bfloat16 [131072, 128], P('seq')
- grad_pair_bias: bfloat16 [16, 16384, 512], P('head', 'seq')
- grad_atom_bias: bfloat16 [4, 131072, 128], P('head', 'seq')
The draws below stay inside these ranges and needn't reach their ends.
Inputs may be any that keep to these rules, and one draw needn't show every extreme that they name: `used_blocks`: for query block b the first used_count[b] entries are distinct key blocks whose shard (block) lies at most 2 shards from b's shard around the loop of 128 shards; the other entries equal b. `used_count`: some query block lists 4 key blocks. `atom_counts`: each row sums to 1024.
All inputs are finite; a program needn't handle non-finite values.
Results may differ from the reference program's by a relative error of at most 0.025.
Values may be sent and summed in bfloat16 or wider, within the bound.
No kernel may reach another device: no remote copies, remote signals or barrier semaphores. Data moves between devices by JAX's collectives and lax.ppermute only.
A program may use at most 64 MiB of HBM per device.

```python
import math
import jax
import jax.numpy as jnp
import numpy as np
from jax import lax

C = 384
H = 16
DH = 24
CA = 128
HA = 4
DA = 32
BLK = 128
S = 4
WIN = 2
TOK_DEV = 128
ATOM_DEV = 1024
AMOST = 24
AQ = 32
AK = 128
SHARDS = 128
TOKENS = 16384
NB = 128
QB = 1
SK = 512
ATOMS = 131072
WINDOWS = 4096


def spiked(key, heads, rows, columns):
    key_base = jax.random.fold_in(key, 0)
    baseline = jnp.clip(1.5 * jax.random.normal(key_base, (heads, rows, columns)), -6.0, 6.0)
    return baseline.astype(jnp.bfloat16)


def draw_pair_bias(key, part):
    return spiked(key, H, TOKENS, S * BLK)


def draw_atom_bias(key, part):
    return spiked(key, HA, ATOMS, AK)


def block_lists(key):
    key_order, key_count, key_force = jax.random.split(jax.random.fold_in(key, 11), 3)
    candidates = (2 * WIN + 1) * QB
    rank_keys = jax.random.randint(key_order, (NB, candidates), 0, 1048576) * candidates + jnp.arange(candidates)
    ordering = jnp.argsort(rank_keys, axis=1, stable=True)[:, :S]
    block_ids = jnp.arange(NB)
    owner_dev = (block_ids // QB)[:, None] + ordering // QB - WIN
    chosen_ids = jnp.mod(owner_dev, SHARDS) * QB + ordering % QB
    counts = jax.random.randint(key_count, (NB,), 1, S + 1)
    forced = jax.random.randint(key_force, (), 0, NB)
    counts = jnp.where(block_ids == forced, S, counts)
    block_list = jnp.where(jnp.arange(S)[None, :] < counts[:, None], chosen_ids, block_ids[:, None])
    return (block_list.astype(jnp.int32), counts.astype(jnp.int32))


def draw_used_blocks(key, part):
    return block_lists(key)[0]


def draw_used_count(key, part):
    return block_lists(key)[1]


def touch_ends(drawn, own_key, least, largest):
    index_at = [jax.random.randint(jax.random.fold_in(own_key, axis), (), 0, length) for axis, length in enumerate(drawn.shape)]
    widest = drawn.shape.index(max(drawn.shape))
    next_to = index_at[:widest] + [(index_at[widest] + 1) % drawn.shape[widest]] + index_at[widest + 1:]
    return drawn.at[tuple(index_at)].set(least).at[tuple(next_to)].set(largest)


def shard_levels(own_key, extent, cuts, low, high):
    loudness = 1.0
    for dim, parts in cuts:
        draws = jax.random.uniform(jax.random.fold_in(jax.random.fold_in(own_key, 6), dim), (parts,), jnp.float32, low / len(cuts), high / len(cuts))
        loudness = loudness * jnp.repeat(jnp.exp(draws), extent[dim] // parts).reshape((-1,) + (1,) * (len(extent) - 1 - dim))
    return loudness


def profile(number_of, total, reach, lean):
    loads = [(1 << 20) // math.isqrt(grade ** lean) + 1 for grade in range(2, number_of + 1)]
    surplus, holding = total - reach - (number_of - 1), [1] * (number_of - 1)
    while surplus > 0:
        free = [i for i in range(number_of - 1) if holding[i] < reach]
        pool, budget = sum([loads[i] for i in free]), surplus
        for i in free:
            more = min(reach - holding[i], max(1, budget * loads[i] // pool), surplus)
            holding[i] = holding[i] + more
            surplus = surplus - more
    return np.array([reach] + holding)


def ragged_sizes(stream_key, number_of, total, limit, lean):
    if number_of == 2:
        one = jax.random.randint(stream_key, (), max(1, total - limit), min(limit, total - 1) + 1)
        return jnp.stack([one, total - one])
    lengths = jnp.asarray(profile(number_of, total, limit, lean), jnp.int32)
    pairs = (number_of - 1) // 2
    donor, sink = lengths[1:1 + 2 * pairs:2], lengths[2:2 + 2 * pairs:2]
    margin = jnp.minimum(donor - 1, limit - sink)
    passed = jax.random.randint(jax.random.fold_in(stream_key, 1), (pairs,), 0, 1 << 20) % (margin + 1)
    lengths = lengths.at[1:1 + 2 * pairs:2].set(donor - passed).at[2:2 + 2 * pairs:2].set(sink + passed)
    return lengths[jax.random.permutation(jax.random.fold_in(stream_key, 2), number_of)]


def normal_values(key, dims, spread, limit, shards=(), kind=jnp.bfloat16):
    entries = jax.random.normal(key, dims, jnp.float32) * spread
    if len(shards) > 0:
        entries = shard_levels(key, dims, shards, -0.22, 0.18) * entries
    return jnp.clip(entries, min=-limit, max=limit).astype(kind)


def setup_inputs(seed: int = 0) -> dict:
    key_of = jax.random.split(jax.random.key(seed), 18)
    return {
        "single": normal_values(key_of[0], (TOKENS, C), 1.0, 6.0, ((0, 128),)),
        "atoms": normal_values(key_of[1], (ATOMS, CA), 1.0, 6.0, ((0, 128),)),
        "gain_single": jnp.clip(1.0 + 0.15 * jax.random.normal(key_of[2], (C,), jnp.float32), 0.25, 1.75),
        "gain_atom": jnp.clip(1.0 + 0.15 * jax.random.normal(key_of[3], (CA,), jnp.float32), 0.25, 1.75),
        "w_token": normal_values(key_of[4], (4, C, H * DH), C ** -0.5, 0.3125, ((2, 4),)),
        "w_token_out": normal_values(key_of[5], (H * DH, C), (H * DH) ** -0.5, 0.3125, ((0, 4),)),
        "w_cond": normal_values(key_of[6], (C, CA), C ** -0.5, 0.3125),
        "w_atom": normal_values(key_of[7], (4, CA, HA * DA), CA ** -0.5, 0.5, ((2, 4),)),
        "w_atom_out": normal_values(key_of[8], (HA * DA, CA), (HA * DA) ** -0.5, 0.5, ((0, 4),)),
        "pair_bias": draw_pair_bias(jax.random.fold_in(key_of[17], 71), 0),
        "atom_bias": draw_atom_bias(jax.random.fold_in(key_of[17], 71), 0),
        "used_blocks": draw_used_blocks(jax.random.fold_in(key_of[17], 71), 0),
        "used_count": draw_used_count(jax.random.fold_in(key_of[17], 71), 0),
        "atom_counts": jax.vmap(lambda own: ragged_sizes(own, TOK_DEV, ATOM_DEV, AMOST, 2))(jax.random.split(key_of[13], SHARDS)).reshape((SHARDS, TOK_DEV)).astype(jnp.int32),
        "key_offset": touch_ends(jax.random.randint(key_of[14], (WINDOWS,), 0 - AK // 2, AQ + 1 - AK // 2), jax.random.fold_in(key_of[14], 1), 0 - AK // 2, (AQ + 1 - AK // 2) - 1).astype(jnp.int32),
        "grad_token": normal_values(key_of[15], (TOKENS, C), 1.0, 6.0, ((0, 128),)),
        "grad_atom": normal_values(key_of[16], (ATOMS, CA), 1.0, 6.0, ((0, 128),)),
    }


EPSILON = 1e-05
HIGHEST = lax.Precision.HIGHEST

def norm_rows(inputs, gains):
    row_mean = lax.optimization_barrier(jnp.mean(inputs, axis=-1, keepdims=True))
    centred = inputs - row_mean
    variance = lax.optimization_barrier(jnp.mean(centred * centred, axis=-1, keepdims=True))
    return centred * lax.rsqrt(variance + EPSILON) * gains

def norm_back(inputs, gains, cotangent):
    row_mean = lax.optimization_barrier(jnp.mean(inputs, axis=-1, keepdims=True))
    centred = inputs - row_mean
    variance = lax.optimization_barrier(jnp.mean(centred * centred, axis=-1, keepdims=True))
    inverse = lax.rsqrt(variance + EPSILON)
    standard = centred * inverse
    scaled = cotangent * gains
    return inverse * (scaled - lax.optimization_barrier(jnp.mean(scaled, axis=-1, keepdims=True)) - standard * lax.optimization_barrier(jnp.mean(scaled * standard, axis=-1, keepdims=True)))

def to_low(values_in):
    return lax.optimization_barrier(values_in.astype(jnp.bfloat16)).astype(jnp.float32)

def attend(queries, key_block, value_block, bias_block, valid_keys, scaling):
    scores = jnp.einsum('bqhd,bkhd->bhqk', queries.astype(jnp.float32), key_block.astype(jnp.float32)) * scaling + bias_block
    scores = jnp.where(valid_keys[:, None, None, :], scores, -jnp.inf)
    row_max = lax.optimization_barrier(jnp.max(scores, axis=-1, keepdims=True))
    exponent = jnp.exp(scores - row_max)
    weights = exponent / lax.optimization_barrier(jnp.sum(exponent, axis=-1, keepdims=True))
    attended = jnp.einsum('bhqk,bkhd->bqhd', to_low(weights), value_block.astype(jnp.float32))
    return (weights, attended)

def attend_back(weights, queries, key_block, value_block, grad_out, row_delta, scaling):
    grad_low = grad_out.astype(jnp.float32)
    weight_grad = jnp.einsum('bqhd,bkhd->bhqk', grad_low, value_block.astype(jnp.float32))
    dscore = weights * (weight_grad - row_delta[..., None])
    dscore_low = to_low(dscore)
    dquery = jnp.einsum('bhqk,bkhd->bqhd', dscore_low, key_block.astype(jnp.float32)) * scaling
    key_grad = jnp.einsum('bhqk,bqhd->bkhd', dscore_low, queries.astype(jnp.float32)) * scaling
    dvalue = jnp.einsum('bhqk,bqhd->bkhd', to_low(weights), grad_low)
    return (dscore, dquery, key_grad, dvalue)

def reference(single, atoms, gain_single, gain_atom, w_token, w_token_out, w_cond, w_atom, w_atom_out, pair_bias, atom_bias, used_blocks, used_count, atom_counts, key_offset, grad_token, grad_atom):
    features = H * DH
    atom_feat = HA * DA
    scaling = DH ** (-0.5)
    atom_scaling = DA ** (-0.5)
    offsets = jnp.arange(BLK, dtype=jnp.int32)
    normed_low = norm_rows(single.astype(jnp.float32), gain_single).astype(jnp.bfloat16)
    projected = [jnp.dot(normed_low, w_token[which], preferred_element_type=jnp.float32) for which in range(4)]
    queries = projected[0].astype(jnp.bfloat16).reshape(TOKENS, H, DH)
    key_all = projected[1].astype(jnp.bfloat16).reshape(TOKENS, H, DH)
    value_all = projected[2].astype(jnp.bfloat16).reshape(TOKENS, H, DH)
    gate_act = jax.nn.sigmoid(projected[3])

    def fetch(block):
        first_row = block * BLK
        query_block = lax.dynamic_slice_in_dim(queries, first_row, BLK, 0)
        key_rows = (used_blocks[block][:, None] * BLK + offsets[None, :]).reshape(SK).astype(jnp.int32)
        key_block = key_all[key_rows]
        value_block = value_all[key_rows]
        bias_block = lax.dynamic_slice_in_dim(pair_bias, first_row, BLK, 1).astype(jnp.float32)
        valid_keys = jnp.repeat(jnp.arange(S, dtype=jnp.int32) < used_count[block], BLK)
        weights, attended = attend(query_block[None], key_block[None], value_block[None], bias_block[None], valid_keys[None], scaling)
        return (key_rows, query_block, key_block, value_block, weights, attended[0])
    block_ids = jnp.arange(NB, dtype=jnp.int32)
    attended = lax.map(lambda block: fetch(block)[5], block_ids).reshape(TOKENS, features)
    token_out = jnp.dot((attended * gate_act).astype(jnp.bfloat16), w_token_out, preferred_element_type=jnp.float32).astype(jnp.bfloat16)
    grad_gated = jnp.dot(grad_token, w_token_out.T, preferred_element_type=jnp.float32)
    grad_attended = (grad_gated * gate_act).astype(jnp.bfloat16)
    grad_gate = (grad_gated * attended * gate_act * (1.0 - gate_act)).astype(jnp.bfloat16)
    row_delta = lax.optimization_barrier(jnp.sum((grad_attended.astype(jnp.float32) * attended).reshape(TOKENS, H, DH), axis=-1))
    grad_heads = grad_attended.reshape(TOKENS, H, DH)

    def token_back(carry, block):
        key_rows, query_block, key_block, value_block, weights, unused_out = fetch(block)
        grad_block = lax.dynamic_slice_in_dim(grad_heads, block * BLK, BLK, 0)
        delta_block = lax.dynamic_slice_in_dim(row_delta, block * BLK, BLK, 0).T
        dscore, dquery, key_grad, dvalue = attend_back(weights, query_block[None], key_block[None], value_block[None], grad_block[None], delta_block[None], scaling)
        carry = (carry[0].at[key_rows].add(key_grad[0]), carry[1].at[key_rows].add(dvalue[0]))
        return (carry, (dscore[0].astype(jnp.bfloat16), dquery[0]))
    zeros_tok = jnp.zeros((TOKENS, H, DH), jnp.float32)
    (key_total, value_total), (score_grads, query_grads) = lax.scan(token_back, (zeros_tok, zeros_tok), block_ids)
    grad_pair_bias = score_grads.transpose(1, 0, 2, 3).reshape(H, TOKENS, SK)
    token_grads = [query_grads.reshape(TOKENS, features).astype(jnp.bfloat16), key_total.reshape(TOKENS, features).astype(jnp.bfloat16), value_total.reshape(TOKENS, features).astype(jnp.bfloat16), grad_gate]
    grad_normed = jnp.dot(token_grads[0], w_token[0].T, preferred_element_type=jnp.float32)
    for which in range(1, 4):
        grad_normed = grad_normed + jnp.dot(token_grads[which], w_token[which].T, preferred_element_type=jnp.float32)
    normed_atoms = norm_rows(atoms.astype(jnp.float32), gain_atom)
    ends = jnp.cumsum(atom_counts, axis=1).astype(jnp.int32)
    atom_index = jnp.arange(ATOM_DEV, dtype=jnp.int32)
    token_local = lax.optimization_barrier(jnp.sum((ends[:, None, :] <= atom_index[None, :, None]).astype(jnp.int32), axis=2)).astype(jnp.int32)
    atom_token = (token_local + jnp.arange(SHARDS, dtype=jnp.int32)[:, None] * TOK_DEV).reshape(ATOMS).astype(jnp.int32)
    condition = jnp.dot(normed_low, w_cond, preferred_element_type=jnp.float32)
    atom_input = (normed_atoms + condition[atom_token]).astype(jnp.bfloat16)
    atom_proj = [jnp.dot(atom_input, w_atom[which], preferred_element_type=jnp.float32) for which in range(4)]
    atom_queries = atom_proj[0].astype(jnp.bfloat16).reshape(ATOMS, HA, DA)
    atom_keys = atom_proj[1].astype(jnp.bfloat16).reshape(ATOMS, HA, DA)
    atom_values = atom_proj[2].astype(jnp.bfloat16).reshape(ATOMS, HA, DA)
    atom_gate = jax.nn.sigmoid(atom_proj[3])
    per_group = ATOM_DEV // AQ
    window_pos = jnp.arange(AK, dtype=jnp.int32)

    def atom_fetch(group):
        first_window = group * per_group
        window_ids = first_window + jnp.arange(per_group, dtype=jnp.int32)
        starts = lax.dynamic_slice_in_dim(key_offset, first_window, per_group, 0)
        key_rows = jnp.mod((window_ids * AQ + starts)[:, None] + window_pos[None, :], ATOMS).astype(jnp.int32)
        query_block = lax.dynamic_slice_in_dim(atom_queries, group * ATOM_DEV, ATOM_DEV, 0).reshape(per_group, AQ, HA, DA)
        key_block = atom_keys[key_rows]
        value_block = atom_values[key_rows]
        bias_block = lax.dynamic_slice_in_dim(atom_bias, group * ATOM_DEV, ATOM_DEV, 1).reshape(HA, per_group, AQ, AK).transpose(1, 0, 2, 3).astype(jnp.float32)
        valid_keys = jnp.ones((per_group, AK), dtype=bool)
        weights, attended = attend(query_block, key_block, value_block, bias_block, valid_keys, atom_scaling)
        return (key_rows, query_block, key_block, value_block, weights, attended)
    group_ids = jnp.arange(SHARDS, dtype=jnp.int32)
    atom_attended = lax.map(lambda group: atom_fetch(group)[5], group_ids).reshape(ATOMS, atom_feat)
    atom_out = jnp.dot((atom_attended * atom_gate).astype(jnp.bfloat16), w_atom_out, preferred_element_type=jnp.float32).astype(jnp.bfloat16)
    agrad_gated = jnp.dot(grad_atom, w_atom_out.T, preferred_element_type=jnp.float32)
    agrad_attended = (agrad_gated * atom_gate).astype(jnp.bfloat16)
    agrad_gate = (agrad_gated * atom_attended * atom_gate * (1.0 - atom_gate)).astype(jnp.bfloat16)
    atom_delta = lax.optimization_barrier(jnp.sum((agrad_attended.astype(jnp.float32) * atom_attended).reshape(ATOMS, HA, DA), axis=-1))
    agrad_heads = agrad_attended.reshape(ATOMS, HA, DA)

    def atom_back(carry, group):
        key_rows, query_block, key_block, value_block, weights, unused_out = atom_fetch(group)
        grad_block = lax.dynamic_slice_in_dim(agrad_heads, group * ATOM_DEV, ATOM_DEV, 0).reshape(per_group, AQ, HA, DA)
        delta_block = lax.dynamic_slice_in_dim(atom_delta, group * ATOM_DEV, ATOM_DEV, 0).reshape(per_group, AQ, HA).transpose(0, 2, 1)
        dscore, dquery, key_grad, dvalue = attend_back(weights, query_block, key_block, value_block, grad_block, delta_block, atom_scaling)
        flat_rows = key_rows.reshape(per_group * AK)
        carry = (carry[0].at[flat_rows].add(key_grad.reshape(per_group * AK, HA, DA)), carry[1].at[flat_rows].add(dvalue.reshape(per_group * AK, HA, DA)))
        return (carry, (dscore.astype(jnp.bfloat16), dquery))
    zeros_atom = jnp.zeros((ATOMS, HA, DA), jnp.float32)
    (akey_total, avalue_total), (ascore_grads, aquery_grads) = lax.scan(atom_back, (zeros_atom, zeros_atom), group_ids)
    grad_atom_bias = ascore_grads.transpose(2, 0, 1, 3, 4).reshape(HA, ATOMS, AK)
    atom_grads = [aquery_grads.reshape(ATOMS, atom_feat).astype(jnp.bfloat16), akey_total.reshape(ATOMS, atom_feat).astype(jnp.bfloat16), avalue_total.reshape(ATOMS, atom_feat).astype(jnp.bfloat16), agrad_gate]
    agrad_input = jnp.dot(atom_grads[0], w_atom[0].T, preferred_element_type=jnp.float32)
    for which in range(1, 4):
        agrad_input = agrad_input + jnp.dot(atom_grads[which], w_atom[which].T, preferred_element_type=jnp.float32)
    grad_atoms = norm_back(atoms.astype(jnp.float32), gain_atom, agrad_input).astype(jnp.bfloat16)
    cond_grad = jax.ops.segment_sum(agrad_input, atom_token, num_segments=TOKENS)
    grad_normed = grad_normed + jnp.dot(cond_grad, w_cond.astype(jnp.float32).T, precision=HIGHEST)
    grad_single = norm_back(single.astype(jnp.float32), gain_single, grad_normed).astype(jnp.bfloat16)
    return (token_out, atom_out, grad_single, grad_atoms, grad_pair_bias, grad_atom_bias)
```

```python
import jax
import jax.numpy as jnp
from jax import lax
from jax.sharding import PartitionSpec as P

DH = 24
DA = 32
BLK = 128
S = 4
WIN = 2
AQ = 32
AK = 128


EPSILON = 1e-05
HIGHEST = lax.Precision.HIGHEST


def shifted(block, axis, distance):
    devices = range(lax.axis_size(axis))
    route = [((i - distance) % len(devices), i) for i in devices]
    return lax.ppermute(block, axis, route)


def extended_2(block, sides, width):
    for axis, dim in sides:
        count = lax.axis_size(axis)
        forward = [(i, i + 1) for i in range(count - 1)]
        forward.append((count - 1, 0))
        backward = [(target, source) for source, target in forward]
        low = lax.ppermute(
            lax.slice_in_dim(block, block.shape[dim] - width, None, axis=dim), axis, forward
        )
        high = lax.ppermute(lax.slice_in_dim(block, 0, width, axis=dim), axis, backward)
        block = jnp.concatenate([low, block, high], axis=dim)
    return block


def head_sum(parts, axis):
    count = lax.axis_size(axis)
    if count != 4:
        return [lax.psum(p.astype(jnp.bfloat16), axis) for p in parts]
    pieces = []
    for part in parts:
        for col in range(part.shape[1] // 128):
            pieces.append(part[:, col * 128 : (col + 1) * 128])
    buf = jnp.concatenate(pieces, axis=0)
    rows = buf.shape[0]
    place = lax.axis_index(axis)
    low_bit = place % 2
    high_bit = (place // 2) % 2
    pair_near = [(i, i ^ 1) for i in range(count)]
    pair_far = [(i, i ^ 2) for i in range(count)]
    halves = buf.reshape(2, rows // 2, 128)
    keep = jnp.where(low_bit == 0, halves[0], halves[1])
    give = jnp.where(low_bit == 0, halves[1], halves[0])
    got = lax.ppermute(give.astype(jnp.bfloat16), axis, pair_near)
    summed = (keep + got.astype(jnp.float32)).reshape(2, rows // 4, 128)
    keep = jnp.where(high_bit == 0, summed[0], summed[1])
    give = jnp.where(high_bit == 0, summed[1], summed[0])
    got = lax.ppermute(give.astype(jnp.bfloat16), axis, pair_far)
    own = (keep + got.astype(jnp.float32)).astype(jnp.bfloat16)
    got = lax.ppermute(own, axis, pair_far)
    half = jnp.where(
        high_bit == 0, jnp.concatenate([own, got], axis=0), jnp.concatenate([got, own], axis=0)
    )
    got = lax.ppermute(half, axis, pair_near)
    full = jnp.where(
        low_bit == 0, jnp.concatenate([half, got], axis=0), jnp.concatenate([got, half], axis=0)
    )
    outs = []
    start = 0
    for part in parts:
        width = part.shape[1] // 128
        rows_here = part.shape[0]
        cols = [full[start + k * rows_here : start + (k + 1) * rows_here] for k in range(width)]
        start += width * rows_here
        outs.append(jnp.concatenate(cols, axis=1) if width > 1 else cols[0])
    return outs


def norm_rows(inputs, gains):
    row_mean = jnp.mean(inputs, axis=-1, keepdims=True)
    centred = inputs - row_mean
    variance = jnp.mean(centred * centred, axis=-1, keepdims=True)
    return centred * lax.rsqrt(variance + EPSILON) * gains


def norm_back(inputs, gains, cotangent):
    row_mean = jnp.mean(inputs, axis=-1, keepdims=True)
    centred = inputs - row_mean
    variance = jnp.mean(centred * centred, axis=-1, keepdims=True)
    inverse = lax.rsqrt(variance + EPSILON)
    standard = centred * inverse
    scaled = cotangent * gains
    return inverse * (
        scaled
        - jnp.mean(scaled, axis=-1, keepdims=True)
        - standard * jnp.mean(scaled * standard, axis=-1, keepdims=True)
    )


def attend_local(queries, key_block, value_block, bias_block, valid_keys, scaling):
    scores = (
        jnp.einsum("bqhd,bkhd->bhqk", queries, key_block, preferred_element_type=jnp.float32)
        * scaling
        + bias_block
    )
    scores = jnp.where(valid_keys[:, None, None, :], scores, -jnp.inf)
    row_max = jnp.max(scores, axis=-1, keepdims=True)
    exponent = jnp.exp(scores - row_max)
    weights = exponent / jnp.sum(exponent, axis=-1, keepdims=True)
    weights_low = weights.astype(jnp.bfloat16)
    attended = jnp.einsum(
        "bhqk,bkhd->bqhd", weights_low, value_block, preferred_element_type=jnp.float32
    )
    return (weights, weights_low, attended)


def attend_grads(
    weights, weights_low, queries, key_block, value_block, grad_out, row_delta, scaling
):
    weight_grad = jnp.einsum(
        "bqhd,bkhd->bhqk", grad_out, value_block, preferred_element_type=jnp.float32
    )
    dscore = weights * (weight_grad - row_delta[..., None])
    dscore_low = dscore.astype(jnp.bfloat16)
    dquery = (
        jnp.einsum("bhqk,bkhd->bqhd", dscore_low, key_block, preferred_element_type=jnp.float32)
        * scaling
    )
    key_grad = (
        jnp.einsum("bhqk,bqhd->bkhd", dscore_low, queries, preferred_element_type=jnp.float32)
        * scaling
    )
    dvalue = jnp.einsum(
        "bhqk,bqhd->bkhd", weights_low, grad_out, preferred_element_type=jnp.float32
    )
    return (dscore_low, dquery, key_grad, dvalue)


def body(
    single,
    atoms,
    gain_single,
    gain_atom,
    w_token,
    w_token_out,
    w_cond,
    w_atom,
    w_atom_out,
    pair_bias,
    atom_bias,
    used_blocks,
    used_count,
    atom_counts,
    key_offset,
    grad_token,
    grad_atom,
):
    device = lax.axis_index("seq")
    shards = lax.axis_size("seq")
    tok_rows = single.shape[0]
    blocks_here = tok_rows // BLK
    local_heads = w_token.shape[2] // DH
    features = local_heads * DH
    scaling = DH ** (-0.5)
    normed_low = norm_rows(single.astype(jnp.float32), gain_single).astype(jnp.bfloat16)
    projected = [
        jnp.dot(normed_low, w_token[which], preferred_element_type=jnp.float32)
        for which in range(4)
    ]
    queries = projected[0].astype(jnp.bfloat16)
    gate_act = jax.nn.sigmoid(projected[3])
    key_value = jnp.concatenate(
        [projected[1].astype(jnp.bfloat16), projected[2].astype(jnp.bfloat16)], axis=1
    )
    owner_dev = used_blocks // blocks_here
    relative = jnp.mod(owner_dev - device, shards)
    relative = jnp.where(relative > shards // 2, relative - shards, relative)
    pieces = [key_value for distance in range(-WIN, WIN + 1)]
    for distance in range(-WIN, WIN + 1):
        if distance != 0:
            pieces[distance + WIN] = shifted(key_value, "seq", -distance)
    window = jnp.stack(pieces)
    candidates = (2 * WIN + 1) * blocks_here
    window_flat = window.reshape(candidates, BLK * 2 * features)
    picked = (relative + WIN) * blocks_here + used_blocks % blocks_here
    selector_mask = picked[:, :, None] == jnp.arange(candidates, dtype=jnp.int32)[None, None, :]
    selector = selector_mask.astype(jnp.bfloat16)
    stashed = jnp.einsum(
        "bsc,cx->bsx", selector, window_flat, preferred_element_type=jnp.float32
    ).astype(jnp.bfloat16)
    stashed = stashed.reshape(blocks_here, S, BLK, 2 * features)
    key_blocks = stashed[..., :features].reshape(blocks_here, S * BLK, local_heads, DH)
    value_blocks = stashed[..., features:].reshape(blocks_here, S * BLK, local_heads, DH)
    query_blocks = queries.reshape(blocks_here, BLK, local_heads, DH)
    bias_blocks = (
        pair_bias.reshape(local_heads, blocks_here, BLK, S * BLK)
        .transpose(1, 0, 2, 3)
        .astype(jnp.float32)
    )
    valid_keys = jnp.repeat(
        jnp.arange(S, dtype=jnp.int32)[None, :] < used_count[:, None], BLK, axis=1
    )
    weights, weights_low, attended = attend_local(
        query_blocks, key_blocks, value_blocks, bias_blocks, valid_keys, scaling
    )
    attended = attended.reshape(tok_rows, features)
    token_part = jnp.dot(
        (attended * gate_act).astype(jnp.bfloat16), w_token_out, preferred_element_type=jnp.float32
    )
    grad_gated = jnp.dot(grad_token, w_token_out.T, preferred_element_type=jnp.float32)
    grad_attended = (grad_gated * gate_act).astype(jnp.bfloat16)
    grad_gate = (grad_gated * attended * gate_act * (1.0 - gate_act)).astype(jnp.bfloat16)
    row_delta = jnp.sum(
        (grad_attended.astype(jnp.float32) * attended).reshape(blocks_here, BLK, local_heads, DH),
        axis=-1,
    ).transpose(0, 2, 1)
    score_low, dquery, key_grad, dvalue = attend_grads(
        weights,
        weights_low,
        query_blocks,
        key_blocks,
        value_blocks,
        grad_attended.reshape(blocks_here, BLK, local_heads, DH),
        row_delta,
        scaling,
    )
    grad_pair = score_low.transpose(1, 0, 2, 3).reshape(local_heads, tok_rows, S * BLK)
    returned = jnp.concatenate(
        [
            key_grad.reshape(blocks_here, S, BLK, features),
            dvalue.reshape(blocks_here, S, BLK, features),
        ],
        axis=-1,
    )
    returned_flat = returned.reshape(blocks_here, S, BLK * 2 * features)
    outgoing = jnp.einsum(
        "bsc,bsx->cx", selector_mask.astype(jnp.float32), returned_flat, precision=HIGHEST
    )
    outgoing = outgoing.reshape(2 * WIN + 1, tok_rows, 2 * features)
    collected = outgoing[WIN]
    for distance in range(-WIN, WIN + 1):
        if distance != 0:
            collected = collected + shifted(
                outgoing[distance + WIN].astype(jnp.bfloat16), "seq", distance
            ).astype(jnp.float32)
    token_grads = [
        dquery.reshape(tok_rows, features).astype(jnp.bfloat16),
        collected[:, :features].astype(jnp.bfloat16),
        collected[:, features:].astype(jnp.bfloat16),
        grad_gate,
    ]
    w_atom_all, w_atom_out_all, atom_bias_all = (w_atom, w_atom_out, atom_bias)
    atom_rows = atoms.shape[0]
    heads_atom = w_atom_all.shape[2] // DA
    atom_feat = heads_atom * DA
    halo_rows = AK // 2
    windows_here = atom_rows // AQ
    group_span = AK // AQ + 1
    slab_rows = group_span * AQ
    atom_scaling = DA ** (-0.5)
    normed_atoms = norm_rows(atoms.astype(jnp.float32), gain_atom)
    counts = atom_counts[0]
    ends = jnp.cumsum(counts)
    atom_place = jnp.arange(atom_rows, dtype=jnp.int32)
    token_local = jnp.sum((ends[None, :] <= atom_place[:, None]).astype(jnp.int32), axis=1)
    token_pick = (token_local[:, None] == jnp.arange(tok_rows, dtype=jnp.int32)[None, :]).astype(
        jnp.float32
    )
    condition = jnp.dot(normed_low, w_cond, preferred_element_type=jnp.float32)
    atom_input = (normed_atoms + jnp.dot(token_pick, condition, precision=HIGHEST)).astype(
        jnp.bfloat16
    )
    atom_proj = [
        jnp.dot(atom_input, w_atom_all[which], preferred_element_type=jnp.float32)
        for which in range(4)
    ]
    atom_gate = jax.nn.sigmoid(atom_proj[3])
    atom_kv = jnp.concatenate(
        [atom_proj[1].astype(jnp.bfloat16), atom_proj[2].astype(jnp.bfloat16)], axis=1
    )
    extended = extended_2(atom_kv, (("seq", 0),), halo_rows)
    ext_groups = extended.reshape(windows_here + AK // AQ, AQ, 2 * atom_feat)
    slabs = jnp.concatenate(
        [ext_groups[step : step + windows_here] for step in range(group_span)], axis=1
    )
    shift_here = key_offset + halo_rows
    placer_mask = (
        jnp.arange(slab_rows, dtype=jnp.int32)[None, None, :]
        == jnp.arange(AK, dtype=jnp.int32)[None, :, None] + shift_here[:, None, None]
    )
    window_kv = jnp.einsum(
        "wrs,wsf->wrf", placer_mask.astype(jnp.bfloat16), slabs, preferred_element_type=jnp.float32
    ).astype(jnp.bfloat16)
    atom_keys = window_kv[..., :atom_feat].reshape(windows_here, AK, heads_atom, DA)
    atom_values = window_kv[..., atom_feat:].reshape(windows_here, AK, heads_atom, DA)
    atom_queries = atom_proj[0].astype(jnp.bfloat16).reshape(windows_here, AQ, heads_atom, DA)
    atom_bias_blocks = (
        atom_bias_all.reshape(heads_atom, windows_here, AQ, AK)
        .transpose(1, 0, 2, 3)
        .astype(jnp.float32)
    )
    all_valid = jnp.ones((windows_here, AK), dtype=bool)
    aweights, aweights_low, atom_attended = attend_local(
        atom_queries, atom_keys, atom_values, atom_bias_blocks, all_valid, atom_scaling
    )
    atom_attended = atom_attended.reshape(atom_rows, atom_feat)
    atom_part = jnp.dot(
        (atom_attended * atom_gate).astype(jnp.bfloat16),
        w_atom_out_all,
        preferred_element_type=jnp.float32,
    )
    agrad_gated = jnp.dot(grad_atom, w_atom_out_all.T, preferred_element_type=jnp.float32)
    agrad_attended = (agrad_gated * atom_gate).astype(jnp.bfloat16)
    agrad_gate = (agrad_gated * atom_attended * atom_gate * (1.0 - atom_gate)).astype(jnp.bfloat16)
    atom_delta = jnp.sum(
        (agrad_attended.astype(jnp.float32) * atom_attended).reshape(
            windows_here, AQ, heads_atom, DA
        ),
        axis=-1,
    ).transpose(0, 2, 1)
    ascore_low, aquery_grad, akey_grad, avalue_grad = attend_grads(
        aweights,
        aweights_low,
        atom_queries,
        atom_keys,
        atom_values,
        agrad_attended.reshape(windows_here, AQ, heads_atom, DA),
        atom_delta,
        atom_scaling,
    )
    grad_abias = ascore_low.transpose(1, 0, 2, 3).reshape(heads_atom, atom_rows, AK)
    spread_grads = jnp.concatenate(
        [
            akey_grad.reshape(windows_here, AK, atom_feat),
            avalue_grad.reshape(windows_here, AK, atom_feat),
        ],
        axis=-1,
    )
    slab_grads = jnp.einsum(
        "wrs,wrf->wsf", placer_mask.astype(jnp.float32), spread_grads, precision=HIGHEST
    )
    slab_grads = slab_grads.reshape(windows_here, group_span, AQ, 2 * atom_feat)
    ext_grad = jnp.pad(slab_grads[:, 0], ((0, group_span - 1), (0, 0), (0, 0)))
    for step in range(1, group_span):
        ext_grad = ext_grad + jnp.pad(
            slab_grads[:, step], ((step, group_span - 1 - step), (0, 0), (0, 0))
        )
    ext_grad = ext_grad.reshape(atom_rows + 2 * halo_rows, 2 * atom_feat)
    rims = jnp.concatenate([ext_grad[:halo_rows], ext_grad[atom_rows + halo_rows :]], axis=0)
    edges = extended_2(rims.astype(jnp.bfloat16), (("seq", 0),), halo_rows).astype(rims.dtype)
    own_grad = ext_grad[halo_rows : halo_rows + atom_rows]
    own_grad = jnp.concatenate(
        [
            own_grad[:halo_rows] + edges[:halo_rows],
            own_grad[halo_rows : atom_rows - halo_rows],
            own_grad[atom_rows - halo_rows :] + edges[3 * halo_rows :],
        ],
        axis=0,
    )
    atom_grads = [
        aquery_grad.reshape(atom_rows, atom_feat).astype(jnp.bfloat16),
        own_grad[:, :atom_feat].astype(jnp.bfloat16),
        own_grad[:, atom_feat:].astype(jnp.bfloat16),
        agrad_gate,
    ]
    agrad_input = jnp.dot(atom_grads[0], w_atom_all[0].T, preferred_element_type=jnp.float32)
    for which in range(1, 4):
        agrad_input = agrad_input + jnp.dot(
            atom_grads[which], w_atom_all[which].T, preferred_element_type=jnp.float32
        )
    atoms_part = norm_back(atoms.astype(jnp.float32), gain_atom, agrad_input)
    cond_grad = jnp.dot(token_pick.T, agrad_input, precision=HIGHEST)
    cond_term = jnp.dot(cond_grad, w_cond.astype(jnp.float32).T, precision=HIGHEST)
    grad_normed = cond_term
    for which in range(4):
        grad_normed = grad_normed + jnp.dot(
            token_grads[which], w_token[which].T, preferred_element_type=jnp.float32
        )
    single_part = norm_back(single.astype(jnp.float32), gain_single, grad_normed)
    token_total, atom_total, single_total, atoms_total = head_sum(
        [token_part, atom_part, single_part, atoms_part], "head"
    )
    return (
        token_total.astype(jnp.bfloat16),
        atom_total.astype(jnp.bfloat16),
        single_total.astype(jnp.bfloat16),
        atoms_total.astype(jnp.bfloat16),
        grad_pair,
        grad_abias,
    )


def solution(mesh):
    return jax.shard_map(
        body,
        mesh=mesh,
        in_specs=(
            P("seq", None),
            P("seq", None),
            P(),
            P(),
            P(None, None, "head"),
            P("head", None),
            P(),
            P(None, None, "head"),
            P("head", None),
            P("head", "seq", None),
            P("head", "seq", None),
            P("seq", None),
            P("seq"),
            P("seq", None),
            P("seq"),
            P("seq", None),
            P("seq", None),
        ),
        out_specs=(
            P("seq", None),
            P("seq", None),
            P("seq", None),
            P("seq", None),
            P("head", "seq", None),
            P("head", "seq", None),
        ),
        check_vma=False,
    )
```

```python
import jax
import jax.numpy as jnp
from jax import lax
from jax.sharding import PartitionSpec as P

DH = 24
DA = 32
BLK = 128
S = 4
WIN = 2
AQ = 32
AK = 128


EPSILON = 1e-05
HIGHEST = lax.Precision.HIGHEST


def shifted(block, axis, distance):
    devices = range(lax.axis_size(axis))
    route = [((i - distance) % len(devices), i) for i in devices]
    return lax.ppermute(block, axis, route)


def shifted_pair(block, extra, axis, distance):
    width = block.shape[1]
    padded = jnp.pad(extra, ((0, block.shape[0] - extra.shape[0]), (0, 0)))
    both = shifted(jnp.concatenate([block, padded], axis=1), axis, distance)
    return both[:, :width], both[: extra.shape[0], width:]


def extended_2(block, sides, width):
    for axis, dim in sides:
        count = lax.axis_size(axis)
        forward = [(i, i + 1) for i in range(count - 1)]
        forward.append((count - 1, 0))
        backward = [(target, source) for source, target in forward]
        low = lax.ppermute(
            lax.slice_in_dim(block, block.shape[dim] - width, None, axis=dim), axis, forward
        )
        high = lax.ppermute(lax.slice_in_dim(block, 0, width, axis=dim), axis, backward)
        block = jnp.concatenate([low, block, high], axis=dim)
    return block


def head_sum(parts, axis):
    count = lax.axis_size(axis)
    if count != 4:
        return [lax.psum(p.astype(jnp.bfloat16), axis) for p in parts]
    pieces = []
    for part in parts:
        for col in range(part.shape[1] // 128):
            pieces.append(part[:, col * 128 : (col + 1) * 128])
    buf = jnp.concatenate(pieces, axis=0)
    rows = buf.shape[0]
    place = lax.axis_index(axis)
    low_bit = place % 2
    high_bit = (place // 2) % 2
    pair_near = [(i, i ^ 1) for i in range(count)]
    pair_far = [(i, i ^ 2) for i in range(count)]
    halves = buf.reshape(2, rows // 2, 128)
    keep = jnp.where(low_bit == 0, halves[0], halves[1])
    give = jnp.where(low_bit == 0, halves[1], halves[0])
    got = lax.ppermute(give.astype(jnp.bfloat16), axis, pair_near)
    summed = (keep + got.astype(jnp.float32)).reshape(2, rows // 4, 128)
    keep = jnp.where(high_bit == 0, summed[0], summed[1])
    give = jnp.where(high_bit == 0, summed[1], summed[0])
    got = lax.ppermute(give.astype(jnp.bfloat16), axis, pair_far)
    own = (keep + got.astype(jnp.float32)).astype(jnp.bfloat16)
    got = lax.ppermute(own, axis, pair_far)
    half = jnp.where(
        high_bit == 0, jnp.concatenate([own, got], axis=0), jnp.concatenate([got, own], axis=0)
    )
    got = lax.ppermute(half, axis, pair_near)
    full = jnp.where(
        low_bit == 0, jnp.concatenate([half, got], axis=0), jnp.concatenate([got, half], axis=0)
    )
    outs = []
    start = 0
    for part in parts:
        width = part.shape[1] // 128
        rows_here = part.shape[0]
        cols = [full[start + k * rows_here : start + (k + 1) * rows_here] for k in range(width)]
        start += width * rows_here
        outs.append(jnp.concatenate(cols, axis=1) if width > 1 else cols[0])
    return outs


def norm_rows(inputs, gains):
    row_mean = jnp.mean(inputs, axis=-1, keepdims=True)
    centred = inputs - row_mean
    variance = jnp.mean(centred * centred, axis=-1, keepdims=True)
    return centred * lax.rsqrt(variance + EPSILON) * gains


def norm_back(inputs, gains, cotangent):
    row_mean = jnp.mean(inputs, axis=-1, keepdims=True)
    centred = inputs - row_mean
    variance = jnp.mean(centred * centred, axis=-1, keepdims=True)
    inverse = lax.rsqrt(variance + EPSILON)
    standard = centred * inverse
    scaled = cotangent * gains
    return inverse * (
        scaled
        - jnp.mean(scaled, axis=-1, keepdims=True)
        - standard * jnp.mean(scaled * standard, axis=-1, keepdims=True)
    )


def attend_local(queries, key_block, value_block, bias_block, valid_keys, scaling):
    scores = (
        jnp.einsum("bqhd,bkhd->bhqk", queries, key_block, preferred_element_type=jnp.float32)
        * scaling
        + bias_block
    )
    scores = jnp.where(valid_keys[:, None, None, :], scores, -jnp.inf)
    row_max = jnp.max(scores, axis=-1, keepdims=True)
    exponent = jnp.exp(scores - row_max)
    weights = exponent / jnp.sum(exponent, axis=-1, keepdims=True)
    weights_low = weights.astype(jnp.bfloat16)
    attended = jnp.einsum(
        "bhqk,bkhd->bqhd", weights_low, value_block, preferred_element_type=jnp.float32
    )
    return (weights, weights_low, attended)


def attend_grads(
    weights, weights_low, queries, key_block, value_block, grad_out, row_delta, scaling
):
    weight_grad = jnp.einsum(
        "bqhd,bkhd->bhqk", grad_out, value_block, preferred_element_type=jnp.float32
    )
    dscore = weights * (weight_grad - row_delta[..., None])
    dscore_low = dscore.astype(jnp.bfloat16)
    dquery = (
        jnp.einsum("bhqk,bkhd->bqhd", dscore_low, key_block, preferred_element_type=jnp.float32)
        * scaling
    )
    key_grad = (
        jnp.einsum("bhqk,bqhd->bkhd", dscore_low, queries, preferred_element_type=jnp.float32)
        * scaling
    )
    dvalue = jnp.einsum(
        "bhqk,bqhd->bkhd", weights_low, grad_out, preferred_element_type=jnp.float32
    )
    return (dscore_low, dquery, key_grad, dvalue)


def body(
    single,
    atoms,
    gain_single,
    gain_atom,
    w_token,
    w_token_out,
    w_cond,
    w_atom,
    w_atom_out,
    pair_bias,
    atom_bias,
    used_blocks,
    used_count,
    atom_counts,
    key_offset,
    grad_token,
    grad_atom,
):
    device = lax.axis_index("seq")
    shards = lax.axis_size("seq")
    tok_rows = single.shape[0]
    blocks_here = tok_rows // BLK
    local_heads = w_token.shape[2] // DH
    features = local_heads * DH
    scaling = DH ** (-0.5)
    normed_low = norm_rows(single.astype(jnp.float32), gain_single).astype(jnp.bfloat16)
    projected = [
        jnp.dot(normed_low, w_token[which], preferred_element_type=jnp.float32)
        for which in range(4)
    ]
    queries = projected[0].astype(jnp.bfloat16)
    gate_act = jax.nn.sigmoid(projected[3])
    key_value = jnp.concatenate(
        [projected[1].astype(jnp.bfloat16), projected[2].astype(jnp.bfloat16)], axis=1
    )
    w_atom_all, w_atom_out_all, atom_bias_all = (w_atom, w_atom_out, atom_bias)
    atom_rows = atoms.shape[0]
    heads_atom = w_atom_all.shape[2] // DA
    atom_feat = heads_atom * DA
    halo_rows = AK // 2
    windows_here = atom_rows // AQ
    group_span = AK // AQ + 1
    slab_rows = group_span * AQ
    atom_scaling = DA ** (-0.5)
    normed_atoms = norm_rows(atoms.astype(jnp.float32), gain_atom)
    counts = atom_counts[0]
    ends = jnp.cumsum(counts)
    atom_place = jnp.arange(atom_rows, dtype=jnp.int32)
    token_local = jnp.sum((ends[None, :] <= atom_place[:, None]).astype(jnp.int32), axis=1)
    token_pick = (token_local[:, None] == jnp.arange(tok_rows, dtype=jnp.int32)[None, :]).astype(
        jnp.float32
    )
    condition = jnp.dot(normed_low, w_cond, preferred_element_type=jnp.float32)
    atom_input = (normed_atoms + jnp.dot(token_pick, condition, precision=HIGHEST)).astype(
        jnp.bfloat16
    )
    atom_proj = [
        jnp.dot(atom_input, w_atom_all[which], preferred_element_type=jnp.float32)
        for which in range(4)
    ]
    atom_gate = jax.nn.sigmoid(atom_proj[3])
    atom_kv = jnp.concatenate(
        [atom_proj[1].astype(jnp.bfloat16), atom_proj[2].astype(jnp.bfloat16)], axis=1
    )
    owner_dev = used_blocks // blocks_here
    relative = jnp.mod(owner_dev - device, shards)
    relative = jnp.where(relative > shards // 2, relative - shards, relative)
    pieces = [key_value for distance in range(-WIN, WIN + 1)]
    for distance in range(-WIN, WIN + 1):
        if abs(distance) > 1:
            pieces[distance + WIN] = shifted(key_value, "seq", -distance)
    pieces[WIN - 1], halo_low = shifted_pair(
        key_value, atom_kv[atom_kv.shape[0] - AK // 2 :], "seq", 1
    )
    pieces[WIN + 1], halo_high = shifted_pair(key_value, atom_kv[: AK // 2], "seq", -1)
    window = jnp.stack(pieces)
    candidates = (2 * WIN + 1) * blocks_here
    window_flat = window.reshape(candidates, BLK * 2 * features)
    picked = (relative + WIN) * blocks_here + used_blocks % blocks_here
    selector_mask = picked[:, :, None] == jnp.arange(candidates, dtype=jnp.int32)[None, None, :]
    selector = selector_mask.astype(jnp.bfloat16)
    stashed = jnp.einsum(
        "bsc,cx->bsx", selector, window_flat, preferred_element_type=jnp.float32
    ).astype(jnp.bfloat16)
    stashed = stashed.reshape(blocks_here, S, BLK, 2 * features)
    key_blocks = stashed[..., :features].reshape(blocks_here, S * BLK, local_heads, DH)
    value_blocks = stashed[..., features:].reshape(blocks_here, S * BLK, local_heads, DH)
    query_blocks = queries.reshape(blocks_here, BLK, local_heads, DH)
    bias_blocks = (
        pair_bias.reshape(local_heads, blocks_here, BLK, S * BLK)
        .transpose(1, 0, 2, 3)
        .astype(jnp.float32)
    )
    valid_keys = jnp.repeat(
        jnp.arange(S, dtype=jnp.int32)[None, :] < used_count[:, None], BLK, axis=1
    )
    weights, weights_low, attended = attend_local(
        query_blocks, key_blocks, value_blocks, bias_blocks, valid_keys, scaling
    )
    attended = attended.reshape(tok_rows, features)
    token_part = jnp.dot(
        (attended * gate_act).astype(jnp.bfloat16), w_token_out, preferred_element_type=jnp.float32
    )
    grad_gated = jnp.dot(grad_token, w_token_out.T, preferred_element_type=jnp.float32)
    grad_attended = (grad_gated * gate_act).astype(jnp.bfloat16)
    grad_gate = (grad_gated * attended * gate_act * (1.0 - gate_act)).astype(jnp.bfloat16)
    row_delta = jnp.sum(
        (grad_attended.astype(jnp.float32) * attended).reshape(blocks_here, BLK, local_heads, DH),
        axis=-1,
    ).transpose(0, 2, 1)
    score_low, dquery, key_grad, dvalue = attend_grads(
        weights,
        weights_low,
        query_blocks,
        key_blocks,
        value_blocks,
        grad_attended.reshape(blocks_here, BLK, local_heads, DH),
        row_delta,
        scaling,
    )
    grad_pair = score_low.transpose(1, 0, 2, 3).reshape(local_heads, tok_rows, S * BLK)
    returned = jnp.concatenate(
        [
            key_grad.reshape(blocks_here, S, BLK, features),
            dvalue.reshape(blocks_here, S, BLK, features),
        ],
        axis=-1,
    )
    returned_flat = returned.reshape(blocks_here, S, BLK * 2 * features)
    outgoing = jnp.einsum(
        "bsc,bsx->cx", selector_mask.astype(jnp.float32), returned_flat, precision=HIGHEST
    )
    outgoing = outgoing.reshape(2 * WIN + 1, tok_rows, 2 * features)
    extended = jnp.concatenate([halo_low, atom_kv, halo_high], axis=0)
    ext_groups = extended.reshape(windows_here + AK // AQ, AQ, 2 * atom_feat)
    slabs = jnp.concatenate(
        [ext_groups[step : step + windows_here] for step in range(group_span)], axis=1
    )
    shift_here = key_offset + halo_rows
    placer_mask = (
        jnp.arange(slab_rows, dtype=jnp.int32)[None, None, :]
        == jnp.arange(AK, dtype=jnp.int32)[None, :, None] + shift_here[:, None, None]
    )
    window_kv = jnp.einsum(
        "wrs,wsf->wrf", placer_mask.astype(jnp.bfloat16), slabs, preferred_element_type=jnp.float32
    ).astype(jnp.bfloat16)
    atom_keys = window_kv[..., :atom_feat].reshape(windows_here, AK, heads_atom, DA)
    atom_values = window_kv[..., atom_feat:].reshape(windows_here, AK, heads_atom, DA)
    atom_queries = atom_proj[0].astype(jnp.bfloat16).reshape(windows_here, AQ, heads_atom, DA)
    atom_bias_blocks = (
        atom_bias_all.reshape(heads_atom, windows_here, AQ, AK)
        .transpose(1, 0, 2, 3)
        .astype(jnp.float32)
    )
    all_valid = jnp.ones((windows_here, AK), dtype=bool)
    aweights, aweights_low, atom_attended = attend_local(
        atom_queries, atom_keys, atom_values, atom_bias_blocks, all_valid, atom_scaling
    )
    atom_attended = atom_attended.reshape(atom_rows, atom_feat)
    atom_part = jnp.dot(
        (atom_attended * atom_gate).astype(jnp.bfloat16),
        w_atom_out_all,
        preferred_element_type=jnp.float32,
    )
    agrad_gated = jnp.dot(grad_atom, w_atom_out_all.T, preferred_element_type=jnp.float32)
    agrad_attended = (agrad_gated * atom_gate).astype(jnp.bfloat16)
    agrad_gate = (agrad_gated * atom_attended * atom_gate * (1.0 - atom_gate)).astype(jnp.bfloat16)
    atom_delta = jnp.sum(
        (agrad_attended.astype(jnp.float32) * atom_attended).reshape(
            windows_here, AQ, heads_atom, DA
        ),
        axis=-1,
    ).transpose(0, 2, 1)
    ascore_low, aquery_grad, akey_grad, avalue_grad = attend_grads(
        aweights,
        aweights_low,
        atom_queries,
        atom_keys,
        atom_values,
        agrad_attended.reshape(windows_here, AQ, heads_atom, DA),
        atom_delta,
        atom_scaling,
    )
    grad_abias = ascore_low.transpose(1, 0, 2, 3).reshape(heads_atom, atom_rows, AK)
    spread_grads = jnp.concatenate(
        [
            akey_grad.reshape(windows_here, AK, atom_feat),
            avalue_grad.reshape(windows_here, AK, atom_feat),
        ],
        axis=-1,
    )
    slab_grads = jnp.einsum(
        "wrs,wrf->wsf", placer_mask.astype(jnp.float32), spread_grads, precision=HIGHEST
    )
    slab_grads = slab_grads.reshape(windows_here, group_span, AQ, 2 * atom_feat)
    ext_grad = jnp.pad(slab_grads[:, 0], ((0, group_span - 1), (0, 0), (0, 0)))
    for step in range(1, group_span):
        ext_grad = ext_grad + jnp.pad(
            slab_grads[:, step], ((step, group_span - 1 - step), (0, 0), (0, 0))
        )
    ext_grad = ext_grad.reshape(atom_rows + 2 * halo_rows, 2 * atom_feat)
    rims = jnp.concatenate([ext_grad[:halo_rows], ext_grad[atom_rows + halo_rows :]], axis=0)
    collected = outgoing[WIN]
    for distance in range(-WIN, WIN + 1):
        if abs(distance) > 1:
            collected = collected + shifted(
                outgoing[distance + WIN].astype(jnp.bfloat16), "seq", distance
            ).astype(jnp.float32)
    came_low, edge_low = shifted_pair(
        outgoing[WIN + 1].astype(jnp.bfloat16), rims[halo_rows:].astype(jnp.bfloat16), "seq", 1
    )
    came_high, edge_high = shifted_pair(
        outgoing[WIN - 1].astype(jnp.bfloat16), rims[:halo_rows].astype(jnp.bfloat16), "seq", -1
    )
    collected = collected + came_low.astype(jnp.float32) + came_high.astype(jnp.float32)
    edges = jnp.concatenate(
        [edge_low, rims.astype(jnp.bfloat16), edge_high], axis=0
    ).astype(rims.dtype)
    token_grads = [
        dquery.reshape(tok_rows, features).astype(jnp.bfloat16),
        collected[:, :features].astype(jnp.bfloat16),
        collected[:, features:].astype(jnp.bfloat16),
        grad_gate,
    ]
    own_grad = ext_grad[halo_rows : halo_rows + atom_rows]
    own_grad = jnp.concatenate(
        [
            own_grad[:halo_rows] + edges[:halo_rows],
            own_grad[halo_rows : atom_rows - halo_rows],
            own_grad[atom_rows - halo_rows :] + edges[3 * halo_rows :],
        ],
        axis=0,
    )
    atom_grads = [
        aquery_grad.reshape(atom_rows, atom_feat).astype(jnp.bfloat16),
        own_grad[:, :atom_feat].astype(jnp.bfloat16),
        own_grad[:, atom_feat:].astype(jnp.bfloat16),
        agrad_gate,
    ]
    agrad_input = jnp.dot(atom_grads[0], w_atom_all[0].T, preferred_element_type=jnp.float32)
    for which in range(1, 4):
        agrad_input = agrad_input + jnp.dot(
            atom_grads[which], w_atom_all[which].T, preferred_element_type=jnp.float32
        )
    atoms_part = norm_back(atoms.astype(jnp.float32), gain_atom, agrad_input)
    cond_grad = jnp.dot(token_pick.T, agrad_input, precision=HIGHEST)
    cond_term = jnp.dot(cond_grad, w_cond.astype(jnp.float32).T, precision=HIGHEST)
    grad_normed = cond_term
    for which in range(4):
        grad_normed = grad_normed + jnp.dot(
            token_grads[which], w_token[which].T, preferred_element_type=jnp.float32
        )
    single_part = norm_back(single.astype(jnp.float32), gain_single, grad_normed)
    token_total, atom_total, single_total, atoms_total = head_sum(
        [token_part, atom_part, single_part, atoms_part], "head"
    )
    return (
        token_total.astype(jnp.bfloat16),
        atom_total.astype(jnp.bfloat16),
        single_total.astype(jnp.bfloat16),
        atoms_total.astype(jnp.bfloat16),
        grad_pair,
        grad_abias,
    )


def solution(mesh):
    return jax.shard_map(
        body,
        mesh=mesh,
        in_specs=(
            P("seq", None),
            P("seq", None),
            P(),
            P(),
            P(None, None, "head"),
            P("head", None),
            P(),
            P(None, None, "head"),
            P("head", None),
            P("head", "seq", None),
            P("head", "seq", None),
            P("seq", None),
            P("seq"),
            P("seq", None),
            P("seq"),
            P("seq", None),
            P("seq", None),
        ),
        out_specs=(
            P("seq", None),
            P("seq", None),
            P("seq", None),
            P("seq", None),
            P("head", "seq", None),
            P("head", "seq", None),
        ),
        check_vma=False,
    )
```

```python
import jax
import jax.numpy as jnp
from jax import lax
from jax.sharding import PartitionSpec as P

DH = 24
DA = 32
BLK = 128
S = 4
WIN = 2
AQ = 32
AK = 128


EPSILON = 1e-05
HIGHEST = lax.Precision.HIGHEST


def shifted(block, axis, distance):
    devices = range(lax.axis_size(axis))
    route = [((i - distance) % len(devices), i) for i in devices]
    return lax.ppermute(block, axis, route)


def shifted_pair(block, extra, axis, distance):
    width = block.shape[1]
    padded = jnp.pad(extra, ((0, block.shape[0] - extra.shape[0]), (0, 0)))
    both = shifted(jnp.concatenate([block, padded], axis=1), axis, distance)
    return both[:, :width], both[: extra.shape[0], width:]


def extended_2(block, sides, width):
    for axis, dim in sides:
        count = lax.axis_size(axis)
        forward = [(i, i + 1) for i in range(count - 1)]
        forward.append((count - 1, 0))
        backward = [(target, source) for source, target in forward]
        low = lax.ppermute(
            lax.slice_in_dim(block, block.shape[dim] - width, None, axis=dim), axis, forward
        )
        high = lax.ppermute(lax.slice_in_dim(block, 0, width, axis=dim), axis, backward)
        block = jnp.concatenate([low, block, high], axis=dim)
    return block


def head_sum(parts, axis):
    count = lax.axis_size(axis)
    if count != 4:
        return [lax.psum(p.astype(jnp.bfloat16), axis) for p in parts]
    pieces = []
    for part in parts:
        for col in range(part.shape[1] // 128):
            pieces.append(part[:, col * 128 : (col + 1) * 128])
    buf = jnp.concatenate(pieces, axis=0)
    rows = buf.shape[0]
    place = lax.axis_index(axis)
    low_bit = place % 2
    high_bit = (place // 2) % 2
    pair_near = [(i, i ^ 1) for i in range(count)]
    pair_far = [(i, i ^ 2) for i in range(count)]
    halves = buf.reshape(2, rows // 2, 128)
    keep = jnp.where(low_bit == 0, halves[0], halves[1])
    give = jnp.where(low_bit == 0, halves[1], halves[0])
    got = lax.ppermute(give.astype(jnp.bfloat16), axis, pair_near)
    summed = (keep + got.astype(jnp.float32)).reshape(2, rows // 4, 128)
    keep = jnp.where(high_bit == 0, summed[0], summed[1])
    give = jnp.where(high_bit == 0, summed[1], summed[0])
    got = lax.ppermute(give.astype(jnp.bfloat16), axis, pair_far)
    own = (keep + got.astype(jnp.float32)).astype(jnp.bfloat16)
    got = lax.ppermute(own, axis, pair_far)
    half = jnp.where(
        high_bit == 0, jnp.concatenate([own, got], axis=0), jnp.concatenate([got, own], axis=0)
    )
    got = lax.ppermute(half, axis, pair_near)
    full = jnp.where(
        low_bit == 0, jnp.concatenate([half, got], axis=0), jnp.concatenate([got, half], axis=0)
    )
    outs = []
    start = 0
    for part in parts:
        width = part.shape[1] // 128
        rows_here = part.shape[0]
        cols = [full[start + k * rows_here : start + (k + 1) * rows_here] for k in range(width)]
        start += width * rows_here
        outs.append(jnp.concatenate(cols, axis=1) if width > 1 else cols[0])
    return outs


def norm_rows(inputs, gains):
    row_mean = jnp.mean(inputs, axis=-1, keepdims=True)
    centred = inputs - row_mean
    variance = jnp.mean(centred * centred, axis=-1, keepdims=True)
    return centred * lax.rsqrt(variance + EPSILON) * gains


def norm_back(inputs, gains, cotangent):
    row_mean = jnp.mean(inputs, axis=-1, keepdims=True)
    centred = inputs - row_mean
    variance = jnp.mean(centred * centred, axis=-1, keepdims=True)
    inverse = lax.rsqrt(variance + EPSILON)
    standard = centred * inverse
    scaled = cotangent * gains
    return inverse * (
        scaled
        - jnp.mean(scaled, axis=-1, keepdims=True)
        - standard * jnp.mean(scaled * standard, axis=-1, keepdims=True)
    )


def attend_local(queries, key_block, value_block, bias_block, valid_keys, scaling):
    scores = (
        jnp.einsum("bqhd,bkhd->bhqk", queries, key_block, preferred_element_type=jnp.float32)
        * scaling
        + bias_block
    )
    scores = jnp.where(valid_keys[:, None, None, :], scores, -jnp.inf)
    row_max = jnp.max(scores, axis=-1, keepdims=True)
    exponent = jnp.exp(scores - row_max)
    weights = exponent / jnp.sum(exponent, axis=-1, keepdims=True)
    weights_low = weights.astype(jnp.bfloat16)
    attended = jnp.einsum(
        "bhqk,bkhd->bqhd", weights_low, value_block, preferred_element_type=jnp.float32
    )
    return (weights, weights_low, attended)


def attend_grads(
    weights, weights_low, queries, key_block, value_block, grad_out, row_delta, scaling
):
    weight_grad = jnp.einsum(
        "bqhd,bkhd->bhqk", grad_out, value_block, preferred_element_type=jnp.float32
    )
    dscore = weights * (weight_grad - row_delta[..., None])
    dscore_low = dscore.astype(jnp.bfloat16)
    dquery = (
        jnp.einsum("bhqk,bkhd->bqhd", dscore_low, key_block, preferred_element_type=jnp.float32)
        * scaling
    )
    key_grad = (
        jnp.einsum("bhqk,bqhd->bkhd", dscore_low, queries, preferred_element_type=jnp.float32)
        * scaling
    )
    dvalue = jnp.einsum(
        "bhqk,bqhd->bkhd", weights_low, grad_out, preferred_element_type=jnp.float32
    )
    return (dscore_low, dquery, key_grad, dvalue)


def body(
    single,
    atoms,
    gain_single,
    gain_atom,
    w_token,
    w_token_out,
    w_cond,
    w_atom,
    w_atom_out,
    pair_bias,
    atom_bias,
    used_blocks,
    used_count,
    atom_counts,
    key_offset,
    grad_token,
    grad_atom,
):
    device = lax.axis_index("seq")
    shards = lax.axis_size("seq")
    tok_rows = single.shape[0]
    blocks_here = tok_rows // BLK
    local_heads = w_token.shape[2] // DH
    features = local_heads * DH
    scaling = DH ** (-0.5)
    normed_low = norm_rows(single.astype(jnp.float32), gain_single).astype(jnp.bfloat16)
    projected = [
        jnp.dot(normed_low, w_token[which], preferred_element_type=jnp.float32)
        for which in range(4)
    ]
    queries = projected[0].astype(jnp.bfloat16)
    gate_act = jax.nn.sigmoid(projected[3])
    key_value = jnp.concatenate(
        [projected[1].astype(jnp.bfloat16), projected[2].astype(jnp.bfloat16)], axis=1
    )
    owner_dev = used_blocks // blocks_here
    relative = jnp.mod(owner_dev - device, shards)
    relative = jnp.where(relative > shards // 2, relative - shards, relative)
    pieces = [key_value for distance in range(-WIN, WIN + 1)]
    for distance in range(-WIN, WIN + 1):
        if distance != 0:
            pieces[distance + WIN] = shifted(key_value, "seq", -distance)
    window = jnp.stack(pieces)
    candidates = (2 * WIN + 1) * blocks_here
    window_flat = window.reshape(candidates, BLK * 2 * features)
    picked = (relative + WIN) * blocks_here + used_blocks % blocks_here
    selector_mask = picked[:, :, None] == jnp.arange(candidates, dtype=jnp.int32)[None, None, :]
    selector = selector_mask.astype(jnp.bfloat16)
    stashed = jnp.einsum(
        "bsc,cx->bsx", selector, window_flat, preferred_element_type=jnp.float32
    ).astype(jnp.bfloat16)
    stashed = stashed.reshape(blocks_here, S, BLK, 2 * features)
    key_blocks = stashed[..., :features].reshape(blocks_here, S * BLK, local_heads, DH)
    value_blocks = stashed[..., features:].reshape(blocks_here, S * BLK, local_heads, DH)
    query_blocks = queries.reshape(blocks_here, BLK, local_heads, DH)
    bias_blocks = (
        pair_bias.reshape(local_heads, blocks_here, BLK, S * BLK)
        .transpose(1, 0, 2, 3)
        .astype(jnp.float32)
    )
    valid_keys = jnp.repeat(
        jnp.arange(S, dtype=jnp.int32)[None, :] < used_count[:, None], BLK, axis=1
    )
    weights, weights_low, attended = attend_local(
        query_blocks, key_blocks, value_blocks, bias_blocks, valid_keys, scaling
    )
    attended = attended.reshape(tok_rows, features)
    token_part = jnp.dot(
        (attended * gate_act).astype(jnp.bfloat16), w_token_out, preferred_element_type=jnp.float32
    )
    grad_gated = jnp.dot(grad_token, w_token_out.T, preferred_element_type=jnp.float32)
    grad_attended = (grad_gated * gate_act).astype(jnp.bfloat16)
    grad_gate = (grad_gated * attended * gate_act * (1.0 - gate_act)).astype(jnp.bfloat16)
    row_delta = jnp.sum(
        (grad_attended.astype(jnp.float32) * attended).reshape(blocks_here, BLK, local_heads, DH),
        axis=-1,
    ).transpose(0, 2, 1)
    score_low, dquery, key_grad, dvalue = attend_grads(
        weights,
        weights_low,
        query_blocks,
        key_blocks,
        value_blocks,
        grad_attended.reshape(blocks_here, BLK, local_heads, DH),
        row_delta,
        scaling,
    )
    grad_pair = score_low.transpose(1, 0, 2, 3).reshape(local_heads, tok_rows, S * BLK)
    returned = jnp.concatenate(
        [
            key_grad.reshape(blocks_here, S, BLK, features),
            dvalue.reshape(blocks_here, S, BLK, features),
        ],
        axis=-1,
    )
    returned_flat = returned.reshape(blocks_here, S, BLK * 2 * features)
    outgoing = jnp.einsum(
        "bsc,bsx->cx", selector_mask.astype(jnp.float32), returned_flat, precision=HIGHEST
    )
    outgoing = outgoing.reshape(2 * WIN + 1, tok_rows, 2 * features)
    w_atom_all, w_atom_out_all, atom_bias_all = (w_atom, w_atom_out, atom_bias)
    atom_rows = atoms.shape[0]
    heads_atom = w_atom_all.shape[2] // DA
    atom_feat = heads_atom * DA
    halo_rows = AK // 2
    windows_here = atom_rows // AQ
    group_span = AK // AQ + 1
    slab_rows = group_span * AQ
    atom_scaling = DA ** (-0.5)
    normed_atoms = norm_rows(atoms.astype(jnp.float32), gain_atom)
    counts = atom_counts[0]
    ends = jnp.cumsum(counts)
    atom_place = jnp.arange(atom_rows, dtype=jnp.int32)
    token_local = jnp.sum((ends[None, :] <= atom_place[:, None]).astype(jnp.int32), axis=1)
    token_pick = (token_local[:, None] == jnp.arange(tok_rows, dtype=jnp.int32)[None, :]).astype(
        jnp.float32
    )
    condition = jnp.dot(normed_low, w_cond, preferred_element_type=jnp.float32)
    atom_input = (normed_atoms + jnp.dot(token_pick, condition, precision=HIGHEST)).astype(
        jnp.bfloat16
    )
    atom_proj = [
        jnp.dot(atom_input, w_atom_all[which], preferred_element_type=jnp.float32)
        for which in range(4)
    ]
    atom_gate = jax.nn.sigmoid(atom_proj[3])
    atom_kv = jnp.concatenate(
        [atom_proj[1].astype(jnp.bfloat16), atom_proj[2].astype(jnp.bfloat16)], axis=1
    )
    extended = extended_2(atom_kv, (("seq", 0),), halo_rows)
    ext_groups = extended.reshape(windows_here + AK // AQ, AQ, 2 * atom_feat)
    slabs = jnp.concatenate(
        [ext_groups[step : step + windows_here] for step in range(group_span)], axis=1
    )
    shift_here = key_offset + halo_rows
    placer_mask = (
        jnp.arange(slab_rows, dtype=jnp.int32)[None, None, :]
        == jnp.arange(AK, dtype=jnp.int32)[None, :, None] + shift_here[:, None, None]
    )
    window_kv = jnp.einsum(
        "wrs,wsf->wrf", placer_mask.astype(jnp.bfloat16), slabs, preferred_element_type=jnp.float32
    ).astype(jnp.bfloat16)
    atom_keys = window_kv[..., :atom_feat].reshape(windows_here, AK, heads_atom, DA)
    atom_values = window_kv[..., atom_feat:].reshape(windows_here, AK, heads_atom, DA)
    atom_queries = atom_proj[0].astype(jnp.bfloat16).reshape(windows_here, AQ, heads_atom, DA)
    atom_bias_blocks = (
        atom_bias_all.reshape(heads_atom, windows_here, AQ, AK)
        .transpose(1, 0, 2, 3)
        .astype(jnp.float32)
    )
    all_valid = jnp.ones((windows_here, AK), dtype=bool)
    aweights, aweights_low, atom_attended = attend_local(
        atom_queries, atom_keys, atom_values, atom_bias_blocks, all_valid, atom_scaling
    )
    atom_attended = atom_attended.reshape(atom_rows, atom_feat)
    atom_part = jnp.dot(
        (atom_attended * atom_gate).astype(jnp.bfloat16),
        w_atom_out_all,
        preferred_element_type=jnp.float32,
    )
    agrad_gated = jnp.dot(grad_atom, w_atom_out_all.T, preferred_element_type=jnp.float32)
    agrad_attended = (agrad_gated * atom_gate).astype(jnp.bfloat16)
    agrad_gate = (agrad_gated * atom_attended * atom_gate * (1.0 - atom_gate)).astype(jnp.bfloat16)
    atom_delta = jnp.sum(
        (agrad_attended.astype(jnp.float32) * atom_attended).reshape(
            windows_here, AQ, heads_atom, DA
        ),
        axis=-1,
    ).transpose(0, 2, 1)
    ascore_low, aquery_grad, akey_grad, avalue_grad = attend_grads(
        aweights,
        aweights_low,
        atom_queries,
        atom_keys,
        atom_values,
        agrad_attended.reshape(windows_here, AQ, heads_atom, DA),
        atom_delta,
        atom_scaling,
    )
    grad_abias = ascore_low.transpose(1, 0, 2, 3).reshape(heads_atom, atom_rows, AK)
    spread_grads = jnp.concatenate(
        [
            akey_grad.reshape(windows_here, AK, atom_feat),
            avalue_grad.reshape(windows_here, AK, atom_feat),
        ],
        axis=-1,
    )
    slab_grads = jnp.einsum(
        "wrs,wrf->wsf", placer_mask.astype(jnp.float32), spread_grads, precision=HIGHEST
    )
    slab_grads = slab_grads.reshape(windows_here, group_span, AQ, 2 * atom_feat)
    ext_grad = jnp.pad(slab_grads[:, 0], ((0, group_span - 1), (0, 0), (0, 0)))
    for step in range(1, group_span):
        ext_grad = ext_grad + jnp.pad(
            slab_grads[:, step], ((step, group_span - 1 - step), (0, 0), (0, 0))
        )
    ext_grad = ext_grad.reshape(atom_rows + 2 * halo_rows, 2 * atom_feat)
    rims = jnp.concatenate([ext_grad[:halo_rows], ext_grad[atom_rows + halo_rows :]], axis=0)
    collected = outgoing[WIN]
    for distance in range(-WIN, WIN + 1):
        if abs(distance) > 1:
            collected = collected + shifted(
                outgoing[distance + WIN].astype(jnp.bfloat16), "seq", distance
            ).astype(jnp.float32)
    came_low, edge_low = shifted_pair(
        outgoing[WIN + 1].astype(jnp.bfloat16), rims[halo_rows:].astype(jnp.bfloat16), "seq", 1
    )
    came_high, edge_high = shifted_pair(
        outgoing[WIN - 1].astype(jnp.bfloat16), rims[:halo_rows].astype(jnp.bfloat16), "seq", -1
    )
    collected = collected + came_low.astype(jnp.float32) + came_high.astype(jnp.float32)
    edges = jnp.concatenate(
        [edge_low, rims.astype(jnp.bfloat16), edge_high], axis=0
    ).astype(rims.dtype)
    token_grads = [
        dquery.reshape(tok_rows, features).astype(jnp.bfloat16),
        collected[:, :features].astype(jnp.bfloat16),
        collected[:, features:].astype(jnp.bfloat16),
        grad_gate,
    ]
    own_grad = ext_grad[halo_rows : halo_rows + atom_rows]
    own_grad = jnp.concatenate(
        [
            own_grad[:halo_rows] + edges[:halo_rows],
            own_grad[halo_rows : atom_rows - halo_rows],
            own_grad[atom_rows - halo_rows :] + edges[3 * halo_rows :],
        ],
        axis=0,
    )
    atom_grads = [
        aquery_grad.reshape(atom_rows, atom_feat).astype(jnp.bfloat16),
        own_grad[:, :atom_feat].astype(jnp.bfloat16),
        own_grad[:, atom_feat:].astype(jnp.bfloat16),
        agrad_gate,
    ]
    agrad_input = jnp.dot(atom_grads[0], w_atom_all[0].T, preferred_element_type=jnp.float32)
    for which in range(1, 4):
        agrad_input = agrad_input + jnp.dot(
            atom_grads[which], w_atom_all[which].T, preferred_element_type=jnp.float32
        )
    atoms_part = norm_back(atoms.astype(jnp.float32), gain_atom, agrad_input)
    cond_grad = jnp.dot(token_pick.T, agrad_input, precision=HIGHEST)
    cond_term = jnp.dot(cond_grad, w_cond.astype(jnp.float32).T, precision=HIGHEST)
    grad_normed = cond_term
    for which in range(4):
        grad_normed = grad_normed + jnp.dot(
            token_grads[which], w_token[which].T, preferred_element_type=jnp.float32
        )
    single_part = norm_back(single.astype(jnp.float32), gain_single, grad_normed)
    token_total, atom_total, single_total, atoms_total = head_sum(
        [token_part, atom_part, single_part, atoms_part], "head"
    )
    return (
        token_total.astype(jnp.bfloat16),
        atom_total.astype(jnp.bfloat16),
        single_total.astype(jnp.bfloat16),
        atoms_total.astype(jnp.bfloat16),
        grad_pair,
        grad_abias,
    )


def solution(mesh):
    return jax.shard_map(
        body,
        mesh=mesh,
        in_specs=(
            P("seq", None),
            P("seq", None),
            P(),
            P(),
            P(None, None, "head"),
            P("head", None),
            P(),
            P(None, None, "head"),
            P("head", None),
            P("head", "seq", None),
            P("head", "seq", None),
            P("seq", None),
            P("seq"),
            P("seq", None),
            P("seq"),
            P("seq", None),
            P("seq", None),
        ),
        out_specs=(
            P("seq", None),
            P("seq", None),
            P("seq", None),
            P("seq", None),
            P("head", "seq", None),
            P("head", "seq", None),
        ),
        check_vma=False,
    )
```

```python
import jax
import jax.numpy as jnp
from jax import lax
from jax.sharding import PartitionSpec as P

DH = 24
DA = 32
BLK = 128
S = 4
WIN = 2
AQ = 32
AK = 128


EPSILON = 1e-05
ONE_HOT_PRECISION = lax.Precision.HIGH


def shifted(block, axis, distance):
    devices = range(lax.axis_size(axis))
    route = [((i - distance) % len(devices), i) for i in devices]
    return lax.ppermute(block, axis, route)


def extended_2(block, sides, width):
    for axis, dim in sides:
        count = lax.axis_size(axis)
        forward = [(i, i + 1) for i in range(count - 1)]
        forward.append((count - 1, 0))
        backward = [(target, source) for source, target in forward]
        low = lax.ppermute(
            lax.slice_in_dim(block, block.shape[dim] - width, None, axis=dim), axis, forward
        )
        high = lax.ppermute(lax.slice_in_dim(block, 0, width, axis=dim), axis, backward)
        block = jnp.concatenate([low, block, high], axis=dim)
    return block


def head_sum(parts, axis):
    count = lax.axis_size(axis)
    if count != 4:
        return [lax.psum(p.astype(jnp.bfloat16), axis) for p in parts]
    pieces = []
    for part in parts:
        for col in range(part.shape[1] // 128):
            pieces.append(part[:, col * 128 : (col + 1) * 128])
    buf = jnp.concatenate(pieces, axis=0)
    rows = buf.shape[0]
    place = lax.axis_index(axis)
    low_bit = place % 2
    high_bit = (place // 2) % 2
    pair_near = [(i, i ^ 1) for i in range(count)]
    pair_far = [(i, i ^ 2) for i in range(count)]
    halves = buf.reshape(2, rows // 2, 128)
    keep = jnp.where(low_bit == 0, halves[0], halves[1])
    give = jnp.where(low_bit == 0, halves[1], halves[0])
    got = lax.ppermute(give.astype(jnp.bfloat16), axis, pair_near)
    summed = (keep + got.astype(jnp.float32)).reshape(2, rows // 4, 128)
    keep = jnp.where(high_bit == 0, summed[0], summed[1])
    give = jnp.where(high_bit == 0, summed[1], summed[0])
    got = lax.ppermute(give.astype(jnp.bfloat16), axis, pair_far)
    own = (keep + got.astype(jnp.float32)).astype(jnp.bfloat16)
    got = lax.ppermute(own, axis, pair_far)
    half = jnp.where(
        high_bit == 0, jnp.concatenate([own, got], axis=0), jnp.concatenate([got, own], axis=0)
    )
    got = lax.ppermute(half, axis, pair_near)
    full = jnp.where(
        low_bit == 0, jnp.concatenate([half, got], axis=0), jnp.concatenate([got, half], axis=0)
    )
    outs = []
    start = 0
    for part in parts:
        width = part.shape[1] // 128
        rows_here = part.shape[0]
        cols = [full[start + k * rows_here : start + (k + 1) * rows_here] for k in range(width)]
        start += width * rows_here
        outs.append(jnp.concatenate(cols, axis=1) if width > 1 else cols[0])
    return outs


def norm_rows(inputs, gains):
    row_mean = jnp.mean(inputs, axis=-1, keepdims=True)
    centred = inputs - row_mean
    variance = jnp.mean(centred * centred, axis=-1, keepdims=True)
    return centred * lax.rsqrt(variance + EPSILON) * gains


def norm_back(inputs, gains, cotangent):
    row_mean = jnp.mean(inputs, axis=-1, keepdims=True)
    centred = inputs - row_mean
    variance = jnp.mean(centred * centred, axis=-1, keepdims=True)
    inverse = lax.rsqrt(variance + EPSILON)
    standard = centred * inverse
    scaled = cotangent * gains
    return inverse * (
        scaled
        - jnp.mean(scaled, axis=-1, keepdims=True)
        - standard * jnp.mean(scaled * standard, axis=-1, keepdims=True)
    )


def attend_local(queries, key_block, value_block, bias_block, valid_keys, scaling):
    scores = (
        jnp.einsum("bqhd,bkhd->bhqk", queries, key_block, preferred_element_type=jnp.float32)
        * scaling
        + bias_block
    )
    scores = jnp.where(valid_keys[:, None, None, :], scores, -jnp.inf)
    row_max = jnp.max(scores, axis=-1, keepdims=True)
    exponent = jnp.exp(scores - row_max)
    weights = exponent / jnp.sum(exponent, axis=-1, keepdims=True)
    weights_low = weights.astype(jnp.bfloat16)
    attended = jnp.einsum(
        "bhqk,bkhd->bqhd", weights_low, value_block, preferred_element_type=jnp.float32
    )
    return (weights, weights_low, attended)


def attend_grads(
    weights, weights_low, queries, key_block, value_block, grad_out, row_delta, scaling
):
    weight_grad = jnp.einsum(
        "bqhd,bkhd->bhqk", grad_out, value_block, preferred_element_type=jnp.float32
    )
    dscore = weights * (weight_grad - row_delta[..., None])
    dscore_low = dscore.astype(jnp.bfloat16)
    dquery = (
        jnp.einsum("bhqk,bkhd->bqhd", dscore_low, key_block, preferred_element_type=jnp.float32)
        * scaling
    )
    key_grad = (
        jnp.einsum("bhqk,bqhd->bkhd", dscore_low, queries, preferred_element_type=jnp.float32)
        * scaling
    )
    dvalue = jnp.einsum(
        "bhqk,bqhd->bkhd", weights_low, grad_out, preferred_element_type=jnp.float32
    )
    return (dscore_low, dquery, key_grad, dvalue)


def body(
    single,
    atoms,
    gain_single,
    gain_atom,
    w_token,
    w_token_out,
    w_cond,
    w_atom,
    w_atom_out,
    pair_bias,
    atom_bias,
    used_blocks,
    used_count,
    atom_counts,
    key_offset,
    grad_token,
    grad_atom,
):
    device = lax.axis_index("seq")
    shards = lax.axis_size("seq")
    tok_rows = single.shape[0]
    blocks_here = tok_rows // BLK
    local_heads = w_token.shape[2] // DH
    features = local_heads * DH
    scaling = DH ** (-0.5)
    normed_low = norm_rows(single.astype(jnp.float32), gain_single).astype(jnp.bfloat16)
    token_width = w_token.shape[2]
    projected_all = jnp.dot(
        normed_low,
        w_token.transpose(1, 0, 2).reshape(w_token.shape[1], 4 * token_width),
        preferred_element_type=jnp.float32,
    )
    projected = [
        projected_all[:, which * token_width : (which + 1) * token_width] for which in range(4)
    ]
    queries = projected[0].astype(jnp.bfloat16)
    gate_act = jax.nn.sigmoid(projected[3])
    key_value = jnp.concatenate(
        [projected[1].astype(jnp.bfloat16), projected[2].astype(jnp.bfloat16)], axis=1
    )
    owner_dev = used_blocks // blocks_here
    relative = jnp.mod(owner_dev - device, shards)
    relative = jnp.where(relative > shards // 2, relative - shards, relative)
    pieces = [key_value for distance in range(-WIN, WIN + 1)]
    for distance in range(-WIN, WIN + 1):
        if distance != 0:
            pieces[distance + WIN] = shifted(key_value, "seq", -distance)
    window = jnp.stack(pieces)
    candidates = (2 * WIN + 1) * blocks_here
    window_flat = window.reshape(candidates, BLK * 2 * features)
    picked = (relative + WIN) * blocks_here + used_blocks % blocks_here
    selector_mask = picked[:, :, None] == jnp.arange(candidates, dtype=jnp.int32)[None, None, :]
    selector = selector_mask.astype(jnp.bfloat16)
    stashed = jnp.einsum(
        "bsc,cx->bsx", selector, window_flat, preferred_element_type=jnp.float32
    ).astype(jnp.bfloat16)
    stashed = stashed.reshape(blocks_here, S, BLK, 2 * features)
    key_blocks = stashed[..., :features].reshape(blocks_here, S * BLK, local_heads, DH)
    value_blocks = stashed[..., features:].reshape(blocks_here, S * BLK, local_heads, DH)
    query_blocks = queries.reshape(blocks_here, BLK, local_heads, DH)
    bias_blocks = (
        pair_bias.reshape(local_heads, blocks_here, BLK, S * BLK)
        .transpose(1, 0, 2, 3)
        .astype(jnp.float32)
    )
    valid_keys = jnp.repeat(
        jnp.arange(S, dtype=jnp.int32)[None, :] < used_count[:, None], BLK, axis=1
    )
    weights, weights_low, attended = attend_local(
        query_blocks, key_blocks, value_blocks, bias_blocks, valid_keys, scaling
    )
    attended = attended.reshape(tok_rows, features)
    token_part = jnp.dot(
        (attended * gate_act).astype(jnp.bfloat16), w_token_out, preferred_element_type=jnp.float32
    )
    grad_gated = jnp.dot(grad_token, w_token_out.T, preferred_element_type=jnp.float32)
    grad_attended = (grad_gated * gate_act).astype(jnp.bfloat16)
    grad_gate = (grad_gated * attended * gate_act * (1.0 - gate_act)).astype(jnp.bfloat16)
    row_delta = jnp.sum(
        (grad_attended.astype(jnp.float32) * attended).reshape(blocks_here, BLK, local_heads, DH),
        axis=-1,
    ).transpose(0, 2, 1)
    score_low, dquery, key_grad, dvalue = attend_grads(
        weights,
        weights_low,
        query_blocks,
        key_blocks,
        value_blocks,
        grad_attended.reshape(blocks_here, BLK, local_heads, DH),
        row_delta,
        scaling,
    )
    grad_pair = score_low.transpose(1, 0, 2, 3).reshape(local_heads, tok_rows, S * BLK)
    returned = jnp.concatenate(
        [
            key_grad.reshape(blocks_here, S, BLK, features),
            dvalue.reshape(blocks_here, S, BLK, features),
        ],
        axis=-1,
    )
    returned_flat = returned.reshape(blocks_here, S, BLK * 2 * features)
    outgoing = jnp.einsum(
        "bsc,bsx->cx", selector_mask.astype(jnp.float32), returned_flat, precision=ONE_HOT_PRECISION
    )
    outgoing = outgoing.reshape(2 * WIN + 1, tok_rows, 2 * features)
    collected = outgoing[WIN]
    for distance in range(-WIN, WIN + 1):
        if distance != 0:
            collected = collected + shifted(
                outgoing[distance + WIN].astype(jnp.bfloat16), "seq", distance
            ).astype(jnp.float32)
    token_grads = [
        dquery.reshape(tok_rows, features).astype(jnp.bfloat16),
        collected[:, :features].astype(jnp.bfloat16),
        collected[:, features:].astype(jnp.bfloat16),
        grad_gate,
    ]
    w_atom_all, w_atom_out_all, atom_bias_all = (w_atom, w_atom_out, atom_bias)
    atom_rows = atoms.shape[0]
    heads_atom = w_atom_all.shape[2] // DA
    atom_feat = heads_atom * DA
    halo_rows = AK // 2
    windows_here = atom_rows // AQ
    group_span = AK // AQ + 1
    slab_rows = group_span * AQ
    atom_scaling = DA ** (-0.5)
    normed_atoms = norm_rows(atoms.astype(jnp.float32), gain_atom)
    counts = atom_counts[0]
    ends = jnp.cumsum(counts)
    atom_place = jnp.arange(atom_rows, dtype=jnp.int32)
    token_local = jnp.sum((ends[None, :] <= atom_place[:, None]).astype(jnp.int32), axis=1)
    token_pick = (token_local[:, None] == jnp.arange(tok_rows, dtype=jnp.int32)[None, :]).astype(
        jnp.float32
    )
    condition = jnp.dot(normed_low, w_cond, preferred_element_type=jnp.float32)
    atom_input = (normed_atoms + jnp.dot(token_pick, condition, precision=ONE_HOT_PRECISION)).astype(
        jnp.bfloat16
    )
    atom_width = w_atom_all.shape[2]
    atom_proj_all = jnp.dot(
        atom_input,
        w_atom_all.transpose(1, 0, 2).reshape(w_atom_all.shape[1], 4 * atom_width),
        preferred_element_type=jnp.float32,
    )
    atom_proj = [
        atom_proj_all[:, which * atom_width : (which + 1) * atom_width] for which in range(4)
    ]
    atom_gate = jax.nn.sigmoid(atom_proj[3])
    atom_kv = jnp.concatenate(
        [atom_proj[1].astype(jnp.bfloat16), atom_proj[2].astype(jnp.bfloat16)], axis=1
    )
    extended = extended_2(atom_kv, (("seq", 0),), halo_rows)
    ext_groups = extended.reshape(windows_here + AK // AQ, AQ, 2 * atom_feat)
    slabs = jnp.concatenate(
        [ext_groups[step : step + windows_here] for step in range(group_span)], axis=1
    )
    shift_here = key_offset + halo_rows
    placer_mask = (
        jnp.arange(slab_rows, dtype=jnp.int32)[None, None, :]
        == jnp.arange(AK, dtype=jnp.int32)[None, :, None] + shift_here[:, None, None]
    )
    window_kv = jnp.einsum(
        "wrs,wsf->wrf", placer_mask.astype(jnp.bfloat16), slabs, preferred_element_type=jnp.float32
    ).astype(jnp.bfloat16)
    atom_keys = window_kv[..., :atom_feat].reshape(windows_here, AK, heads_atom, DA)
    atom_values = window_kv[..., atom_feat:].reshape(windows_here, AK, heads_atom, DA)
    atom_queries = atom_proj[0].astype(jnp.bfloat16).reshape(windows_here, AQ, heads_atom, DA)
    atom_bias_blocks = (
        atom_bias_all.reshape(heads_atom, windows_here, AQ, AK)
        .transpose(1, 0, 2, 3)
        .astype(jnp.float32)
    )
    all_valid = jnp.ones((windows_here, AK), dtype=bool)
    aweights, aweights_low, atom_attended = attend_local(
        atom_queries, atom_keys, atom_values, atom_bias_blocks, all_valid, atom_scaling
    )
    atom_attended = atom_attended.reshape(atom_rows, atom_feat)
    atom_part = jnp.dot(
        (atom_attended * atom_gate).astype(jnp.bfloat16),
        w_atom_out_all,
        preferred_element_type=jnp.float32,
    )
    agrad_gated = jnp.dot(grad_atom, w_atom_out_all.T, preferred_element_type=jnp.float32)
    agrad_attended = (agrad_gated * atom_gate).astype(jnp.bfloat16)
    agrad_gate = (agrad_gated * atom_attended * atom_gate * (1.0 - atom_gate)).astype(jnp.bfloat16)
    atom_delta = jnp.sum(
        (agrad_attended.astype(jnp.float32) * atom_attended).reshape(
            windows_here, AQ, heads_atom, DA
        ),
        axis=-1,
    ).transpose(0, 2, 1)
    ascore_low, aquery_grad, akey_grad, avalue_grad = attend_grads(
        aweights,
        aweights_low,
        atom_queries,
        atom_keys,
        atom_values,
        agrad_attended.reshape(windows_here, AQ, heads_atom, DA),
        atom_delta,
        atom_scaling,
    )
    grad_abias = ascore_low.transpose(1, 0, 2, 3).reshape(heads_atom, atom_rows, AK)
    spread_grads = jnp.concatenate(
        [
            akey_grad.reshape(windows_here, AK, atom_feat),
            avalue_grad.reshape(windows_here, AK, atom_feat),
        ],
        axis=-1,
    )
    slab_grads = jnp.einsum(
        "wrs,wrf->wsf", placer_mask.astype(jnp.float32), spread_grads, precision=ONE_HOT_PRECISION
    )
    slab_grads = slab_grads.reshape(windows_here, group_span, AQ, 2 * atom_feat)
    ext_grad = jnp.pad(slab_grads[:, 0], ((0, group_span - 1), (0, 0), (0, 0)))
    for step in range(1, group_span):
        ext_grad = ext_grad + jnp.pad(
            slab_grads[:, step], ((step, group_span - 1 - step), (0, 0), (0, 0))
        )
    ext_grad = ext_grad.reshape(atom_rows + 2 * halo_rows, 2 * atom_feat)
    rims = jnp.concatenate([ext_grad[:halo_rows], ext_grad[atom_rows + halo_rows :]], axis=0)
    edges = extended_2(rims.astype(jnp.bfloat16), (("seq", 0),), halo_rows).astype(rims.dtype)
    own_grad = ext_grad[halo_rows : halo_rows + atom_rows]
    own_grad = jnp.concatenate(
        [
            own_grad[:halo_rows] + edges[:halo_rows],
            own_grad[halo_rows : atom_rows - halo_rows],
            own_grad[atom_rows - halo_rows :] + edges[3 * halo_rows :],
        ],
        axis=0,
    )
    atom_grads = [
        aquery_grad.reshape(atom_rows, atom_feat).astype(jnp.bfloat16),
        own_grad[:, :atom_feat].astype(jnp.bfloat16),
        own_grad[:, atom_feat:].astype(jnp.bfloat16),
        agrad_gate,
    ]
    agrad_input = jnp.dot(
        jnp.concatenate(atom_grads, axis=1),
        w_atom_all.transpose(0, 2, 1).reshape(4 * atom_width, w_atom_all.shape[1]),
        preferred_element_type=jnp.float32,
    )
    atoms_part = norm_back(atoms.astype(jnp.float32), gain_atom, agrad_input)
    cond_grad = jnp.dot(token_pick.T, agrad_input, precision=ONE_HOT_PRECISION)
    cond_term = jnp.dot(cond_grad, w_cond.astype(jnp.float32).T, precision=ONE_HOT_PRECISION)
    grad_normed = cond_term + jnp.dot(
        jnp.concatenate(token_grads, axis=1),
        w_token.transpose(0, 2, 1).reshape(4 * token_width, w_token.shape[1]),
        preferred_element_type=jnp.float32,
    )
    single_part = norm_back(single.astype(jnp.float32), gain_single, grad_normed)
    token_total, atom_total, single_total, atoms_total = head_sum(
        [token_part, atom_part, single_part, atoms_part], "head"
    )
    return (
        token_total.astype(jnp.bfloat16),
        atom_total.astype(jnp.bfloat16),
        single_total.astype(jnp.bfloat16),
        atoms_total.astype(jnp.bfloat16),
        grad_pair,
        grad_abias,
    )


def solution(mesh):
    return jax.shard_map(
        body,
        mesh=mesh,
        in_specs=(
            P("seq", None),
            P("seq", None),
            P(),
            P(),
            P(None, None, "head"),
            P("head", None),
            P(),
            P(None, None, "head"),
            P("head", None),
            P("head", "seq", None),
            P("head", "seq", None),
            P("seq", None),
            P("seq"),
            P("seq", None),
            P("seq"),
            P("seq", None),
            P("seq", None),
        ),
        out_specs=(
            P("seq", None),
            P("seq", None),
            P("seq", None),
            P("seq", None),
            P("head", "seq", None),
            P("head", "seq", None),
        ),
        check_vma=False,
    )
```

```python
import jax
import jax.numpy as jnp
from jax import lax
from jax.sharding import PartitionSpec as P

DH = 24
DA = 32
BLK = 128
S = 4
WIN = 2
AQ = 32
AK = 128


EPSILON = 1e-05
HIGHEST = lax.Precision.HIGHEST


def shifted(block, axis, distance):
    devices = range(lax.axis_size(axis))
    route = [((i - distance) % len(devices), i) for i in devices]
    return lax.ppermute(block, axis, route)


def shifted_pair(block, extra, axis, distance):
    rows = block.shape[0]
    padded = jnp.pad(extra, ((0, 0), (0, block.shape[1] - extra.shape[1])))
    both = shifted(jnp.concatenate([block, padded], axis=0), axis, distance)
    return both[:rows], both[rows:, : extra.shape[1]]


def extended_2(block, sides, width):
    for axis, dim in sides:
        count = lax.axis_size(axis)
        forward = [(i, i + 1) for i in range(count - 1)]
        forward.append((count - 1, 0))
        backward = [(target, source) for source, target in forward]
        low = lax.ppermute(
            lax.slice_in_dim(block, block.shape[dim] - width, None, axis=dim), axis, forward
        )
        high = lax.ppermute(lax.slice_in_dim(block, 0, width, axis=dim), axis, backward)
        block = jnp.concatenate([low, block, high], axis=dim)
    return block


def head_sum(parts, axis):
    count = lax.axis_size(axis)
    if count != 4:
        return [lax.psum(p.astype(jnp.bfloat16), axis) for p in parts]
    pieces = []
    for part in parts:
        for col in range(part.shape[1] // 128):
            pieces.append(part[:, col * 128 : (col + 1) * 128])
    buf = jnp.concatenate(pieces, axis=0)
    rows = buf.shape[0]
    place = lax.axis_index(axis)
    low_bit = place % 2
    high_bit = (place // 2) % 2
    pair_near = [(i, i ^ 1) for i in range(count)]
    pair_far = [(i, i ^ 2) for i in range(count)]
    halves = buf.reshape(2, rows // 2, 128)
    keep = jnp.where(low_bit == 0, halves[0], halves[1])
    give = jnp.where(low_bit == 0, halves[1], halves[0])
    got = lax.ppermute(give.astype(jnp.bfloat16), axis, pair_near)
    summed = (keep + got.astype(jnp.float32)).reshape(2, rows // 4, 128)
    keep = jnp.where(high_bit == 0, summed[0], summed[1])
    give = jnp.where(high_bit == 0, summed[1], summed[0])
    got = lax.ppermute(give.astype(jnp.bfloat16), axis, pair_far)
    own = (keep + got.astype(jnp.float32)).astype(jnp.bfloat16)
    got = lax.ppermute(own, axis, pair_far)
    half = jnp.where(
        high_bit == 0, jnp.concatenate([own, got], axis=0), jnp.concatenate([got, own], axis=0)
    )
    got = lax.ppermute(half, axis, pair_near)
    full = jnp.where(
        low_bit == 0, jnp.concatenate([half, got], axis=0), jnp.concatenate([got, half], axis=0)
    )
    outs = []
    start = 0
    for part in parts:
        width = part.shape[1] // 128
        rows_here = part.shape[0]
        cols = [full[start + k * rows_here : start + (k + 1) * rows_here] for k in range(width)]
        start += width * rows_here
        outs.append(jnp.concatenate(cols, axis=1) if width > 1 else cols[0])
    return outs


def norm_rows(inputs, gains):
    row_mean = jnp.mean(inputs, axis=-1, keepdims=True)
    centred = inputs - row_mean
    variance = jnp.mean(centred * centred, axis=-1, keepdims=True)
    return centred * lax.rsqrt(variance + EPSILON) * gains


def norm_back(inputs, gains, cotangent):
    row_mean = jnp.mean(inputs, axis=-1, keepdims=True)
    centred = inputs - row_mean
    variance = jnp.mean(centred * centred, axis=-1, keepdims=True)
    inverse = lax.rsqrt(variance + EPSILON)
    standard = centred * inverse
    scaled = cotangent * gains
    return inverse * (
        scaled
        - jnp.mean(scaled, axis=-1, keepdims=True)
        - standard * jnp.mean(scaled * standard, axis=-1, keepdims=True)
    )


def attend_local(queries, key_block, value_block, bias_block, valid_keys, scaling):
    scores = (
        jnp.einsum("bqhd,bkhd->bhqk", queries, key_block, preferred_element_type=jnp.float32)
        * scaling
        + bias_block
    )
    scores = jnp.where(valid_keys[:, None, None, :], scores, -jnp.inf)
    row_max = jnp.max(scores, axis=-1, keepdims=True)
    exponent = jnp.exp(scores - row_max)
    weights = exponent / jnp.sum(exponent, axis=-1, keepdims=True)
    weights_low = weights.astype(jnp.bfloat16)
    attended = jnp.einsum(
        "bhqk,bkhd->bqhd", weights_low, value_block, preferred_element_type=jnp.float32
    )
    return (weights, weights_low, attended)


def attend_grads(
    weights, weights_low, queries, key_block, value_block, grad_out, row_delta, scaling
):
    weight_grad = jnp.einsum(
        "bqhd,bkhd->bhqk", grad_out, value_block, preferred_element_type=jnp.float32
    )
    dscore = weights * (weight_grad - row_delta[..., None])
    dscore_low = dscore.astype(jnp.bfloat16)
    dquery = (
        jnp.einsum("bhqk,bkhd->bqhd", dscore_low, key_block, preferred_element_type=jnp.float32)
        * scaling
    )
    key_grad = (
        jnp.einsum("bhqk,bqhd->bkhd", dscore_low, queries, preferred_element_type=jnp.float32)
        * scaling
    )
    dvalue = jnp.einsum(
        "bhqk,bqhd->bkhd", weights_low, grad_out, preferred_element_type=jnp.float32
    )
    return (dscore_low, dquery, key_grad, dvalue)


def body(
    single,
    atoms,
    gain_single,
    gain_atom,
    w_token,
    w_token_out,
    w_cond,
    w_atom,
    w_atom_out,
    pair_bias,
    atom_bias,
    used_blocks,
    used_count,
    atom_counts,
    key_offset,
    grad_token,
    grad_atom,
):
    device = lax.axis_index("seq")
    shards = lax.axis_size("seq")
    tok_rows = single.shape[0]
    blocks_here = tok_rows // BLK
    local_heads = w_token.shape[2] // DH
    features = local_heads * DH
    scaling = DH ** (-0.5)
    normed_low = norm_rows(single.astype(jnp.float32), gain_single).astype(jnp.bfloat16)
    projected = [
        jnp.dot(normed_low, w_token[which], preferred_element_type=jnp.float32)
        for which in range(4)
    ]
    queries = projected[0].astype(jnp.bfloat16)
    gate_act = jax.nn.sigmoid(projected[3])
    key_value = jnp.concatenate(
        [projected[1].astype(jnp.bfloat16), projected[2].astype(jnp.bfloat16)], axis=1
    )
    w_atom_all, w_atom_out_all, atom_bias_all = (w_atom, w_atom_out, atom_bias)
    atom_rows = atoms.shape[0]
    heads_atom = w_atom_all.shape[2] // DA
    atom_feat = heads_atom * DA
    halo_rows = AK // 2
    windows_here = atom_rows // AQ
    group_span = AK // AQ + 1
    slab_rows = group_span * AQ
    atom_scaling = DA ** (-0.5)
    normed_atoms = norm_rows(atoms.astype(jnp.float32), gain_atom)
    counts = atom_counts[0]
    ends = jnp.cumsum(counts)
    atom_place = jnp.arange(atom_rows, dtype=jnp.int32)
    token_local = jnp.sum((ends[None, :] <= atom_place[:, None]).astype(jnp.int32), axis=1)
    token_pick = (token_local[:, None] == jnp.arange(tok_rows, dtype=jnp.int32)[None, :]).astype(
        jnp.float32
    )
    condition = jnp.dot(normed_low, w_cond, preferred_element_type=jnp.float32)
    atom_input = (normed_atoms + jnp.dot(token_pick, condition, precision=HIGHEST)).astype(
        jnp.bfloat16
    )
    atom_proj = [
        jnp.dot(atom_input, w_atom_all[which], preferred_element_type=jnp.float32)
        for which in range(4)
    ]
    atom_gate = jax.nn.sigmoid(atom_proj[3])
    atom_kv = jnp.concatenate(
        [atom_proj[1].astype(jnp.bfloat16), atom_proj[2].astype(jnp.bfloat16)], axis=1
    )
    owner_dev = used_blocks // blocks_here
    relative = jnp.mod(owner_dev - device, shards)
    relative = jnp.where(relative > shards // 2, relative - shards, relative)
    pieces = [key_value for distance in range(-WIN, WIN + 1)]
    for distance in range(-WIN, WIN + 1):
        if abs(distance) > 1:
            pieces[distance + WIN] = shifted(key_value, "seq", -distance)
    pieces[WIN - 1], halo_low = shifted_pair(
        key_value, atom_kv[atom_kv.shape[0] - AK // 2 :], "seq", 1
    )
    pieces[WIN + 1], halo_high = shifted_pair(key_value, atom_kv[: AK // 2], "seq", -1)
    window = jnp.stack(pieces)
    candidates = (2 * WIN + 1) * blocks_here
    window_flat = window.reshape(candidates, BLK * 2 * features)
    picked = (relative + WIN) * blocks_here + used_blocks % blocks_here
    selector_mask = picked[:, :, None] == jnp.arange(candidates, dtype=jnp.int32)[None, None, :]
    selector = selector_mask.astype(jnp.bfloat16)
    stashed = jnp.einsum(
        "bsc,cx->bsx", selector, window_flat, preferred_element_type=jnp.float32
    ).astype(jnp.bfloat16)
    stashed = stashed.reshape(blocks_here, S, BLK, 2 * features)
    key_blocks = stashed[..., :features].reshape(blocks_here, S * BLK, local_heads, DH)
    value_blocks = stashed[..., features:].reshape(blocks_here, S * BLK, local_heads, DH)
    query_blocks = queries.reshape(blocks_here, BLK, local_heads, DH)
    bias_blocks = (
        pair_bias.reshape(local_heads, blocks_here, BLK, S * BLK)
        .transpose(1, 0, 2, 3)
        .astype(jnp.float32)
    )
    valid_keys = jnp.repeat(
        jnp.arange(S, dtype=jnp.int32)[None, :] < used_count[:, None], BLK, axis=1
    )
    weights, weights_low, attended = attend_local(
        query_blocks, key_blocks, value_blocks, bias_blocks, valid_keys, scaling
    )
    attended = attended.reshape(tok_rows, features)
    token_part = jnp.dot(
        (attended * gate_act).astype(jnp.bfloat16), w_token_out, preferred_element_type=jnp.float32
    )
    grad_gated = jnp.dot(grad_token, w_token_out.T, preferred_element_type=jnp.float32)
    grad_attended = (grad_gated * gate_act).astype(jnp.bfloat16)
    grad_gate = (grad_gated * attended * gate_act * (1.0 - gate_act)).astype(jnp.bfloat16)
    row_delta = jnp.sum(
        (grad_attended.astype(jnp.float32) * attended).reshape(blocks_here, BLK, local_heads, DH),
        axis=-1,
    ).transpose(0, 2, 1)
    score_low, dquery, key_grad, dvalue = attend_grads(
        weights,
        weights_low,
        query_blocks,
        key_blocks,
        value_blocks,
        grad_attended.reshape(blocks_here, BLK, local_heads, DH),
        row_delta,
        scaling,
    )
    grad_pair = score_low.transpose(1, 0, 2, 3).reshape(local_heads, tok_rows, S * BLK)
    returned = jnp.concatenate(
        [
            key_grad.reshape(blocks_here, S, BLK, features),
            dvalue.reshape(blocks_here, S, BLK, features),
        ],
        axis=-1,
    )
    returned_flat = returned.reshape(blocks_here, S, BLK * 2 * features)
    outgoing = jnp.einsum(
        "bsc,bsx->cx", selector_mask.astype(jnp.float32), returned_flat, precision=HIGHEST
    )
    outgoing = outgoing.reshape(2 * WIN + 1, tok_rows, 2 * features)
    extended = jnp.concatenate([halo_low, atom_kv, halo_high], axis=0)
    ext_groups = extended.reshape(windows_here + AK // AQ, AQ, 2 * atom_feat)
    slabs = jnp.concatenate(
        [ext_groups[step : step + windows_here] for step in range(group_span)], axis=1
    )
    shift_here = key_offset + halo_rows
    placer_mask = (
        jnp.arange(slab_rows, dtype=jnp.int32)[None, None, :]
        == jnp.arange(AK, dtype=jnp.int32)[None, :, None] + shift_here[:, None, None]
    )
    window_kv = jnp.einsum(
        "wrs,wsf->wrf", placer_mask.astype(jnp.bfloat16), slabs, preferred_element_type=jnp.float32
    ).astype(jnp.bfloat16)
    atom_keys = window_kv[..., :atom_feat].reshape(windows_here, AK, heads_atom, DA)
    atom_values = window_kv[..., atom_feat:].reshape(windows_here, AK, heads_atom, DA)
    atom_queries = atom_proj[0].astype(jnp.bfloat16).reshape(windows_here, AQ, heads_atom, DA)
    atom_bias_blocks = (
        atom_bias_all.reshape(heads_atom, windows_here, AQ, AK)
        .transpose(1, 0, 2, 3)
        .astype(jnp.float32)
    )
    all_valid = jnp.ones((windows_here, AK), dtype=bool)
    aweights, aweights_low, atom_attended = attend_local(
        atom_queries, atom_keys, atom_values, atom_bias_blocks, all_valid, atom_scaling
    )
    atom_attended = atom_attended.reshape(atom_rows, atom_feat)
    atom_part = jnp.dot(
        (atom_attended * atom_gate).astype(jnp.bfloat16),
        w_atom_out_all,
        preferred_element_type=jnp.float32,
    )
    agrad_gated = jnp.dot(grad_atom, w_atom_out_all.T, preferred_element_type=jnp.float32)
    agrad_attended = (agrad_gated * atom_gate).astype(jnp.bfloat16)
    agrad_gate = (agrad_gated * atom_attended * atom_gate * (1.0 - atom_gate)).astype(jnp.bfloat16)
    atom_delta = jnp.sum(
        (agrad_attended.astype(jnp.float32) * atom_attended).reshape(
            windows_here, AQ, heads_atom, DA
        ),
        axis=-1,
    ).transpose(0, 2, 1)
    ascore_low, aquery_grad, akey_grad, avalue_grad = attend_grads(
        aweights,
        aweights_low,
        atom_queries,
        atom_keys,
        atom_values,
        agrad_attended.reshape(windows_here, AQ, heads_atom, DA),
        atom_delta,
        atom_scaling,
    )
    grad_abias = ascore_low.transpose(1, 0, 2, 3).reshape(heads_atom, atom_rows, AK)
    spread_grads = jnp.concatenate(
        [
            akey_grad.reshape(windows_here, AK, atom_feat),
            avalue_grad.reshape(windows_here, AK, atom_feat),
        ],
        axis=-1,
    )
    slab_grads = jnp.einsum(
        "wrs,wrf->wsf", placer_mask.astype(jnp.float32), spread_grads, precision=HIGHEST
    )
    slab_grads = slab_grads.reshape(windows_here, group_span, AQ, 2 * atom_feat)
    ext_grad = jnp.pad(slab_grads[:, 0], ((0, group_span - 1), (0, 0), (0, 0)))
    for step in range(1, group_span):
        ext_grad = ext_grad + jnp.pad(
            slab_grads[:, step], ((step, group_span - 1 - step), (0, 0), (0, 0))
        )
    ext_grad = ext_grad.reshape(atom_rows + 2 * halo_rows, 2 * atom_feat)
    rims = jnp.concatenate([ext_grad[:halo_rows], ext_grad[atom_rows + halo_rows :]], axis=0)
    collected = outgoing[WIN]
    for distance in range(-WIN, WIN + 1):
        if abs(distance) > 1:
            collected = collected + shifted(
                outgoing[distance + WIN].astype(jnp.bfloat16), "seq", distance
            ).astype(jnp.float32)
    came_low, edge_low = shifted_pair(
        outgoing[WIN + 1].astype(jnp.bfloat16), rims[halo_rows:].astype(jnp.bfloat16), "seq", 1
    )
    came_high, edge_high = shifted_pair(
        outgoing[WIN - 1].astype(jnp.bfloat16), rims[:halo_rows].astype(jnp.bfloat16), "seq", -1
    )
    collected = collected + came_low.astype(jnp.float32) + came_high.astype(jnp.float32)
    edges = jnp.concatenate(
        [edge_low, rims.astype(jnp.bfloat16), edge_high], axis=0
    ).astype(rims.dtype)
    token_grads = [
        dquery.reshape(tok_rows, features).astype(jnp.bfloat16),
        collected[:, :features].astype(jnp.bfloat16),
        collected[:, features:].astype(jnp.bfloat16),
        grad_gate,
    ]
    own_grad = ext_grad[halo_rows : halo_rows + atom_rows]
    own_grad = jnp.concatenate(
        [
            own_grad[:halo_rows] + edges[:halo_rows],
            own_grad[halo_rows : atom_rows - halo_rows],
            own_grad[atom_rows - halo_rows :] + edges[3 * halo_rows :],
        ],
        axis=0,
    )
    atom_grads = [
        aquery_grad.reshape(atom_rows, atom_feat).astype(jnp.bfloat16),
        own_grad[:, :atom_feat].astype(jnp.bfloat16),
        own_grad[:, atom_feat:].astype(jnp.bfloat16),
        agrad_gate,
    ]
    agrad_input = jnp.dot(atom_grads[0], w_atom_all[0].T, preferred_element_type=jnp.float32)
    for which in range(1, 4):
        agrad_input = agrad_input + jnp.dot(
            atom_grads[which], w_atom_all[which].T, preferred_element_type=jnp.float32
        )
    atoms_part = norm_back(atoms.astype(jnp.float32), gain_atom, agrad_input)
    cond_grad = jnp.dot(token_pick.T, agrad_input, precision=HIGHEST)
    cond_term = jnp.dot(cond_grad, w_cond.astype(jnp.float32).T, precision=HIGHEST)
    grad_normed = cond_term
    for which in range(4):
        grad_normed = grad_normed + jnp.dot(
            token_grads[which], w_token[which].T, preferred_element_type=jnp.float32
        )
    single_part = norm_back(single.astype(jnp.float32), gain_single, grad_normed)
    token_total, atom_total, single_total, atoms_total = head_sum(
        [token_part, atom_part, single_part, atoms_part], "head"
    )
    return (
        token_total.astype(jnp.bfloat16),
        atom_total.astype(jnp.bfloat16),
        single_total.astype(jnp.bfloat16),
        atoms_total.astype(jnp.bfloat16),
        grad_pair,
        grad_abias,
    )


def solution(mesh):
    return jax.shard_map(
        body,
        mesh=mesh,
        in_specs=(
            P("seq", None),
            P("seq", None),
            P(),
            P(),
            P(None, None, "head"),
            P("head", None),
            P(),
            P(None, None, "head"),
            P("head", None),
            P("head", "seq", None),
            P("head", "seq", None),
            P("seq", None),
            P("seq"),
            P("seq", None),
            P("seq"),
            P("seq", None),
            P("seq", None),
        ),
        out_specs=(
            P("seq", None),
            P("seq", None),
            P("seq", None),
            P("seq", None),
            P("head", "seq", None),
            P("head", "seq", None),
        ),
        check_vma=False,
    )
```

```python
import jax
import jax.numpy as jnp
from jax import lax
from jax.sharding import PartitionSpec as P

DH = 24
DA = 32
BLK = 128
S = 4
WIN = 2
AQ = 32
AK = 128


EPSILON = 1e-05
HIGHEST = lax.Precision.HIGHEST


def shifted(block, axis, distance):
    devices = range(lax.axis_size(axis))
    route = [((i - distance) % len(devices), i) for i in devices]
    return lax.ppermute(block, axis, route)


def extended_2(block, sides, width):
    for axis, dim in sides:
        count = lax.axis_size(axis)
        forward = [(i, i + 1) for i in range(count - 1)]
        forward.append((count - 1, 0))
        backward = [(target, source) for source, target in forward]
        low = lax.ppermute(
            lax.slice_in_dim(block, block.shape[dim] - width, None, axis=dim), axis, forward
        )
        high = lax.ppermute(lax.slice_in_dim(block, 0, width, axis=dim), axis, backward)
        block = jnp.concatenate([low, block, high], axis=dim)
    return block


def head_sum(parts, axis):
    count = lax.axis_size(axis)
    if count != 4:
        return [lax.psum(p.astype(jnp.bfloat16), axis) for p in parts]
    pieces = []
    for part in parts:
        for col in range(part.shape[1] // 128):
            pieces.append(part[:, col * 128 : (col + 1) * 128])
    buf = jnp.concatenate(pieces, axis=0)
    rows = buf.shape[0]
    place = lax.axis_index(axis)
    low_bit = place % 2
    high_bit = (place // 2) % 2
    pair_near = [(i, i ^ 1) for i in range(count)]
    pair_far = [(i, i ^ 2) for i in range(count)]
    halves = buf.reshape(2, rows // 2, 128)
    keep = jnp.where(low_bit == 0, halves[0], halves[1])
    give = jnp.where(low_bit == 0, halves[1], halves[0])
    got = lax.ppermute(give.astype(jnp.bfloat16), axis, pair_near)
    summed = (keep + got.astype(jnp.float32)).reshape(2, rows // 4, 128)
    keep = jnp.where(high_bit == 0, summed[0], summed[1])
    give = jnp.where(high_bit == 0, summed[1], summed[0])
    got = lax.ppermute(give.astype(jnp.bfloat16), axis, pair_far)
    own = (keep + got.astype(jnp.float32)).astype(jnp.bfloat16)
    got = lax.ppermute(own, axis, pair_far)
    half = jnp.where(
        high_bit == 0, jnp.concatenate([own, got], axis=0), jnp.concatenate([got, own], axis=0)
    )
    got = lax.ppermute(half, axis, pair_near)
    full = jnp.where(
        low_bit == 0, jnp.concatenate([half, got], axis=0), jnp.concatenate([got, half], axis=0)
    )
    outs = []
    start = 0
    for part in parts:
        width = part.shape[1] // 128
        rows_here = part.shape[0]
        cols = [full[start + k * rows_here : start + (k + 1) * rows_here] for k in range(width)]
        start += width * rows_here
        outs.append(jnp.concatenate(cols, axis=1) if width > 1 else cols[0])
    return outs


def head_sum_small(part, axis):
    count = lax.axis_size(axis)
    low = part.astype(jnp.bfloat16)
    if count != 4:
        return lax.psum(low, axis)
    got = lax.ppermute(low, axis, [(i, i ^ 1) for i in range(count)])
    low = (low.astype(jnp.float32) + got.astype(jnp.float32)).astype(jnp.bfloat16)
    got = lax.ppermute(low, axis, [(i, i ^ 2) for i in range(count)])
    return low.astype(jnp.float32) + got.astype(jnp.float32)


def norm_rows(inputs, gains):
    row_mean = jnp.mean(inputs, axis=-1, keepdims=True)
    centred = inputs - row_mean
    variance = jnp.mean(centred * centred, axis=-1, keepdims=True)
    return centred * lax.rsqrt(variance + EPSILON) * gains


def norm_back(inputs, gains, cotangent):
    row_mean = jnp.mean(inputs, axis=-1, keepdims=True)
    centred = inputs - row_mean
    variance = jnp.mean(centred * centred, axis=-1, keepdims=True)
    inverse = lax.rsqrt(variance + EPSILON)
    standard = centred * inverse
    scaled = cotangent * gains
    return inverse * (
        scaled
        - jnp.mean(scaled, axis=-1, keepdims=True)
        - standard * jnp.mean(scaled * standard, axis=-1, keepdims=True)
    )


def attend_local(queries, key_block, value_block, bias_block, valid_keys, scaling):
    scores = (
        jnp.einsum("bqhd,bkhd->bhqk", queries, key_block, preferred_element_type=jnp.float32)
        * scaling
        + bias_block
    )
    scores = jnp.where(valid_keys[:, None, None, :], scores, -jnp.inf)
    row_max = jnp.max(scores, axis=-1, keepdims=True)
    exponent = jnp.exp(scores - row_max)
    weights = exponent / jnp.sum(exponent, axis=-1, keepdims=True)
    weights_low = weights.astype(jnp.bfloat16)
    attended = jnp.einsum(
        "bhqk,bkhd->bqhd", weights_low, value_block, preferred_element_type=jnp.float32
    )
    return (weights, weights_low, attended)


def attend_grads(
    weights, weights_low, queries, key_block, value_block, grad_out, row_delta, scaling
):
    weight_grad = jnp.einsum(
        "bqhd,bkhd->bhqk", grad_out, value_block, preferred_element_type=jnp.float32
    )
    dscore = weights * (weight_grad - row_delta[..., None])
    dscore_low = dscore.astype(jnp.bfloat16)
    dquery = (
        jnp.einsum("bhqk,bkhd->bqhd", dscore_low, key_block, preferred_element_type=jnp.float32)
        * scaling
    )
    key_grad = (
        jnp.einsum("bhqk,bqhd->bkhd", dscore_low, queries, preferred_element_type=jnp.float32)
        * scaling
    )
    dvalue = jnp.einsum(
        "bhqk,bqhd->bkhd", weights_low, grad_out, preferred_element_type=jnp.float32
    )
    return (dscore_low, dquery, key_grad, dvalue)


def body(
    single,
    atoms,
    gain_single,
    gain_atom,
    w_token,
    w_token_out,
    w_cond,
    w_atom,
    w_atom_out,
    pair_bias,
    atom_bias,
    used_blocks,
    used_count,
    atom_counts,
    key_offset,
    grad_token,
    grad_atom,
):
    device = lax.axis_index("seq")
    shards = lax.axis_size("seq")
    tok_rows = single.shape[0]
    blocks_here = tok_rows // BLK
    local_heads = w_token.shape[2] // DH
    features = local_heads * DH
    scaling = DH ** (-0.5)
    normed_low = norm_rows(single.astype(jnp.float32), gain_single).astype(jnp.bfloat16)
    projected = [
        jnp.dot(normed_low, w_token[which], preferred_element_type=jnp.float32)
        for which in range(4)
    ]
    queries = projected[0].astype(jnp.bfloat16)
    gate_act = jax.nn.sigmoid(projected[3])
    key_value = jnp.concatenate(
        [projected[1].astype(jnp.bfloat16), projected[2].astype(jnp.bfloat16)], axis=1
    )
    owner_dev = used_blocks // blocks_here
    relative = jnp.mod(owner_dev - device, shards)
    relative = jnp.where(relative > shards // 2, relative - shards, relative)
    pieces = [key_value for distance in range(-WIN, WIN + 1)]
    for distance in range(-WIN, WIN + 1):
        if distance != 0:
            pieces[distance + WIN] = shifted(key_value, "seq", -distance)
    window = jnp.stack(pieces)
    candidates = (2 * WIN + 1) * blocks_here
    window_flat = window.reshape(candidates, BLK * 2 * features)
    picked = (relative + WIN) * blocks_here + used_blocks % blocks_here
    selector_mask = picked[:, :, None] == jnp.arange(candidates, dtype=jnp.int32)[None, None, :]
    selector = selector_mask.astype(jnp.bfloat16)
    stashed = jnp.einsum(
        "bsc,cx->bsx", selector, window_flat, preferred_element_type=jnp.float32
    ).astype(jnp.bfloat16)
    stashed = stashed.reshape(blocks_here, S, BLK, 2 * features)
    key_blocks = stashed[..., :features].reshape(blocks_here, S * BLK, local_heads, DH)
    value_blocks = stashed[..., features:].reshape(blocks_here, S * BLK, local_heads, DH)
    query_blocks = queries.reshape(blocks_here, BLK, local_heads, DH)
    bias_blocks = (
        pair_bias.reshape(local_heads, blocks_here, BLK, S * BLK)
        .transpose(1, 0, 2, 3)
        .astype(jnp.float32)
    )
    valid_keys = jnp.repeat(
        jnp.arange(S, dtype=jnp.int32)[None, :] < used_count[:, None], BLK, axis=1
    )
    weights, weights_low, attended = attend_local(
        query_blocks, key_blocks, value_blocks, bias_blocks, valid_keys, scaling
    )
    attended = attended.reshape(tok_rows, features)
    token_part = jnp.dot(
        (attended * gate_act).astype(jnp.bfloat16), w_token_out, preferred_element_type=jnp.float32
    )
    grad_gated = jnp.dot(grad_token, w_token_out.T, preferred_element_type=jnp.float32)
    grad_attended = (grad_gated * gate_act).astype(jnp.bfloat16)
    grad_gate = (grad_gated * attended * gate_act * (1.0 - gate_act)).astype(jnp.bfloat16)
    row_delta = jnp.sum(
        (grad_attended.astype(jnp.float32) * attended).reshape(blocks_here, BLK, local_heads, DH),
        axis=-1,
    ).transpose(0, 2, 1)
    score_low, dquery, key_grad, dvalue = attend_grads(
        weights,
        weights_low,
        query_blocks,
        key_blocks,
        value_blocks,
        grad_attended.reshape(blocks_here, BLK, local_heads, DH),
        row_delta,
        scaling,
    )
    grad_pair = score_low.transpose(1, 0, 2, 3).reshape(local_heads, tok_rows, S * BLK)
    returned = jnp.concatenate(
        [
            key_grad.reshape(blocks_here, S, BLK, features),
            dvalue.reshape(blocks_here, S, BLK, features),
        ],
        axis=-1,
    )
    returned_flat = returned.reshape(blocks_here, S, BLK * 2 * features)
    outgoing = jnp.einsum(
        "bsc,bsx->cx", selector_mask.astype(jnp.float32), returned_flat, precision=HIGHEST
    )
    outgoing = outgoing.reshape(2 * WIN + 1, tok_rows, 2 * features)
    collected = outgoing[WIN]
    for distance in range(-WIN, WIN + 1):
        if distance != 0:
            collected = collected + shifted(
                outgoing[distance + WIN].astype(jnp.bfloat16), "seq", distance
            ).astype(jnp.float32)
    token_grads = [
        dquery.reshape(tok_rows, features).astype(jnp.bfloat16),
        collected[:, :features].astype(jnp.bfloat16),
        collected[:, features:].astype(jnp.bfloat16),
        grad_gate,
    ]
    w_atom_all, w_atom_out_all, atom_bias_all = (w_atom, w_atom_out, atom_bias)
    atom_rows = atoms.shape[0]
    heads_atom = w_atom_all.shape[2] // DA
    atom_feat = heads_atom * DA
    halo_rows = AK // 2
    windows_here = atom_rows // AQ
    group_span = AK // AQ + 1
    slab_rows = group_span * AQ
    atom_scaling = DA ** (-0.5)
    normed_atoms = norm_rows(atoms.astype(jnp.float32), gain_atom)
    counts = atom_counts[0]
    ends = jnp.cumsum(counts)
    atom_place = jnp.arange(atom_rows, dtype=jnp.int32)
    token_local = jnp.sum((ends[None, :] <= atom_place[:, None]).astype(jnp.int32), axis=1)
    token_pick = (token_local[:, None] == jnp.arange(tok_rows, dtype=jnp.int32)[None, :]).astype(
        jnp.float32
    )
    condition = jnp.dot(normed_low, w_cond, preferred_element_type=jnp.float32)
    atom_input = (normed_atoms + jnp.dot(token_pick, condition, precision=HIGHEST)).astype(
        jnp.bfloat16
    )
    atom_proj = [
        jnp.dot(atom_input, w_atom_all[which], preferred_element_type=jnp.float32)
        for which in range(4)
    ]
    atom_gate = jax.nn.sigmoid(atom_proj[3])
    atom_kv = jnp.concatenate(
        [atom_proj[1].astype(jnp.bfloat16), atom_proj[2].astype(jnp.bfloat16)], axis=1
    )
    extended = extended_2(atom_kv, (("seq", 0),), halo_rows)
    ext_groups = extended.reshape(windows_here + AK // AQ, AQ, 2 * atom_feat)
    slabs = jnp.concatenate(
        [ext_groups[step : step + windows_here] for step in range(group_span)], axis=1
    )
    shift_here = key_offset + halo_rows
    placer_mask = (
        jnp.arange(slab_rows, dtype=jnp.int32)[None, None, :]
        == jnp.arange(AK, dtype=jnp.int32)[None, :, None] + shift_here[:, None, None]
    )
    window_kv = jnp.einsum(
        "wrs,wsf->wrf", placer_mask.astype(jnp.bfloat16), slabs, preferred_element_type=jnp.float32
    ).astype(jnp.bfloat16)
    atom_keys = window_kv[..., :atom_feat].reshape(windows_here, AK, heads_atom, DA)
    atom_values = window_kv[..., atom_feat:].reshape(windows_here, AK, heads_atom, DA)
    atom_queries = atom_proj[0].astype(jnp.bfloat16).reshape(windows_here, AQ, heads_atom, DA)
    atom_bias_blocks = (
        atom_bias_all.reshape(heads_atom, windows_here, AQ, AK)
        .transpose(1, 0, 2, 3)
        .astype(jnp.float32)
    )
    all_valid = jnp.ones((windows_here, AK), dtype=bool)
    aweights, aweights_low, atom_attended = attend_local(
        atom_queries, atom_keys, atom_values, atom_bias_blocks, all_valid, atom_scaling
    )
    atom_attended = atom_attended.reshape(atom_rows, atom_feat)
    atom_part = jnp.dot(
        (atom_attended * atom_gate).astype(jnp.bfloat16),
        w_atom_out_all,
        preferred_element_type=jnp.float32,
    )
    agrad_gated = jnp.dot(grad_atom, w_atom_out_all.T, preferred_element_type=jnp.float32)
    agrad_attended = (agrad_gated * atom_gate).astype(jnp.bfloat16)
    agrad_gate = (agrad_gated * atom_attended * atom_gate * (1.0 - atom_gate)).astype(jnp.bfloat16)
    atom_delta = jnp.sum(
        (agrad_attended.astype(jnp.float32) * atom_attended).reshape(
            windows_here, AQ, heads_atom, DA
        ),
        axis=-1,
    ).transpose(0, 2, 1)
    ascore_low, aquery_grad, akey_grad, avalue_grad = attend_grads(
        aweights,
        aweights_low,
        atom_queries,
        atom_keys,
        atom_values,
        agrad_attended.reshape(windows_here, AQ, heads_atom, DA),
        atom_delta,
        atom_scaling,
    )
    grad_abias = ascore_low.transpose(1, 0, 2, 3).reshape(heads_atom, atom_rows, AK)
    spread_grads = jnp.concatenate(
        [
            akey_grad.reshape(windows_here, AK, atom_feat),
            avalue_grad.reshape(windows_here, AK, atom_feat),
        ],
        axis=-1,
    )
    slab_grads = jnp.einsum(
        "wrs,wrf->wsf", placer_mask.astype(jnp.float32), spread_grads, precision=HIGHEST
    )
    slab_grads = slab_grads.reshape(windows_here, group_span, AQ, 2 * atom_feat)
    ext_grad = jnp.pad(slab_grads[:, 0], ((0, group_span - 1), (0, 0), (0, 0)))
    for step in range(1, group_span):
        ext_grad = ext_grad + jnp.pad(
            slab_grads[:, step], ((step, group_span - 1 - step), (0, 0), (0, 0))
        )
    ext_grad = ext_grad.reshape(atom_rows + 2 * halo_rows, 2 * atom_feat)
    rims = jnp.concatenate([ext_grad[:halo_rows], ext_grad[atom_rows + halo_rows :]], axis=0)
    edges = extended_2(rims.astype(jnp.bfloat16), (("seq", 0),), halo_rows).astype(rims.dtype)
    own_grad = ext_grad[halo_rows : halo_rows + atom_rows]
    own_grad = jnp.concatenate(
        [
            own_grad[:halo_rows] + edges[:halo_rows],
            own_grad[halo_rows : atom_rows - halo_rows],
            own_grad[atom_rows - halo_rows :] + edges[3 * halo_rows :],
        ],
        axis=0,
    )
    atom_grads = [
        aquery_grad.reshape(atom_rows, atom_feat).astype(jnp.bfloat16),
        own_grad[:, :atom_feat].astype(jnp.bfloat16),
        own_grad[:, atom_feat:].astype(jnp.bfloat16),
        agrad_gate,
    ]
    agrad_input = jnp.dot(atom_grads[0], w_atom_all[0].T, preferred_element_type=jnp.float32)
    for which in range(1, 4):
        agrad_input = agrad_input + jnp.dot(
            atom_grads[which], w_atom_all[which].T, preferred_element_type=jnp.float32
        )
    atoms_part = norm_back(atoms.astype(jnp.float32), gain_atom, agrad_input)
    cond_grad = jnp.dot(token_pick.T, agrad_input, precision=HIGHEST)
    cond_term = jnp.dot(cond_grad, w_cond.astype(jnp.float32).T, precision=HIGHEST)
    grad_normed = cond_term
    for which in range(4):
        grad_normed = grad_normed + jnp.dot(
            token_grads[which], w_token[which].T, preferred_element_type=jnp.float32
        )
    single_part = norm_back(single.astype(jnp.float32), gain_single, grad_normed)
    token_total, atom_total, atoms_total = head_sum([token_part, atom_part, atoms_part], "head")
    single_total = head_sum_small(single_part, "head")
    return (
        token_total.astype(jnp.bfloat16),
        atom_total.astype(jnp.bfloat16),
        single_total.astype(jnp.bfloat16),
        atoms_total.astype(jnp.bfloat16),
        grad_pair,
        grad_abias,
    )


def solution(mesh):
    return jax.shard_map(
        body,
        mesh=mesh,
        in_specs=(
            P("seq", None),
            P("seq", None),
            P(),
            P(),
            P(None, None, "head"),
            P("head", None),
            P(),
            P(None, None, "head"),
            P("head", None),
            P("head", "seq", None),
            P("head", "seq", None),
            P("seq", None),
            P("seq"),
            P("seq", None),
            P("seq"),
            P("seq", None),
            P("seq", None),
        ),
        out_specs=(
            P("seq", None),
            P("seq", None),
            P("seq", None),
            P("seq", None),
            P("head", "seq", None),
            P("head", "seq", None),
        ),
        check_vma=False,
    )
```

```python
import jax
import jax.numpy as jnp
from jax import lax
from jax.sharding import PartitionSpec as P

DH = 24
DA = 32
BLK = 128
S = 4
WIN = 2
AQ = 32
AK = 128


EPSILON = 1e-05
ONE_HOT_PRECISION = lax.Precision.HIGH


def shifted(block, axis, distance):
    devices = range(lax.axis_size(axis))
    route = [((i - distance) % len(devices), i) for i in devices]
    return lax.ppermute(block, axis, route)


def extended_2(block, sides, width):
    for axis, dim in sides:
        count = lax.axis_size(axis)
        forward = [(i, i + 1) for i in range(count - 1)]
        forward.append((count - 1, 0))
        backward = [(target, source) for source, target in forward]
        low = lax.ppermute(
            lax.slice_in_dim(block, block.shape[dim] - width, None, axis=dim), axis, forward
        )
        high = lax.ppermute(lax.slice_in_dim(block, 0, width, axis=dim), axis, backward)
        block = jnp.concatenate([low, block, high], axis=dim)
    return block


def head_sum(parts, axis):
    count = lax.axis_size(axis)
    if count != 4:
        return [lax.psum(p.astype(jnp.bfloat16), axis) for p in parts]
    pieces = []
    for part in parts:
        for col in range(part.shape[1] // 128):
            pieces.append(part[:, col * 128 : (col + 1) * 128])
    buf = jnp.concatenate(pieces, axis=0)
    rows = buf.shape[0]
    place = lax.axis_index(axis)
    low_bit = place % 2
    high_bit = (place // 2) % 2
    pair_near = [(i, i ^ 1) for i in range(count)]
    pair_far = [(i, i ^ 2) for i in range(count)]
    halves = buf.reshape(2, rows // 2, 128)
    keep = jnp.where(low_bit == 0, halves[0], halves[1])
    give = jnp.where(low_bit == 0, halves[1], halves[0])
    got = lax.ppermute(give.astype(jnp.bfloat16), axis, pair_near)
    summed = (keep + got.astype(jnp.float32)).reshape(2, rows // 4, 128)
    keep = jnp.where(high_bit == 0, summed[0], summed[1])
    give = jnp.where(high_bit == 0, summed[1], summed[0])
    got = lax.ppermute(give.astype(jnp.bfloat16), axis, pair_far)
    own = (keep + got.astype(jnp.float32)).astype(jnp.bfloat16)
    got = lax.ppermute(own, axis, pair_far)
    half = jnp.where(
        high_bit == 0, jnp.concatenate([own, got], axis=0), jnp.concatenate([got, own], axis=0)
    )
    got = lax.ppermute(half, axis, pair_near)
    full = jnp.where(
        low_bit == 0, jnp.concatenate([half, got], axis=0), jnp.concatenate([got, half], axis=0)
    )
    outs = []
    start = 0
    for part in parts:
        width = part.shape[1] // 128
        rows_here = part.shape[0]
        cols = [full[start + k * rows_here : start + (k + 1) * rows_here] for k in range(width)]
        start += width * rows_here
        outs.append(jnp.concatenate(cols, axis=1) if width > 1 else cols[0])
    return outs


def norm_rows(inputs, gains):
    row_mean = jnp.mean(inputs, axis=-1, keepdims=True)
    centred = inputs - row_mean
    variance = jnp.mean(centred * centred, axis=-1, keepdims=True)
    return centred * lax.rsqrt(variance + EPSILON) * gains


def norm_back(inputs, gains, cotangent):
    row_mean = jnp.mean(inputs, axis=-1, keepdims=True)
    centred = inputs - row_mean
    variance = jnp.mean(centred * centred, axis=-1, keepdims=True)
    inverse = lax.rsqrt(variance + EPSILON)
    standard = centred * inverse
    scaled = cotangent * gains
    return inverse * (
        scaled
        - jnp.mean(scaled, axis=-1, keepdims=True)
        - standard * jnp.mean(scaled * standard, axis=-1, keepdims=True)
    )


def attend_local(queries, key_block, value_block, bias_block, valid_keys, scaling):
    scores = (
        jnp.einsum("bqhd,bkhd->bhqk", queries, key_block, preferred_element_type=jnp.float32)
        * scaling
        + bias_block
    )
    scores = jnp.where(valid_keys[:, None, None, :], scores, -jnp.inf)
    row_max = jnp.max(scores, axis=-1, keepdims=True)
    exponent = jnp.exp(scores - row_max)
    weights = exponent / jnp.sum(exponent, axis=-1, keepdims=True)
    weights_low = weights.astype(jnp.bfloat16)
    attended = jnp.einsum(
        "bhqk,bkhd->bqhd", weights_low, value_block, preferred_element_type=jnp.float32
    )
    return (weights, weights_low, attended)


def attend_grads(
    weights, weights_low, queries, key_block, value_block, grad_out, row_delta, scaling
):
    weight_grad = jnp.einsum(
        "bqhd,bkhd->bhqk", grad_out, value_block, preferred_element_type=jnp.float32
    )
    dscore = weights * (weight_grad - row_delta[..., None])
    dscore_low = dscore.astype(jnp.bfloat16)
    dquery = (
        jnp.einsum("bhqk,bkhd->bqhd", dscore_low, key_block, preferred_element_type=jnp.float32)
        * scaling
    )
    key_grad = (
        jnp.einsum("bhqk,bqhd->bkhd", dscore_low, queries, preferred_element_type=jnp.float32)
        * scaling
    )
    dvalue = jnp.einsum(
        "bhqk,bqhd->bkhd", weights_low, grad_out, preferred_element_type=jnp.float32
    )
    return (dscore_low, dquery, key_grad, dvalue)


def body(
    single,
    atoms,
    gain_single,
    gain_atom,
    w_token,
    w_token_out,
    w_cond,
    w_atom,
    w_atom_out,
    pair_bias,
    atom_bias,
    used_blocks,
    used_count,
    atom_counts,
    key_offset,
    grad_token,
    grad_atom,
):
    device = lax.axis_index("seq")
    shards = lax.axis_size("seq")
    tok_rows = single.shape[0]
    blocks_here = tok_rows // BLK
    local_heads = w_token.shape[2] // DH
    features = local_heads * DH
    scaling = DH ** (-0.5)
    normed_low = norm_rows(single.astype(jnp.float32), gain_single).astype(jnp.bfloat16)
    projected = [
        jnp.dot(normed_low, w_token[which], preferred_element_type=jnp.float32)
        for which in range(4)
    ]
    queries = projected[0].astype(jnp.bfloat16)
    gate_act = jax.nn.sigmoid(projected[3])
    key_value = jnp.concatenate(
        [projected[1].astype(jnp.bfloat16), projected[2].astype(jnp.bfloat16)], axis=1
    )
    owner_dev = used_blocks // blocks_here
    relative = jnp.mod(owner_dev - device, shards)
    relative = jnp.where(relative > shards // 2, relative - shards, relative)
    pieces = [key_value for distance in range(-WIN, WIN + 1)]
    for distance in range(-WIN, WIN + 1):
        if distance != 0:
            pieces[distance + WIN] = shifted(key_value, "seq", -distance)
    window = jnp.stack(pieces)
    candidates = (2 * WIN + 1) * blocks_here
    window_flat = window.reshape(candidates, BLK * 2 * features)
    picked = (relative + WIN) * blocks_here + used_blocks % blocks_here
    selector_mask = picked[:, :, None] == jnp.arange(candidates, dtype=jnp.int32)[None, None, :]
    selector = selector_mask.astype(jnp.bfloat16)
    stashed = jnp.einsum(
        "bsc,cx->bsx", selector, window_flat, preferred_element_type=jnp.float32
    ).astype(jnp.bfloat16)
    stashed = stashed.reshape(blocks_here, S, BLK, 2 * features)
    key_blocks = stashed[..., :features].reshape(blocks_here, S * BLK, local_heads, DH)
    value_blocks = stashed[..., features:].reshape(blocks_here, S * BLK, local_heads, DH)
    query_blocks = queries.reshape(blocks_here, BLK, local_heads, DH)
    bias_blocks = (
        pair_bias.reshape(local_heads, blocks_here, BLK, S * BLK)
        .transpose(1, 0, 2, 3)
        .astype(jnp.float32)
    )
    valid_keys = jnp.repeat(
        jnp.arange(S, dtype=jnp.int32)[None, :] < used_count[:, None], BLK, axis=1
    )
    weights, weights_low, attended = attend_local(
        query_blocks, key_blocks, value_blocks, bias_blocks, valid_keys, scaling
    )
    attended = attended.reshape(tok_rows, features)
    token_part = jnp.dot(
        (attended * gate_act).astype(jnp.bfloat16), w_token_out, preferred_element_type=jnp.float32
    )
    grad_gated = jnp.dot(grad_token, w_token_out.T, preferred_element_type=jnp.float32)
    grad_attended = (grad_gated * gate_act).astype(jnp.bfloat16)
    grad_gate = (grad_gated * attended * gate_act * (1.0 - gate_act)).astype(jnp.bfloat16)
    row_delta = jnp.sum(
        (grad_attended.astype(jnp.float32) * attended).reshape(blocks_here, BLK, local_heads, DH),
        axis=-1,
    ).transpose(0, 2, 1)
    score_low, dquery, key_grad, dvalue = attend_grads(
        weights,
        weights_low,
        query_blocks,
        key_blocks,
        value_blocks,
        grad_attended.reshape(blocks_here, BLK, local_heads, DH),
        row_delta,
        scaling,
    )
    grad_pair = score_low.transpose(1, 0, 2, 3).reshape(local_heads, tok_rows, S * BLK)
    returned = jnp.concatenate(
        [
            key_grad.reshape(blocks_here, S, BLK, features),
            dvalue.reshape(blocks_here, S, BLK, features),
        ],
        axis=-1,
    )
    returned_flat = returned.reshape(blocks_here, S, BLK * 2 * features)
    outgoing = jnp.einsum(
        "bsc,bsx->cx", selector_mask.astype(jnp.float32), returned_flat, precision=ONE_HOT_PRECISION
    )
    outgoing = outgoing.reshape(2 * WIN + 1, tok_rows, 2 * features)
    collected = outgoing[WIN]
    for distance in range(-WIN, WIN + 1):
        if distance != 0:
            collected = collected + shifted(
                outgoing[distance + WIN].astype(jnp.bfloat16), "seq", distance
            ).astype(jnp.float32)
    token_grads = [
        dquery.reshape(tok_rows, features).astype(jnp.bfloat16),
        collected[:, :features].astype(jnp.bfloat16),
        collected[:, features:].astype(jnp.bfloat16),
        grad_gate,
    ]
    w_atom_all, w_atom_out_all, atom_bias_all = (w_atom, w_atom_out, atom_bias)
    atom_rows = atoms.shape[0]
    heads_atom = w_atom_all.shape[2] // DA
    atom_feat = heads_atom * DA
    halo_rows = AK // 2
    windows_here = atom_rows // AQ
    group_span = AK // AQ + 1
    slab_rows = group_span * AQ
    atom_scaling = DA ** (-0.5)
    normed_atoms = norm_rows(atoms.astype(jnp.float32), gain_atom)
    counts = atom_counts[0]
    ends = jnp.cumsum(counts)
    atom_place = jnp.arange(atom_rows, dtype=jnp.int32)
    token_local = jnp.sum((ends[None, :] <= atom_place[:, None]).astype(jnp.int32), axis=1)
    token_pick = (token_local[:, None] == jnp.arange(tok_rows, dtype=jnp.int32)[None, :]).astype(
        jnp.float32
    )
    condition = jnp.dot(normed_low, w_cond, preferred_element_type=jnp.float32)
    atom_input = (normed_atoms + jnp.dot(token_pick, condition, precision=ONE_HOT_PRECISION)).astype(
        jnp.bfloat16
    )
    atom_proj = [
        jnp.dot(atom_input, w_atom_all[which], preferred_element_type=jnp.float32)
        for which in range(4)
    ]
    atom_gate = jax.nn.sigmoid(atom_proj[3])
    atom_kv = jnp.concatenate(
        [atom_proj[1].astype(jnp.bfloat16), atom_proj[2].astype(jnp.bfloat16)], axis=1
    )
    extended = extended_2(atom_kv, (("seq", 0),), halo_rows)
    ext_groups = extended.reshape(windows_here + AK // AQ, AQ, 2 * atom_feat)
    slabs = jnp.concatenate(
        [ext_groups[step : step + windows_here] for step in range(group_span)], axis=1
    )
    shift_here = key_offset + halo_rows
    placer_mask = (
        jnp.arange(slab_rows, dtype=jnp.int32)[None, None, :]
        == jnp.arange(AK, dtype=jnp.int32)[None, :, None] + shift_here[:, None, None]
    )
    window_kv = jnp.einsum(
        "wrs,wsf->wrf", placer_mask.astype(jnp.bfloat16), slabs, preferred_element_type=jnp.float32
    ).astype(jnp.bfloat16)
    atom_keys = window_kv[..., :atom_feat].reshape(windows_here, AK, heads_atom, DA)
    atom_values = window_kv[..., atom_feat:].reshape(windows_here, AK, heads_atom, DA)
    atom_queries = atom_proj[0].astype(jnp.bfloat16).reshape(windows_here, AQ, heads_atom, DA)
    atom_bias_blocks = (
        atom_bias_all.reshape(heads_atom, windows_here, AQ, AK)
        .transpose(1, 0, 2, 3)
        .astype(jnp.float32)
    )
    all_valid = jnp.ones((windows_here, AK), dtype=bool)
    aweights, aweights_low, atom_attended = attend_local(
        atom_queries, atom_keys, atom_values, atom_bias_blocks, all_valid, atom_scaling
    )
    atom_attended = atom_attended.reshape(atom_rows, atom_feat)
    atom_part = jnp.dot(
        (atom_attended * atom_gate).astype(jnp.bfloat16),
        w_atom_out_all,
        preferred_element_type=jnp.float32,
    )
    agrad_gated = jnp.dot(grad_atom, w_atom_out_all.T, preferred_element_type=jnp.float32)
    agrad_attended = (agrad_gated * atom_gate).astype(jnp.bfloat16)
    agrad_gate = (agrad_gated * atom_attended * atom_gate * (1.0 - atom_gate)).astype(jnp.bfloat16)
    atom_delta = jnp.sum(
        (agrad_attended.astype(jnp.float32) * atom_attended).reshape(
            windows_here, AQ, heads_atom, DA
        ),
        axis=-1,
    ).transpose(0, 2, 1)
    ascore_low, aquery_grad, akey_grad, avalue_grad = attend_grads(
        aweights,
        aweights_low,
        atom_queries,
        atom_keys,
        atom_values,
        agrad_attended.reshape(windows_here, AQ, heads_atom, DA),
        atom_delta,
        atom_scaling,
    )
    grad_abias = ascore_low.transpose(1, 0, 2, 3).reshape(heads_atom, atom_rows, AK)
    spread_grads = jnp.concatenate(
        [
            akey_grad.reshape(windows_here, AK, atom_feat),
            avalue_grad.reshape(windows_here, AK, atom_feat),
        ],
        axis=-1,
    )
    slab_grads = jnp.einsum(
        "wrs,wrf->wsf", placer_mask.astype(jnp.float32), spread_grads, precision=ONE_HOT_PRECISION
    )
    slab_grads = slab_grads.reshape(windows_here, group_span, AQ, 2 * atom_feat)
    ext_grad = jnp.pad(slab_grads[:, 0], ((0, group_span - 1), (0, 0), (0, 0)))
    for step in range(1, group_span):
        ext_grad = ext_grad + jnp.pad(
            slab_grads[:, step], ((step, group_span - 1 - step), (0, 0), (0, 0))
        )
    ext_grad = ext_grad.reshape(atom_rows + 2 * halo_rows, 2 * atom_feat)
    rims = jnp.concatenate([ext_grad[:halo_rows], ext_grad[atom_rows + halo_rows :]], axis=0)
    edges = extended_2(rims.astype(jnp.bfloat16), (("seq", 0),), halo_rows).astype(rims.dtype)
    own_grad = ext_grad[halo_rows : halo_rows + atom_rows]
    own_grad = jnp.concatenate(
        [
            own_grad[:halo_rows] + edges[:halo_rows],
            own_grad[halo_rows : atom_rows - halo_rows],
            own_grad[atom_rows - halo_rows :] + edges[3 * halo_rows :],
        ],
        axis=0,
    )
    atom_grads = [
        aquery_grad.reshape(atom_rows, atom_feat).astype(jnp.bfloat16),
        own_grad[:, :atom_feat].astype(jnp.bfloat16),
        own_grad[:, atom_feat:].astype(jnp.bfloat16),
        agrad_gate,
    ]
    agrad_input = jnp.dot(atom_grads[0], w_atom_all[0].T, preferred_element_type=jnp.float32)
    for which in range(1, 4):
        agrad_input = agrad_input + jnp.dot(
            atom_grads[which], w_atom_all[which].T, preferred_element_type=jnp.float32
        )
    atoms_part = norm_back(atoms.astype(jnp.float32), gain_atom, agrad_input)
    cond_grad = jnp.dot(token_pick.T, agrad_input, precision=ONE_HOT_PRECISION)
    cond_term = jnp.dot(cond_grad, w_cond.astype(jnp.float32).T, precision=ONE_HOT_PRECISION)
    grad_normed = cond_term
    for which in range(4):
        grad_normed = grad_normed + jnp.dot(
            token_grads[which], w_token[which].T, preferred_element_type=jnp.float32
        )
    single_part = norm_back(single.astype(jnp.float32), gain_single, grad_normed)
    token_total, atom_total, single_total, atoms_total = head_sum(
        [token_part, atom_part, single_part, atoms_part], "head"
    )
    return (
        token_total.astype(jnp.bfloat16),
        atom_total.astype(jnp.bfloat16),
        single_total.astype(jnp.bfloat16),
        atoms_total.astype(jnp.bfloat16),
        grad_pair,
        grad_abias,
    )


def solution(mesh):
    return jax.shard_map(
        body,
        mesh=mesh,
        in_specs=(
            P("seq", None),
            P("seq", None),
            P(),
            P(),
            P(None, None, "head"),
            P("head", None),
            P(),
            P(None, None, "head"),
            P("head", None),
            P("head", "seq", None),
            P("head", "seq", None),
            P("seq", None),
            P("seq"),
            P("seq", None),
            P("seq"),
            P("seq", None),
            P("seq", None),
        ),
        out_specs=(
            P("seq", None),
            P("seq", None),
            P("seq", None),
            P("seq", None),
            P("head", "seq", None),
            P("head", "seq", None),
        ),
        check_vma=False,
    )
```

```python
import jax
import jax.numpy as jnp
from jax import lax
from jax.sharding import PartitionSpec as P

DH = 24
DA = 32
BLK = 128
S = 4
WIN = 2
AQ = 32
AK = 128


EPSILON = 1e-05
HIGHEST = lax.Precision.HIGHEST


def shifted(block, axis, distance):
    devices = range(lax.axis_size(axis))
    route = [((i - distance) % len(devices), i) for i in devices]
    return lax.ppermute(block, axis, route)


def extended_2(block, sides, width):
    for axis, dim in sides:
        count = lax.axis_size(axis)
        forward = [(i, i + 1) for i in range(count - 1)]
        forward.append((count - 1, 0))
        backward = [(target, source) for source, target in forward]
        low = lax.ppermute(
            lax.slice_in_dim(block, block.shape[dim] - width, None, axis=dim), axis, forward
        )
        high = lax.ppermute(lax.slice_in_dim(block, 0, width, axis=dim), axis, backward)
        block = jnp.concatenate([low, block, high], axis=dim)
    return block


def head_sum(parts, axis):
    count = lax.axis_size(axis)
    if count != 4:
        return [lax.psum(p.astype(jnp.bfloat16), axis) for p in parts]
    pieces = []
    for part in parts:
        for col in range(part.shape[1] // 128):
            pieces.append(part[:, col * 128 : (col + 1) * 128])
    buf = jnp.concatenate(pieces, axis=0)
    rows = buf.shape[0]
    place = lax.axis_index(axis)
    low_bit = place % 2
    high_bit = (place // 2) % 2
    pair_near = [(i, i ^ 1) for i in range(count)]
    pair_far = [(i, i ^ 2) for i in range(count)]
    halves = buf.reshape(2, rows // 2, 128)
    keep = jnp.where(low_bit == 0, halves[0], halves[1])
    give = jnp.where(low_bit == 0, halves[1], halves[0])
    got = lax.ppermute(give.astype(jnp.bfloat16), axis, pair_near)
    summed = (keep + got.astype(jnp.float32)).reshape(2, rows // 4, 128)
    keep = jnp.where(high_bit == 0, summed[0], summed[1])
    give = jnp.where(high_bit == 0, summed[1], summed[0])
    got = lax.ppermute(give.astype(jnp.bfloat16), axis, pair_far)
    own = (keep + got.astype(jnp.float32)).astype(jnp.bfloat16)
    got = lax.ppermute(own, axis, pair_far)
    half = jnp.where(
        high_bit == 0, jnp.concatenate([own, got], axis=0), jnp.concatenate([got, own], axis=0)
    )
    got = lax.ppermute(half, axis, pair_near)
    full = jnp.where(
        low_bit == 0, jnp.concatenate([half, got], axis=0), jnp.concatenate([got, half], axis=0)
    )
    outs = []
    start = 0
    for part in parts:
        width = part.shape[1] // 128
        rows_here = part.shape[0]
        cols = [full[start + k * rows_here : start + (k + 1) * rows_here] for k in range(width)]
        start += width * rows_here
        outs.append(jnp.concatenate(cols, axis=1) if width > 1 else cols[0])
    return outs


def norm_rows(inputs, gains):
    row_mean = jnp.mean(inputs, axis=-1, keepdims=True)
    centred = inputs - row_mean
    variance = jnp.mean(centred * centred, axis=-1, keepdims=True)
    return centred * lax.rsqrt(variance + EPSILON) * gains


def norm_back(inputs, gains, cotangent):
    row_mean = jnp.mean(inputs, axis=-1, keepdims=True)
    centred = inputs - row_mean
    variance = jnp.mean(centred * centred, axis=-1, keepdims=True)
    inverse = lax.rsqrt(variance + EPSILON)
    standard = centred * inverse
    scaled = cotangent * gains
    return inverse * (
        scaled
        - jnp.mean(scaled, axis=-1, keepdims=True)
        - standard * jnp.mean(scaled * standard, axis=-1, keepdims=True)
    )


def attend_local(queries, key_block, value_block, bias_block, valid_keys, scaling):
    scores = (
        jnp.einsum("bqhd,bkhd->bhqk", queries, key_block, preferred_element_type=jnp.float32)
        * scaling
        + bias_block
    )
    scores = jnp.where(valid_keys[:, None, None, :], scores, -jnp.inf)
    row_max = jnp.max(scores, axis=-1, keepdims=True)
    exponent = jnp.exp(scores - row_max)
    weights = exponent / jnp.sum(exponent, axis=-1, keepdims=True)
    weights_low = weights.astype(jnp.bfloat16)
    attended = jnp.einsum(
        "bhqk,bkhd->bqhd", weights_low, value_block, preferred_element_type=jnp.float32
    )
    return (weights, weights_low, attended)


def attend_grads(
    weights, weights_low, queries, key_block, value_block, grad_out, row_delta, scaling
):
    weight_grad = jnp.einsum(
        "bqhd,bkhd->bhqk", grad_out, value_block, preferred_element_type=jnp.float32
    )
    dscore = weights * (weight_grad - row_delta[..., None])
    dscore_low = dscore.astype(jnp.bfloat16)
    dquery = (
        jnp.einsum("bhqk,bkhd->bqhd", dscore_low, key_block, preferred_element_type=jnp.float32)
        * scaling
    )
    key_grad = (
        jnp.einsum("bhqk,bqhd->bkhd", dscore_low, queries, preferred_element_type=jnp.float32)
        * scaling
    )
    dvalue = jnp.einsum(
        "bhqk,bqhd->bkhd", weights_low, grad_out, preferred_element_type=jnp.float32
    )
    return (dscore_low, dquery, key_grad, dvalue)


def body(
    single,
    atoms,
    gain_single,
    gain_atom,
    w_token,
    w_token_out,
    w_cond,
    w_atom,
    w_atom_out,
    pair_bias,
    atom_bias,
    used_blocks,
    used_count,
    atom_counts,
    key_offset,
    grad_token,
    grad_atom,
):
    device = lax.axis_index("seq")
    shards = lax.axis_size("seq")
    tok_rows = single.shape[0]
    blocks_here = tok_rows // BLK
    local_heads = w_token.shape[2] // DH
    features = local_heads * DH
    scaling = DH ** (-0.5)
    normed_low = norm_rows(single.astype(jnp.float32), gain_single).astype(jnp.bfloat16)
    projected = [
        jnp.dot(normed_low, w_token[which], preferred_element_type=jnp.float32)
        for which in range(4)
    ]
    queries = projected[0].astype(jnp.bfloat16)
    gate_act = jax.nn.sigmoid(projected[3])
    key_value = jnp.concatenate(
        [projected[1].astype(jnp.bfloat16), projected[2].astype(jnp.bfloat16)], axis=1
    )
    w_atom_all, w_atom_out_all, atom_bias_all = (w_atom, w_atom_out, atom_bias)
    atom_rows = atoms.shape[0]
    heads_atom = w_atom_all.shape[2] // DA
    atom_feat = heads_atom * DA
    halo_rows = AK // 2
    windows_here = atom_rows // AQ
    group_span = AK // AQ + 1
    slab_rows = group_span * AQ
    atom_scaling = DA ** (-0.5)
    normed_atoms = norm_rows(atoms.astype(jnp.float32), gain_atom)
    counts = atom_counts[0]
    ends = jnp.cumsum(counts)
    atom_place = jnp.arange(atom_rows, dtype=jnp.int32)
    token_local = jnp.sum((ends[None, :] <= atom_place[:, None]).astype(jnp.int32), axis=1)
    token_pick = (token_local[:, None] == jnp.arange(tok_rows, dtype=jnp.int32)[None, :]).astype(
        jnp.float32
    )
    condition = jnp.dot(normed_low, w_cond, preferred_element_type=jnp.float32)
    atom_input = (normed_atoms + jnp.dot(token_pick, condition, precision=HIGHEST)).astype(
        jnp.bfloat16
    )
    atom_proj = [
        jnp.dot(atom_input, w_atom_all[which], preferred_element_type=jnp.float32)
        for which in range(4)
    ]
    atom_gate = jax.nn.sigmoid(atom_proj[3])
    atom_kv = jnp.concatenate(
        [atom_proj[1].astype(jnp.bfloat16), atom_proj[2].astype(jnp.bfloat16)], axis=1
    )
    extended = extended_2(atom_kv, (("seq", 0),), halo_rows)
    key_value, extended = lax.optimization_barrier((key_value, extended))
    owner_dev = used_blocks // blocks_here
    relative = jnp.mod(owner_dev - device, shards)
    relative = jnp.where(relative > shards // 2, relative - shards, relative)
    pieces = [key_value for distance in range(-WIN, WIN + 1)]
    for distance in range(-WIN, WIN + 1):
        if distance != 0:
            pieces[distance + WIN] = shifted(key_value, "seq", -distance)
    window = jnp.stack(pieces)
    candidates = (2 * WIN + 1) * blocks_here
    window_flat = window.reshape(candidates, BLK * 2 * features)
    picked = (relative + WIN) * blocks_here + used_blocks % blocks_here
    selector_mask = picked[:, :, None] == jnp.arange(candidates, dtype=jnp.int32)[None, None, :]
    selector = selector_mask.astype(jnp.bfloat16)
    stashed = jnp.einsum(
        "bsc,cx->bsx", selector, window_flat, preferred_element_type=jnp.float32
    ).astype(jnp.bfloat16)
    stashed = stashed.reshape(blocks_here, S, BLK, 2 * features)
    key_blocks = stashed[..., :features].reshape(blocks_here, S * BLK, local_heads, DH)
    value_blocks = stashed[..., features:].reshape(blocks_here, S * BLK, local_heads, DH)
    query_blocks = queries.reshape(blocks_here, BLK, local_heads, DH)
    bias_blocks = (
        pair_bias.reshape(local_heads, blocks_here, BLK, S * BLK)
        .transpose(1, 0, 2, 3)
        .astype(jnp.float32)
    )
    valid_keys = jnp.repeat(
        jnp.arange(S, dtype=jnp.int32)[None, :] < used_count[:, None], BLK, axis=1
    )
    weights, weights_low, attended = attend_local(
        query_blocks, key_blocks, value_blocks, bias_blocks, valid_keys, scaling
    )
    attended = attended.reshape(tok_rows, features)
    token_part = jnp.dot(
        (attended * gate_act).astype(jnp.bfloat16), w_token_out, preferred_element_type=jnp.float32
    )
    grad_gated = jnp.dot(grad_token, w_token_out.T, preferred_element_type=jnp.float32)
    grad_attended = (grad_gated * gate_act).astype(jnp.bfloat16)
    grad_gate = (grad_gated * attended * gate_act * (1.0 - gate_act)).astype(jnp.bfloat16)
    row_delta = jnp.sum(
        (grad_attended.astype(jnp.float32) * attended).reshape(blocks_here, BLK, local_heads, DH),
        axis=-1,
    ).transpose(0, 2, 1)
    score_low, dquery, key_grad, dvalue = attend_grads(
        weights,
        weights_low,
        query_blocks,
        key_blocks,
        value_blocks,
        grad_attended.reshape(blocks_here, BLK, local_heads, DH),
        row_delta,
        scaling,
    )
    grad_pair = score_low.transpose(1, 0, 2, 3).reshape(local_heads, tok_rows, S * BLK)
    returned = jnp.concatenate(
        [
            key_grad.reshape(blocks_here, S, BLK, features),
            dvalue.reshape(blocks_here, S, BLK, features),
        ],
        axis=-1,
    )
    returned_flat = returned.reshape(blocks_here, S, BLK * 2 * features)
    outgoing = jnp.einsum(
        "bsc,bsx->cx", selector_mask.astype(jnp.float32), returned_flat, precision=HIGHEST
    )
    outgoing = outgoing.reshape(2 * WIN + 1, tok_rows, 2 * features)
    collected = outgoing[WIN]
    for distance in range(-WIN, WIN + 1):
        if distance != 0:
            collected = collected + shifted(
                outgoing[distance + WIN].astype(jnp.bfloat16), "seq", distance
            ).astype(jnp.float32)
    token_grads = [
        dquery.reshape(tok_rows, features).astype(jnp.bfloat16),
        collected[:, :features].astype(jnp.bfloat16),
        collected[:, features:].astype(jnp.bfloat16),
        grad_gate,
    ]
    ext_groups = extended.reshape(windows_here + AK // AQ, AQ, 2 * atom_feat)
    slabs = jnp.concatenate(
        [ext_groups[step : step + windows_here] for step in range(group_span)], axis=1
    )
    shift_here = key_offset + halo_rows
    placer_mask = (
        jnp.arange(slab_rows, dtype=jnp.int32)[None, None, :]
        == jnp.arange(AK, dtype=jnp.int32)[None, :, None] + shift_here[:, None, None]
    )
    window_kv = jnp.einsum(
        "wrs,wsf->wrf", placer_mask.astype(jnp.bfloat16), slabs, preferred_element_type=jnp.float32
    ).astype(jnp.bfloat16)
    atom_keys = window_kv[..., :atom_feat].reshape(windows_here, AK, heads_atom, DA)
    atom_values = window_kv[..., atom_feat:].reshape(windows_here, AK, heads_atom, DA)
    atom_queries = atom_proj[0].astype(jnp.bfloat16).reshape(windows_here, AQ, heads_atom, DA)
    atom_bias_blocks = (
        atom_bias_all.reshape(heads_atom, windows_here, AQ, AK)
        .transpose(1, 0, 2, 3)
        .astype(jnp.float32)
    )
    all_valid = jnp.ones((windows_here, AK), dtype=bool)
    aweights, aweights_low, atom_attended = attend_local(
        atom_queries, atom_keys, atom_values, atom_bias_blocks, all_valid, atom_scaling
    )
    atom_attended = atom_attended.reshape(atom_rows, atom_feat)
    atom_part = jnp.dot(
        (atom_attended * atom_gate).astype(jnp.bfloat16),
        w_atom_out_all,
        preferred_element_type=jnp.float32,
    )
    agrad_gated = jnp.dot(grad_atom, w_atom_out_all.T, preferred_element_type=jnp.float32)
    agrad_attended = (agrad_gated * atom_gate).astype(jnp.bfloat16)
    agrad_gate = (agrad_gated * atom_attended * atom_gate * (1.0 - atom_gate)).astype(jnp.bfloat16)
    atom_delta = jnp.sum(
        (agrad_attended.astype(jnp.float32) * atom_attended).reshape(
            windows_here, AQ, heads_atom, DA
        ),
        axis=-1,
    ).transpose(0, 2, 1)
    ascore_low, aquery_grad, akey_grad, avalue_grad = attend_grads(
        aweights,
        aweights_low,
        atom_queries,
        atom_keys,
        atom_values,
        agrad_attended.reshape(windows_here, AQ, heads_atom, DA),
        atom_delta,
        atom_scaling,
    )
    grad_abias = ascore_low.transpose(1, 0, 2, 3).reshape(heads_atom, atom_rows, AK)
    spread_grads = jnp.concatenate(
        [
            akey_grad.reshape(windows_here, AK, atom_feat),
            avalue_grad.reshape(windows_here, AK, atom_feat),
        ],
        axis=-1,
    )
    slab_grads = jnp.einsum(
        "wrs,wrf->wsf", placer_mask.astype(jnp.float32), spread_grads, precision=HIGHEST
    )
    slab_grads = slab_grads.reshape(windows_here, group_span, AQ, 2 * atom_feat)
    ext_grad = jnp.pad(slab_grads[:, 0], ((0, group_span - 1), (0, 0), (0, 0)))
    for step in range(1, group_span):
        ext_grad = ext_grad + jnp.pad(
            slab_grads[:, step], ((step, group_span - 1 - step), (0, 0), (0, 0))
        )
    ext_grad = ext_grad.reshape(atom_rows + 2 * halo_rows, 2 * atom_feat)
    rims = jnp.concatenate([ext_grad[:halo_rows], ext_grad[atom_rows + halo_rows :]], axis=0)
    edges = extended_2(rims.astype(jnp.bfloat16), (("seq", 0),), halo_rows).astype(rims.dtype)
    own_grad = ext_grad[halo_rows : halo_rows + atom_rows]
    own_grad = jnp.concatenate(
        [
            own_grad[:halo_rows] + edges[:halo_rows],
            own_grad[halo_rows : atom_rows - halo_rows],
            own_grad[atom_rows - halo_rows :] + edges[3 * halo_rows :],
        ],
        axis=0,
    )
    atom_grads = [
        aquery_grad.reshape(atom_rows, atom_feat).astype(jnp.bfloat16),
        own_grad[:, :atom_feat].astype(jnp.bfloat16),
        own_grad[:, atom_feat:].astype(jnp.bfloat16),
        agrad_gate,
    ]
    agrad_input = jnp.dot(atom_grads[0], w_atom_all[0].T, preferred_element_type=jnp.float32)
    for which in range(1, 4):
        agrad_input = agrad_input + jnp.dot(
            atom_grads[which], w_atom_all[which].T, preferred_element_type=jnp.float32
        )
    atoms_part = norm_back(atoms.astype(jnp.float32), gain_atom, agrad_input)
    cond_grad = jnp.dot(token_pick.T, agrad_input, precision=HIGHEST)
    cond_term = jnp.dot(cond_grad, w_cond.astype(jnp.float32).T, precision=HIGHEST)
    grad_normed = cond_term
    for which in range(4):
        grad_normed = grad_normed + jnp.dot(
            token_grads[which], w_token[which].T, preferred_element_type=jnp.float32
        )
    single_part = norm_back(single.astype(jnp.float32), gain_single, grad_normed)
    token_total, atom_total, single_total, atoms_total = head_sum(
        [token_part, atom_part, single_part, atoms_part], "head"
    )
    return (
        token_total.astype(jnp.bfloat16),
        atom_total.astype(jnp.bfloat16),
        single_total.astype(jnp.bfloat16),
        atoms_total.astype(jnp.bfloat16),
        grad_pair,
        grad_abias,
    )


def solution(mesh):
    return jax.shard_map(
        body,
        mesh=mesh,
        in_specs=(
            P("seq", None),
            P("seq", None),
            P(),
            P(),
            P(None, None, "head"),
            P("head", None),
            P(),
            P(None, None, "head"),
            P("head", None),
            P("head", "seq", None),
            P("head", "seq", None),
            P("seq", None),
            P("seq"),
            P("seq", None),
            P("seq"),
            P("seq", None),
            P("seq", None),
        ),
        out_specs=(
            P("seq", None),
            P("seq", None),
            P("seq", None),
            P("seq", None),
            P("head", "seq", None),
            P("head", "seq", None),
        ),
        check_vma=False,
    )
```

```python
import jax
import jax.numpy as jnp
from jax import lax
from jax.sharding import PartitionSpec as P

DH = 24
DA = 32
BLK = 128
S = 4
WIN = 2
AQ = 32
AK = 128


EPSILON = 1e-05
HIGHEST = lax.Precision.HIGHEST


def shifted(block, axis, distance):
    devices = range(lax.axis_size(axis))
    route = [((i - distance) % len(devices), i) for i in devices]
    return lax.ppermute(block, axis, route)


def extended_2(block, sides, width):
    for axis, dim in sides:
        count = lax.axis_size(axis)
        forward = [(i, i + 1) for i in range(count - 1)]
        forward.append((count - 1, 0))
        backward = [(target, source) for source, target in forward]
        low = lax.ppermute(
            lax.slice_in_dim(block, block.shape[dim] - width, None, axis=dim), axis, forward
        )
        high = lax.ppermute(lax.slice_in_dim(block, 0, width, axis=dim), axis, backward)
        block = jnp.concatenate([low, block, high], axis=dim)
    return block


def head_sum(parts, axis):
    count = lax.axis_size(axis)
    if count != 4:
        return [lax.psum(p.astype(jnp.bfloat16), axis) for p in parts]
    pieces = []
    for part in parts:
        for col in range(part.shape[1] // 128):
            pieces.append(part[:, col * 128 : (col + 1) * 128])
    buf = jnp.concatenate(pieces, axis=0)
    rows = buf.shape[0]
    place = lax.axis_index(axis)
    low_bit = place % 2
    high_bit = (place // 2) % 2
    pair_near = [(i, i ^ 1) for i in range(count)]
    pair_far = [(i, i ^ 2) for i in range(count)]
    halves = buf.reshape(2, rows // 2, 128)
    keep = jnp.where(low_bit == 0, halves[0], halves[1])
    give = jnp.where(low_bit == 0, halves[1], halves[0])
    got = lax.ppermute(give.astype(jnp.bfloat16), axis, pair_near)
    summed = (keep + got.astype(jnp.float32)).reshape(2, rows // 4, 128)
    keep = jnp.where(high_bit == 0, summed[0], summed[1])
    give = jnp.where(high_bit == 0, summed[1], summed[0])
    got = lax.ppermute(give.astype(jnp.bfloat16), axis, pair_far)
    own = (keep + got.astype(jnp.float32)).astype(jnp.bfloat16)
    got = lax.ppermute(own, axis, pair_far)
    half = jnp.where(
        high_bit == 0, jnp.concatenate([own, got], axis=0), jnp.concatenate([got, own], axis=0)
    )
    got = lax.ppermute(half, axis, pair_near)
    full = jnp.where(
        low_bit == 0, jnp.concatenate([half, got], axis=0), jnp.concatenate([got, half], axis=0)
    )
    outs = []
    start = 0
    for part in parts:
        width = part.shape[1] // 128
        rows_here = part.shape[0]
        cols = [full[start + k * rows_here : start + (k + 1) * rows_here] for k in range(width)]
        start += width * rows_here
        outs.append(jnp.concatenate(cols, axis=1) if width > 1 else cols[0])
    return outs


def norm_rows(inputs, gains):
    row_mean = jnp.mean(inputs, axis=-1, keepdims=True)
    centred = inputs - row_mean
    variance = jnp.mean(centred * centred, axis=-1, keepdims=True)
    return centred * lax.rsqrt(variance + EPSILON) * gains


def norm_back(inputs, gains, cotangent):
    row_mean = jnp.mean(inputs, axis=-1, keepdims=True)
    centred = inputs - row_mean
    variance = jnp.mean(centred * centred, axis=-1, keepdims=True)
    inverse = lax.rsqrt(variance + EPSILON)
    standard = centred * inverse
    scaled = cotangent * gains
    return inverse * (
        scaled
        - jnp.mean(scaled, axis=-1, keepdims=True)
        - standard * jnp.mean(scaled * standard, axis=-1, keepdims=True)
    )


def attend_local(queries, key_block, value_block, bias_block, valid_keys, scaling):
    scores = (
        jnp.einsum("bqhd,bkhd->bhqk", queries, key_block, preferred_element_type=jnp.float32)
        * scaling
        + bias_block
    )
    scores = jnp.where(valid_keys[:, None, None, :], scores, -jnp.inf)
    row_max = jnp.max(scores, axis=-1, keepdims=True)
    exponent = jnp.exp(scores - row_max)
    weights = exponent / jnp.sum(exponent, axis=-1, keepdims=True)
    weights_low = weights.astype(jnp.bfloat16)
    attended = jnp.einsum(
        "bhqk,bkhd->bqhd", weights_low, value_block, preferred_element_type=jnp.float32
    )
    return (weights, weights_low, attended)


def attend_grads(
    weights, weights_low, queries, key_block, value_block, grad_out, row_delta, scaling
):
    weight_grad = jnp.einsum(
        "bqhd,bkhd->bhqk", grad_out, value_block, preferred_element_type=jnp.float32
    )
    dscore = weights * (weight_grad - row_delta[..., None])
    dscore_low = dscore.astype(jnp.bfloat16)
    dquery = (
        jnp.einsum("bhqk,bkhd->bqhd", dscore_low, key_block, preferred_element_type=jnp.float32)
        * scaling
    )
    key_grad = (
        jnp.einsum("bhqk,bqhd->bkhd", dscore_low, queries, preferred_element_type=jnp.float32)
        * scaling
    )
    dvalue = jnp.einsum(
        "bhqk,bqhd->bkhd", weights_low, grad_out, preferred_element_type=jnp.float32
    )
    return (dscore_low, dquery, key_grad, dvalue)


def body(
    single,
    atoms,
    gain_single,
    gain_atom,
    w_token,
    w_token_out,
    w_cond,
    w_atom,
    w_atom_out,
    pair_bias,
    atom_bias,
    used_blocks,
    used_count,
    atom_counts,
    key_offset,
    grad_token,
    grad_atom,
):
    device = lax.axis_index("seq")
    shards = lax.axis_size("seq")
    tok_rows = single.shape[0]
    blocks_here = tok_rows // BLK
    local_heads = w_token.shape[2] // DH
    features = local_heads * DH
    scaling = DH ** (-0.5)
    normed_low = norm_rows(single.astype(jnp.float32), gain_single).astype(jnp.bfloat16)
    projected = [
        jnp.dot(normed_low, w_token[which], preferred_element_type=jnp.float32)
        for which in range(4)
    ]
    queries = projected[0].astype(jnp.bfloat16)
    gate_act = jax.nn.sigmoid(projected[3])
    key_value = jnp.concatenate(
        [projected[1].astype(jnp.bfloat16), projected[2].astype(jnp.bfloat16)], axis=1
    )
    w_atom_all, w_atom_out_all, atom_bias_all = (w_atom, w_atom_out, atom_bias)
    atom_rows = atoms.shape[0]
    heads_atom = w_atom_all.shape[2] // DA
    atom_feat = heads_atom * DA
    halo_rows = AK // 2
    windows_here = atom_rows // AQ
    group_span = AK // AQ + 1
    slab_rows = group_span * AQ
    atom_scaling = DA ** (-0.5)
    normed_atoms = norm_rows(atoms.astype(jnp.float32), gain_atom)
    counts = atom_counts[0]
    ends = jnp.cumsum(counts)
    atom_place = jnp.arange(atom_rows, dtype=jnp.int32)
    token_local = jnp.sum((ends[None, :] <= atom_place[:, None]).astype(jnp.int32), axis=1)
    token_pick = (token_local[:, None] == jnp.arange(tok_rows, dtype=jnp.int32)[None, :]).astype(
        jnp.float32
    )
    condition = jnp.dot(normed_low, w_cond, preferred_element_type=jnp.float32)
    atom_input = (normed_atoms + jnp.dot(token_pick, condition, precision=HIGHEST)).astype(
        jnp.bfloat16
    )
    atom_proj = [
        jnp.dot(atom_input, w_atom_all[which], preferred_element_type=jnp.float32)
        for which in range(4)
    ]
    atom_gate = jax.nn.sigmoid(atom_proj[3])
    atom_kv = jnp.concatenate(
        [atom_proj[1].astype(jnp.bfloat16), atom_proj[2].astype(jnp.bfloat16)], axis=1
    )
    extended = extended_2(atom_kv, (("seq", 0),), halo_rows)
    key_value, extended = lax.optimization_barrier((key_value, extended))
    owner_dev = used_blocks // blocks_here
    relative = jnp.mod(owner_dev - device, shards)
    relative = jnp.where(relative > shards // 2, relative - shards, relative)
    pieces = [key_value for distance in range(-WIN, WIN + 1)]
    for distance in range(-WIN, WIN + 1):
        if distance != 0:
            pieces[distance + WIN] = shifted(key_value, "seq", -distance)
    window = jnp.stack(pieces)
    candidates = (2 * WIN + 1) * blocks_here
    window_flat = window.reshape(candidates, BLK * 2 * features)
    picked = (relative + WIN) * blocks_here + used_blocks % blocks_here
    selector_mask = picked[:, :, None] == jnp.arange(candidates, dtype=jnp.int32)[None, None, :]
    selector = selector_mask.astype(jnp.bfloat16)
    stashed = jnp.einsum(
        "bsc,cx->bsx", selector, window_flat, preferred_element_type=jnp.float32
    ).astype(jnp.bfloat16)
    stashed = stashed.reshape(blocks_here, S, BLK, 2 * features)
    key_blocks = stashed[..., :features].reshape(blocks_here, S * BLK, local_heads, DH)
    value_blocks = stashed[..., features:].reshape(blocks_here, S * BLK, local_heads, DH)
    query_blocks = queries.reshape(blocks_here, BLK, local_heads, DH)
    bias_blocks = (
        pair_bias.reshape(local_heads, blocks_here, BLK, S * BLK)
        .transpose(1, 0, 2, 3)
        .astype(jnp.float32)
    )
    valid_keys = jnp.repeat(
        jnp.arange(S, dtype=jnp.int32)[None, :] < used_count[:, None], BLK, axis=1
    )
    weights, weights_low, attended = attend_local(
        query_blocks, key_blocks, value_blocks, bias_blocks, valid_keys, scaling
    )
    attended = attended.reshape(tok_rows, features)
    token_part = jnp.dot(
        (attended * gate_act).astype(jnp.bfloat16), w_token_out, preferred_element_type=jnp.float32
    )
    grad_gated = jnp.dot(grad_token, w_token_out.T, preferred_element_type=jnp.float32)
    grad_attended = (grad_gated * gate_act).astype(jnp.bfloat16)
    grad_gate = (grad_gated * attended * gate_act * (1.0 - gate_act)).astype(jnp.bfloat16)
    row_delta = jnp.sum(
        (grad_attended.astype(jnp.float32) * attended).reshape(blocks_here, BLK, local_heads, DH),
        axis=-1,
    ).transpose(0, 2, 1)
    score_low, dquery, key_grad, dvalue = attend_grads(
        weights,
        weights_low,
        query_blocks,
        key_blocks,
        value_blocks,
        grad_attended.reshape(blocks_here, BLK, local_heads, DH),
        row_delta,
        scaling,
    )
    grad_pair = score_low.transpose(1, 0, 2, 3).reshape(local_heads, tok_rows, S * BLK)
    returned = jnp.concatenate(
        [
            key_grad.reshape(blocks_here, S, BLK, features),
            dvalue.reshape(blocks_here, S, BLK, features),
        ],
        axis=-1,
    )
    returned_flat = returned.reshape(blocks_here, S, BLK * 2 * features)
    outgoing = jnp.einsum(
        "bsc,bsx->cx", selector_mask.astype(jnp.float32), returned_flat, precision=HIGHEST
    )
    outgoing = outgoing.reshape(2 * WIN + 1, tok_rows, 2 * features)
    ext_groups = extended.reshape(windows_here + AK // AQ, AQ, 2 * atom_feat)
    slabs = jnp.concatenate(
        [ext_groups[step : step + windows_here] for step in range(group_span)], axis=1
    )
    shift_here = key_offset + halo_rows
    placer_mask = (
        jnp.arange(slab_rows, dtype=jnp.int32)[None, None, :]
        == jnp.arange(AK, dtype=jnp.int32)[None, :, None] + shift_here[:, None, None]
    )
    window_kv = jnp.einsum(
        "wrs,wsf->wrf", placer_mask.astype(jnp.bfloat16), slabs, preferred_element_type=jnp.float32
    ).astype(jnp.bfloat16)
    atom_keys = window_kv[..., :atom_feat].reshape(windows_here, AK, heads_atom, DA)
    atom_values = window_kv[..., atom_feat:].reshape(windows_here, AK, heads_atom, DA)
    atom_queries = atom_proj[0].astype(jnp.bfloat16).reshape(windows_here, AQ, heads_atom, DA)
    atom_bias_blocks = (
        atom_bias_all.reshape(heads_atom, windows_here, AQ, AK)
        .transpose(1, 0, 2, 3)
        .astype(jnp.float32)
    )
    all_valid = jnp.ones((windows_here, AK), dtype=bool)
    aweights, aweights_low, atom_attended = attend_local(
        atom_queries, atom_keys, atom_values, atom_bias_blocks, all_valid, atom_scaling
    )
    atom_attended = atom_attended.reshape(atom_rows, atom_feat)
    atom_part = jnp.dot(
        (atom_attended * atom_gate).astype(jnp.bfloat16),
        w_atom_out_all,
        preferred_element_type=jnp.float32,
    )
    agrad_gated = jnp.dot(grad_atom, w_atom_out_all.T, preferred_element_type=jnp.float32)
    agrad_attended = (agrad_gated * atom_gate).astype(jnp.bfloat16)
    agrad_gate = (agrad_gated * atom_attended * atom_gate * (1.0 - atom_gate)).astype(jnp.bfloat16)
    atom_delta = jnp.sum(
        (agrad_attended.astype(jnp.float32) * atom_attended).reshape(
            windows_here, AQ, heads_atom, DA
        ),
        axis=-1,
    ).transpose(0, 2, 1)
    ascore_low, aquery_grad, akey_grad, avalue_grad = attend_grads(
        aweights,
        aweights_low,
        atom_queries,
        atom_keys,
        atom_values,
        agrad_attended.reshape(windows_here, AQ, heads_atom, DA),
        atom_delta,
        atom_scaling,
    )
    grad_abias = ascore_low.transpose(1, 0, 2, 3).reshape(heads_atom, atom_rows, AK)
    spread_grads = jnp.concatenate(
        [
            akey_grad.reshape(windows_here, AK, atom_feat),
            avalue_grad.reshape(windows_here, AK, atom_feat),
        ],
        axis=-1,
    )
    slab_grads = jnp.einsum(
        "wrs,wrf->wsf", placer_mask.astype(jnp.float32), spread_grads, precision=HIGHEST
    )
    slab_grads = slab_grads.reshape(windows_here, group_span, AQ, 2 * atom_feat)
    ext_grad = jnp.pad(slab_grads[:, 0], ((0, group_span - 1), (0, 0), (0, 0)))
    for step in range(1, group_span):
        ext_grad = ext_grad + jnp.pad(
            slab_grads[:, step], ((step, group_span - 1 - step), (0, 0), (0, 0))
        )
    ext_grad = ext_grad.reshape(atom_rows + 2 * halo_rows, 2 * atom_feat)
    rims = jnp.concatenate([ext_grad[:halo_rows], ext_grad[atom_rows + halo_rows :]], axis=0)
    outgoing, rims = lax.optimization_barrier((outgoing, rims))
    edges = extended_2(rims.astype(jnp.bfloat16), (("seq", 0),), halo_rows).astype(rims.dtype)
    collected = outgoing[WIN]
    for distance in range(-WIN, WIN + 1):
        if distance != 0:
            collected = collected + shifted(
                outgoing[distance + WIN].astype(jnp.bfloat16), "seq", distance
            ).astype(jnp.float32)
    token_grads = [
        dquery.reshape(tok_rows, features).astype(jnp.bfloat16),
        collected[:, :features].astype(jnp.bfloat16),
        collected[:, features:].astype(jnp.bfloat16),
        grad_gate,
    ]
    own_grad = ext_grad[halo_rows : halo_rows + atom_rows]
    own_grad = jnp.concatenate(
        [
            own_grad[:halo_rows] + edges[:halo_rows],
            own_grad[halo_rows : atom_rows - halo_rows],
            own_grad[atom_rows - halo_rows :] + edges[3 * halo_rows :],
        ],
        axis=0,
    )
    atom_grads = [
        aquery_grad.reshape(atom_rows, atom_feat).astype(jnp.bfloat16),
        own_grad[:, :atom_feat].astype(jnp.bfloat16),
        own_grad[:, atom_feat:].astype(jnp.bfloat16),
        agrad_gate,
    ]
    agrad_input = jnp.dot(atom_grads[0], w_atom_all[0].T, preferred_element_type=jnp.float32)
    for which in range(1, 4):
        agrad_input = agrad_input + jnp.dot(
            atom_grads[which], w_atom_all[which].T, preferred_element_type=jnp.float32
        )
    atoms_part = norm_back(atoms.astype(jnp.float32), gain_atom, agrad_input)
    cond_grad = jnp.dot(token_pick.T, agrad_input, precision=HIGHEST)
    cond_term = jnp.dot(cond_grad, w_cond.astype(jnp.float32).T, precision=HIGHEST)
    grad_normed = cond_term
    for which in range(4):
        grad_normed = grad_normed + jnp.dot(
            token_grads[which], w_token[which].T, preferred_element_type=jnp.float32
        )
    single_part = norm_back(single.astype(jnp.float32), gain_single, grad_normed)
    token_total, atom_total, single_total, atoms_total = head_sum(
        [token_part, atom_part, single_part, atoms_part], "head"
    )
    return (
        token_total.astype(jnp.bfloat16),
        atom_total.astype(jnp.bfloat16),
        single_total.astype(jnp.bfloat16),
        atoms_total.astype(jnp.bfloat16),
        grad_pair,
        grad_abias,
    )


def solution(mesh):
    return jax.shard_map(
        body,
        mesh=mesh,
        in_specs=(
            P("seq", None),
            P("seq", None),
            P(),
            P(),
            P(None, None, "head"),
            P("head", None),
            P(),
            P(None, None, "head"),
            P("head", None),
            P("head", "seq", None),
            P("head", "seq", None),
            P("seq", None),
            P("seq"),
            P("seq", None),
            P("seq"),
            P("seq", None),
            P("seq", None),
        ),
        out_specs=(
            P("seq", None),
            P("seq", None),
            P("seq", None),
            P("seq", None),
            P("head", "seq", None),
            P("head", "seq", None),
        ),
        check_vma=False,
    )
```

```python
import jax
import jax.numpy as jnp
from jax import lax
from jax.sharding import PartitionSpec as P

DH = 24
DA = 32
BLK = 128
S = 4
WIN = 2
AQ = 32
AK = 128


EPSILON = 1e-05
HIGHEST = lax.Precision.HIGHEST


def shifted(block, axis, distance):
    devices = range(lax.axis_size(axis))
    route = [((i - distance) % len(devices), i) for i in devices]
    return lax.ppermute(block, axis, route)


def extended_2(block, sides, width):
    for axis, dim in sides:
        count = lax.axis_size(axis)
        forward = [(i, i + 1) for i in range(count - 1)]
        forward.append((count - 1, 0))
        backward = [(target, source) for source, target in forward]
        low = lax.ppermute(
            lax.slice_in_dim(block, block.shape[dim] - width, None, axis=dim), axis, forward
        )
        high = lax.ppermute(lax.slice_in_dim(block, 0, width, axis=dim), axis, backward)
        block = jnp.concatenate([low, block, high], axis=dim)
    return block


def head_sum(parts, axis):
    count = lax.axis_size(axis)
    if count != 4:
        return [lax.psum(p.astype(jnp.bfloat16), axis) for p in parts]
    pieces = []
    for part in parts:
        for col in range(part.shape[1] // 128):
            pieces.append(part[:, col * 128 : (col + 1) * 128])
    buf = jnp.concatenate(pieces, axis=0)
    rows = buf.shape[0]
    place = lax.axis_index(axis)
    low_bit = place % 2
    high_bit = (place // 2) % 2
    pair_near = [(i, i ^ 1) for i in range(count)]
    pair_far = [(i, i ^ 2) for i in range(count)]
    halves = buf.reshape(2, rows // 2, 128)
    keep = jnp.where(low_bit == 0, halves[0], halves[1])
    give = jnp.where(low_bit == 0, halves[1], halves[0])
    got = lax.ppermute(give.astype(jnp.bfloat16), axis, pair_near)
    summed = (keep + got.astype(jnp.float32)).reshape(2, rows // 4, 128)
    keep = jnp.where(high_bit == 0, summed[0], summed[1])
    give = jnp.where(high_bit == 0, summed[1], summed[0])
    got = lax.ppermute(give.astype(jnp.bfloat16), axis, pair_far)
    own = (keep + got.astype(jnp.float32)).astype(jnp.bfloat16)
    got = lax.ppermute(own, axis, pair_far)
    half = jnp.where(
        high_bit == 0, jnp.concatenate([own, got], axis=0), jnp.concatenate([got, own], axis=0)
    )
    got = lax.ppermute(half, axis, pair_near)
    full = jnp.where(
        low_bit == 0, jnp.concatenate([half, got], axis=0), jnp.concatenate([got, half], axis=0)
    )
    outs = []
    start = 0
    for part in parts:
        width = part.shape[1] // 128
        rows_here = part.shape[0]
        cols = [full[start + k * rows_here : start + (k + 1) * rows_here] for k in range(width)]
        start += width * rows_here
        outs.append(jnp.concatenate(cols, axis=1) if width > 1 else cols[0])
    return outs


def norm_rows(inputs, gains):
    row_mean = jnp.mean(inputs, axis=-1, keepdims=True)
    centred = inputs - row_mean
    variance = jnp.mean(centred * centred, axis=-1, keepdims=True)
    return centred * lax.rsqrt(variance + EPSILON) * gains


def norm_back(inputs, gains, cotangent):
    row_mean = jnp.mean(inputs, axis=-1, keepdims=True)
    centred = inputs - row_mean
    variance = jnp.mean(centred * centred, axis=-1, keepdims=True)
    inverse = lax.rsqrt(variance + EPSILON)
    standard = centred * inverse
    scaled = cotangent * gains
    return inverse * (
        scaled
        - jnp.mean(scaled, axis=-1, keepdims=True)
        - standard * jnp.mean(scaled * standard, axis=-1, keepdims=True)
    )


def attend_local(queries, key_block, value_block, bias_block, valid_keys, scaling):
    scores = (
        jnp.einsum("bqhd,bkhd->bhqk", queries, key_block, preferred_element_type=jnp.float32)
        * scaling
        + bias_block
    )
    scores = jnp.where(valid_keys[:, None, None, :], scores, -jnp.inf)
    row_max = jnp.max(scores, axis=-1, keepdims=True)
    exponent = jnp.exp(scores - row_max)
    weights = exponent / jnp.sum(exponent, axis=-1, keepdims=True)
    weights_low = weights.astype(jnp.bfloat16)
    attended = jnp.einsum(
        "bhqk,bkhd->bqhd", weights_low, value_block, preferred_element_type=jnp.float32
    )
    return (weights, weights_low, attended)


def attend_grads(
    weights, weights_low, queries, key_block, value_block, grad_out, row_delta, scaling
):
    weight_grad = jnp.einsum(
        "bqhd,bkhd->bhqk", grad_out, value_block, preferred_element_type=jnp.float32
    )
    dscore = weights * (weight_grad - row_delta[..., None])
    dscore_low = dscore.astype(jnp.bfloat16)
    dquery = (
        jnp.einsum("bhqk,bkhd->bqhd", dscore_low, key_block, preferred_element_type=jnp.float32)
        * scaling
    )
    key_grad = (
        jnp.einsum("bhqk,bqhd->bkhd", dscore_low, queries, preferred_element_type=jnp.float32)
        * scaling
    )
    dvalue = jnp.einsum(
        "bhqk,bqhd->bkhd", weights_low, grad_out, preferred_element_type=jnp.float32
    )
    return (dscore_low, dquery, key_grad, dvalue)


def body(
    single,
    atoms,
    gain_single,
    gain_atom,
    w_token,
    w_token_out,
    w_cond,
    w_atom,
    w_atom_out,
    pair_bias,
    atom_bias,
    used_blocks,
    used_count,
    atom_counts,
    key_offset,
    grad_token,
    grad_atom,
):
    device = lax.axis_index("seq")
    shards = lax.axis_size("seq")
    tok_rows = single.shape[0]
    blocks_here = tok_rows // BLK
    local_heads = w_token.shape[2] // DH
    features = local_heads * DH
    scaling = DH ** (-0.5)
    normed_low = norm_rows(single.astype(jnp.float32), gain_single).astype(jnp.bfloat16)
    projected = [
        jnp.dot(normed_low, w_token[which], preferred_element_type=jnp.float32)
        for which in range(4)
    ]
    queries = projected[0].astype(jnp.bfloat16)
    gate_act = jax.nn.sigmoid(projected[3])
    key_value = jnp.concatenate(
        [projected[1].astype(jnp.bfloat16), projected[2].astype(jnp.bfloat16)], axis=1
    )
    w_atom_all, w_atom_out_all, atom_bias_all = (w_atom, w_atom_out, atom_bias)
    atom_rows = atoms.shape[0]
    heads_atom = w_atom_all.shape[2] // DA
    atom_feat = heads_atom * DA
    halo_rows = AK // 2
    windows_here = atom_rows // AQ
    group_span = AK // AQ + 1
    slab_rows = group_span * AQ
    atom_scaling = DA ** (-0.5)
    normed_atoms = norm_rows(atoms.astype(jnp.float32), gain_atom)
    counts = atom_counts[0]
    ends = jnp.cumsum(counts)
    atom_place = jnp.arange(atom_rows, dtype=jnp.int32)
    token_local = jnp.sum((ends[None, :] <= atom_place[:, None]).astype(jnp.int32), axis=1)
    token_pick = (token_local[:, None] == jnp.arange(tok_rows, dtype=jnp.int32)[None, :]).astype(
        jnp.float32
    )
    condition = jnp.dot(normed_low, w_cond, preferred_element_type=jnp.float32)
    atom_input = (normed_atoms + jnp.dot(token_pick, condition, precision=HIGHEST)).astype(
        jnp.bfloat16
    )
    atom_proj = [
        jnp.dot(atom_input, w_atom_all[which], preferred_element_type=jnp.float32)
        for which in range(4)
    ]
    atom_gate = jax.nn.sigmoid(atom_proj[3])
    atom_kv = jnp.concatenate(
        [atom_proj[1].astype(jnp.bfloat16), atom_proj[2].astype(jnp.bfloat16)], axis=1
    )
    extended = extended_2(atom_kv, (("seq", 0),), halo_rows)
    key_value, extended = lax.optimization_barrier((key_value, extended))
    ext_groups = extended.reshape(windows_here + AK // AQ, AQ, 2 * atom_feat)
    slabs = jnp.concatenate(
        [ext_groups[step : step + windows_here] for step in range(group_span)], axis=1
    )
    shift_here = key_offset + halo_rows
    placer_mask = (
        jnp.arange(slab_rows, dtype=jnp.int32)[None, None, :]
        == jnp.arange(AK, dtype=jnp.int32)[None, :, None] + shift_here[:, None, None]
    )
    window_kv = jnp.einsum(
        "wrs,wsf->wrf", placer_mask.astype(jnp.bfloat16), slabs, preferred_element_type=jnp.float32
    ).astype(jnp.bfloat16)
    atom_keys = window_kv[..., :atom_feat].reshape(windows_here, AK, heads_atom, DA)
    atom_values = window_kv[..., atom_feat:].reshape(windows_here, AK, heads_atom, DA)
    atom_queries = atom_proj[0].astype(jnp.bfloat16).reshape(windows_here, AQ, heads_atom, DA)
    atom_bias_blocks = (
        atom_bias_all.reshape(heads_atom, windows_here, AQ, AK)
        .transpose(1, 0, 2, 3)
        .astype(jnp.float32)
    )
    all_valid = jnp.ones((windows_here, AK), dtype=bool)
    aweights, aweights_low, atom_attended = attend_local(
        atom_queries, atom_keys, atom_values, atom_bias_blocks, all_valid, atom_scaling
    )
    atom_attended = atom_attended.reshape(atom_rows, atom_feat)
    atom_part = jnp.dot(
        (atom_attended * atom_gate).astype(jnp.bfloat16),
        w_atom_out_all,
        preferred_element_type=jnp.float32,
    )
    agrad_gated = jnp.dot(grad_atom, w_atom_out_all.T, preferred_element_type=jnp.float32)
    agrad_attended = (agrad_gated * atom_gate).astype(jnp.bfloat16)
    agrad_gate = (agrad_gated * atom_attended * atom_gate * (1.0 - atom_gate)).astype(jnp.bfloat16)
    atom_delta = jnp.sum(
        (agrad_attended.astype(jnp.float32) * atom_attended).reshape(
            windows_here, AQ, heads_atom, DA
        ),
        axis=-1,
    ).transpose(0, 2, 1)
    ascore_low, aquery_grad, akey_grad, avalue_grad = attend_grads(
        aweights,
        aweights_low,
        atom_queries,
        atom_keys,
        atom_values,
        agrad_attended.reshape(windows_here, AQ, heads_atom, DA),
        atom_delta,
        atom_scaling,
    )
    grad_abias = ascore_low.transpose(1, 0, 2, 3).reshape(heads_atom, atom_rows, AK)
    spread_grads = jnp.concatenate(
        [
            akey_grad.reshape(windows_here, AK, atom_feat),
            avalue_grad.reshape(windows_here, AK, atom_feat),
        ],
        axis=-1,
    )
    slab_grads = jnp.einsum(
        "wrs,wrf->wsf", placer_mask.astype(jnp.float32), spread_grads, precision=HIGHEST
    )
    slab_grads = slab_grads.reshape(windows_here, group_span, AQ, 2 * atom_feat)
    ext_grad = jnp.pad(slab_grads[:, 0], ((0, group_span - 1), (0, 0), (0, 0)))
    for step in range(1, group_span):
        ext_grad = ext_grad + jnp.pad(
            slab_grads[:, step], ((step, group_span - 1 - step), (0, 0), (0, 0))
        )
    ext_grad = ext_grad.reshape(atom_rows + 2 * halo_rows, 2 * atom_feat)
    rims = jnp.concatenate([ext_grad[:halo_rows], ext_grad[atom_rows + halo_rows :]], axis=0)
    key_value, rims = lax.optimization_barrier((key_value, rims))
    owner_dev = used_blocks // blocks_here
    relative = jnp.mod(owner_dev - device, shards)
    relative = jnp.where(relative > shards // 2, relative - shards, relative)
    pieces = [key_value for distance in range(-WIN, WIN + 1)]
    for distance in range(-WIN, WIN + 1):
        if distance != 0:
            pieces[distance + WIN] = shifted(key_value, "seq", -distance)
    window = jnp.stack(pieces)
    candidates = (2 * WIN + 1) * blocks_here
    window_flat = window.reshape(candidates, BLK * 2 * features)
    picked = (relative + WIN) * blocks_here + used_blocks % blocks_here
    selector_mask = picked[:, :, None] == jnp.arange(candidates, dtype=jnp.int32)[None, None, :]
    selector = selector_mask.astype(jnp.bfloat16)
    stashed = jnp.einsum(
        "bsc,cx->bsx", selector, window_flat, preferred_element_type=jnp.float32
    ).astype(jnp.bfloat16)
    stashed = stashed.reshape(blocks_here, S, BLK, 2 * features)
    key_blocks = stashed[..., :features].reshape(blocks_here, S * BLK, local_heads, DH)
    value_blocks = stashed[..., features:].reshape(blocks_here, S * BLK, local_heads, DH)
    query_blocks = queries.reshape(blocks_here, BLK, local_heads, DH)
    bias_blocks = (
        pair_bias.reshape(local_heads, blocks_here, BLK, S * BLK)
        .transpose(1, 0, 2, 3)
        .astype(jnp.float32)
    )
    valid_keys = jnp.repeat(
        jnp.arange(S, dtype=jnp.int32)[None, :] < used_count[:, None], BLK, axis=1
    )
    weights, weights_low, attended = attend_local(
        query_blocks, key_blocks, value_blocks, bias_blocks, valid_keys, scaling
    )
    attended = attended.reshape(tok_rows, features)
    token_part = jnp.dot(
        (attended * gate_act).astype(jnp.bfloat16), w_token_out, preferred_element_type=jnp.float32
    )
    grad_gated = jnp.dot(grad_token, w_token_out.T, preferred_element_type=jnp.float32)
    grad_attended = (grad_gated * gate_act).astype(jnp.bfloat16)
    grad_gate = (grad_gated * attended * gate_act * (1.0 - gate_act)).astype(jnp.bfloat16)
    row_delta = jnp.sum(
        (grad_attended.astype(jnp.float32) * attended).reshape(blocks_here, BLK, local_heads, DH),
        axis=-1,
    ).transpose(0, 2, 1)
    score_low, dquery, key_grad, dvalue = attend_grads(
        weights,
        weights_low,
        query_blocks,
        key_blocks,
        value_blocks,
        grad_attended.reshape(blocks_here, BLK, local_heads, DH),
        row_delta,
        scaling,
    )
    grad_pair = score_low.transpose(1, 0, 2, 3).reshape(local_heads, tok_rows, S * BLK)
    returned = jnp.concatenate(
        [
            key_grad.reshape(blocks_here, S, BLK, features),
            dvalue.reshape(blocks_here, S, BLK, features),
        ],
        axis=-1,
    )
    returned_flat = returned.reshape(blocks_here, S, BLK * 2 * features)
    outgoing = jnp.einsum(
        "bsc,bsx->cx", selector_mask.astype(jnp.float32), returned_flat, precision=HIGHEST
    )
    outgoing = outgoing.reshape(2 * WIN + 1, tok_rows, 2 * features)
    collected = outgoing[WIN]
    for distance in range(-WIN, WIN + 1):
        if distance != 0:
            collected = collected + shifted(
                outgoing[distance + WIN].astype(jnp.bfloat16), "seq", distance
            ).astype(jnp.float32)
    token_grads = [
        dquery.reshape(tok_rows, features).astype(jnp.bfloat16),
        collected[:, :features].astype(jnp.bfloat16),
        collected[:, features:].astype(jnp.bfloat16),
        grad_gate,
    ]
    edges = extended_2(rims.astype(jnp.bfloat16), (("seq", 0),), halo_rows).astype(rims.dtype)
    own_grad = ext_grad[halo_rows : halo_rows + atom_rows]
    own_grad = jnp.concatenate(
        [
            own_grad[:halo_rows] + edges[:halo_rows],
            own_grad[halo_rows : atom_rows - halo_rows],
            own_grad[atom_rows - halo_rows :] + edges[3 * halo_rows :],
        ],
        axis=0,
    )
    atom_grads = [
        aquery_grad.reshape(atom_rows, atom_feat).astype(jnp.bfloat16),
        own_grad[:, :atom_feat].astype(jnp.bfloat16),
        own_grad[:, atom_feat:].astype(jnp.bfloat16),
        agrad_gate,
    ]
    agrad_input = jnp.dot(atom_grads[0], w_atom_all[0].T, preferred_element_type=jnp.float32)
    for which in range(1, 4):
        agrad_input = agrad_input + jnp.dot(
            atom_grads[which], w_atom_all[which].T, preferred_element_type=jnp.float32
        )
    atoms_part = norm_back(atoms.astype(jnp.float32), gain_atom, agrad_input)
    cond_grad = jnp.dot(token_pick.T, agrad_input, precision=HIGHEST)
    cond_term = jnp.dot(cond_grad, w_cond.astype(jnp.float32).T, precision=HIGHEST)
    grad_normed = cond_term
    for which in range(4):
        grad_normed = grad_normed + jnp.dot(
            token_grads[which], w_token[which].T, preferred_element_type=jnp.float32
        )
    single_part = norm_back(single.astype(jnp.float32), gain_single, grad_normed)
    token_total, atom_total, single_total, atoms_total = head_sum(
        [token_part, atom_part, single_part, atoms_part], "head"
    )
    return (
        token_total.astype(jnp.bfloat16),
        atom_total.astype(jnp.bfloat16),
        single_total.astype(jnp.bfloat16),
        atoms_total.astype(jnp.bfloat16),
        grad_pair,
        grad_abias,
    )


def solution(mesh):
    return jax.shard_map(
        body,
        mesh=mesh,
        in_specs=(
            P("seq", None),
            P("seq", None),
            P(),
            P(),
            P(None, None, "head"),
            P("head", None),
            P(),
            P(None, None, "head"),
            P("head", None),
            P("head", "seq", None),
            P("head", "seq", None),
            P("seq", None),
            P("seq"),
            P("seq", None),
            P("seq"),
            P("seq", None),
            P("seq", None),
        ),
        out_specs=(
            P("seq", None),
            P("seq", None),
            P("seq", None),
            P("seq", None),
            P("head", "seq", None),
            P("head", "seq", None),
        ),
        check_vma=False,
    )
```

```python
import jax
import jax.numpy as jnp
from jax import lax
from jax.sharding import PartitionSpec as P

DH = 24
DA = 32
BLK = 128
S = 4
WIN = 2
AQ = 32
AK = 128


EPSILON = 1e-05
ONE_HOT_PRECISION = lax.Precision.HIGH


def shifted(block, axis, distance):
    devices = range(lax.axis_size(axis))
    route = [((i - distance) % len(devices), i) for i in devices]
    return lax.ppermute(block, axis, route)


def extended_2(block, sides, width):
    for axis, dim in sides:
        count = lax.axis_size(axis)
        forward = [(i, i + 1) for i in range(count - 1)]
        forward.append((count - 1, 0))
        backward = [(target, source) for source, target in forward]
        low = lax.ppermute(
            lax.slice_in_dim(block, block.shape[dim] - width, None, axis=dim), axis, forward
        )
        high = lax.ppermute(lax.slice_in_dim(block, 0, width, axis=dim), axis, backward)
        block = jnp.concatenate([low, block, high], axis=dim)
    return block


def head_sum(parts, axis):
    count = lax.axis_size(axis)
    if count != 4:
        return [lax.psum(p.astype(jnp.bfloat16), axis) for p in parts]
    pieces = []
    for part in parts:
        for col in range(part.shape[1] // 128):
            pieces.append(part[:, col * 128 : (col + 1) * 128])
    buf = jnp.concatenate(pieces, axis=0)
    rows = buf.shape[0]
    place = lax.axis_index(axis)
    low_bit = place % 2
    high_bit = (place // 2) % 2
    pair_near = [(i, i ^ 1) for i in range(count)]
    pair_far = [(i, i ^ 2) for i in range(count)]
    halves = buf.reshape(2, rows // 2, 128)
    keep = jnp.where(low_bit == 0, halves[0], halves[1])
    give = jnp.where(low_bit == 0, halves[1], halves[0])
    got = lax.ppermute(give.astype(jnp.bfloat16), axis, pair_near)
    summed = (keep + got.astype(jnp.float32)).reshape(2, rows // 4, 128)
    keep = jnp.where(high_bit == 0, summed[0], summed[1])
    give = jnp.where(high_bit == 0, summed[1], summed[0])
    got = lax.ppermute(give.astype(jnp.bfloat16), axis, pair_far)
    own = (keep + got.astype(jnp.float32)).astype(jnp.bfloat16)
    got = lax.ppermute(own, axis, pair_far)
    half = jnp.where(
        high_bit == 0, jnp.concatenate([own, got], axis=0), jnp.concatenate([got, own], axis=0)
    )
    got = lax.ppermute(half, axis, pair_near)
    full = jnp.where(
        low_bit == 0, jnp.concatenate([half, got], axis=0), jnp.concatenate([got, half], axis=0)
    )
    outs = []
    start = 0
    for part in parts:
        width = part.shape[1] // 128
        rows_here = part.shape[0]
        cols = [full[start + k * rows_here : start + (k + 1) * rows_here] for k in range(width)]
        start += width * rows_here
        outs.append(jnp.concatenate(cols, axis=1) if width > 1 else cols[0])
    return outs


def norm_rows(inputs, gains):
    row_mean = jnp.mean(inputs, axis=-1, keepdims=True)
    centred = inputs - row_mean
    variance = jnp.mean(centred * centred, axis=-1, keepdims=True)
    return centred * lax.rsqrt(variance + EPSILON) * gains


def norm_back(inputs, gains, cotangent):
    row_mean = jnp.mean(inputs, axis=-1, keepdims=True)
    centred = inputs - row_mean
    variance = jnp.mean(centred * centred, axis=-1, keepdims=True)
    inverse = lax.rsqrt(variance + EPSILON)
    standard = centred * inverse
    scaled = cotangent * gains
    return inverse * (
        scaled
        - jnp.mean(scaled, axis=-1, keepdims=True)
        - standard * jnp.mean(scaled * standard, axis=-1, keepdims=True)
    )


def attend_local(queries, key_block, value_block, bias_block, valid_keys, scaling):
    scores = (
        jnp.einsum("bqhd,bkhd->bhqk", queries, key_block, preferred_element_type=jnp.float32)
        * scaling
        + bias_block
    )
    scores = jnp.where(valid_keys[:, None, None, :], scores, -jnp.inf)
    row_max = jnp.max(scores, axis=-1, keepdims=True)
    exponent = jnp.exp(scores - row_max)
    weights = exponent / jnp.sum(exponent, axis=-1, keepdims=True)
    weights_low = weights.astype(jnp.bfloat16)
    attended = jnp.einsum(
        "bhqk,bkhd->bqhd", weights_low, value_block, preferred_element_type=jnp.float32
    )
    return (weights, weights_low, attended)


def attend_grads(
    weights, weights_low, queries, key_block, value_block, grad_out, row_delta, scaling
):
    weight_grad = jnp.einsum(
        "bqhd,bkhd->bhqk", grad_out, value_block, preferred_element_type=jnp.float32
    )
    dscore = weights * (weight_grad - row_delta[..., None])
    dscore_low = dscore.astype(jnp.bfloat16)
    dquery = (
        jnp.einsum("bhqk,bkhd->bqhd", dscore_low, key_block, preferred_element_type=jnp.float32)
        * scaling
    )
    key_grad = (
        jnp.einsum("bhqk,bqhd->bkhd", dscore_low, queries, preferred_element_type=jnp.float32)
        * scaling
    )
    dvalue = jnp.einsum(
        "bhqk,bqhd->bkhd", weights_low, grad_out, preferred_element_type=jnp.float32
    )
    return (dscore_low, dquery, key_grad, dvalue)


def body(
    single,
    atoms,
    gain_single,
    gain_atom,
    w_token,
    w_token_out,
    w_cond,
    w_atom,
    w_atom_out,
    pair_bias,
    atom_bias,
    used_blocks,
    used_count,
    atom_counts,
    key_offset,
    grad_token,
    grad_atom,
):
    device = lax.axis_index("seq")
    shards = lax.axis_size("seq")
    tok_rows = single.shape[0]
    blocks_here = tok_rows // BLK
    local_heads = w_token.shape[2] // DH
    features = local_heads * DH
    scaling = DH ** (-0.5)
    normed_low = norm_rows(single.astype(jnp.float32), gain_single).astype(jnp.bfloat16)
    projected = [
        jnp.dot(normed_low, w_token[which], preferred_element_type=jnp.float32)
        for which in range(4)
    ]
    queries = projected[0].astype(jnp.bfloat16)
    gate_act = jax.nn.sigmoid(projected[3])
    key_value = jnp.concatenate(
        [projected[1].astype(jnp.bfloat16), projected[2].astype(jnp.bfloat16)], axis=1
    )
    w_atom_all, w_atom_out_all, atom_bias_all = (w_atom, w_atom_out, atom_bias)
    atom_rows = atoms.shape[0]
    heads_atom = w_atom_all.shape[2] // DA
    atom_feat = heads_atom * DA
    halo_rows = AK // 2
    windows_here = atom_rows // AQ
    group_span = AK // AQ + 1
    slab_rows = group_span * AQ
    atom_scaling = DA ** (-0.5)
    normed_atoms = norm_rows(atoms.astype(jnp.float32), gain_atom)
    counts = atom_counts[0]
    ends = jnp.cumsum(counts)
    atom_place = jnp.arange(atom_rows, dtype=jnp.int32)
    token_local = jnp.sum((ends[None, :] <= atom_place[:, None]).astype(jnp.int32), axis=1)
    token_pick = (token_local[:, None] == jnp.arange(tok_rows, dtype=jnp.int32)[None, :]).astype(
        jnp.float32
    )
    condition = jnp.dot(normed_low, w_cond, preferred_element_type=jnp.float32)
    atom_input = (normed_atoms + jnp.dot(token_pick, condition, precision=ONE_HOT_PRECISION)).astype(
        jnp.bfloat16
    )
    atom_proj = [
        jnp.dot(atom_input, w_atom_all[which], preferred_element_type=jnp.float32)
        for which in range(4)
    ]
    atom_gate = jax.nn.sigmoid(atom_proj[3])
    atom_kv = jnp.concatenate(
        [atom_proj[1].astype(jnp.bfloat16), atom_proj[2].astype(jnp.bfloat16)], axis=1
    )
    extended = extended_2(atom_kv, (("seq", 0),), halo_rows)
    key_value, extended = lax.optimization_barrier((key_value, extended))
    owner_dev = used_blocks // blocks_here
    relative = jnp.mod(owner_dev - device, shards)
    relative = jnp.where(relative > shards // 2, relative - shards, relative)
    pieces = [key_value for distance in range(-WIN, WIN + 1)]
    for distance in range(-WIN, WIN + 1):
        if distance != 0:
            pieces[distance + WIN] = shifted(key_value, "seq", -distance)
    window = jnp.stack(pieces)
    candidates = (2 * WIN + 1) * blocks_here
    window_flat = window.reshape(candidates, BLK * 2 * features)
    picked = (relative + WIN) * blocks_here + used_blocks % blocks_here
    selector_mask = picked[:, :, None] == jnp.arange(candidates, dtype=jnp.int32)[None, None, :]
    selector = selector_mask.astype(jnp.bfloat16)
    stashed = jnp.einsum(
        "bsc,cx->bsx", selector, window_flat, preferred_element_type=jnp.float32
    ).astype(jnp.bfloat16)
    stashed = stashed.reshape(blocks_here, S, BLK, 2 * features)
    key_blocks = stashed[..., :features].reshape(blocks_here, S * BLK, local_heads, DH)
    value_blocks = stashed[..., features:].reshape(blocks_here, S * BLK, local_heads, DH)
    query_blocks = queries.reshape(blocks_here, BLK, local_heads, DH)
    bias_blocks = (
        pair_bias.reshape(local_heads, blocks_here, BLK, S * BLK)
        .transpose(1, 0, 2, 3)
        .astype(jnp.float32)
    )
    valid_keys = jnp.repeat(
        jnp.arange(S, dtype=jnp.int32)[None, :] < used_count[:, None], BLK, axis=1
    )
    weights, weights_low, attended = attend_local(
        query_blocks, key_blocks, value_blocks, bias_blocks, valid_keys, scaling
    )
    attended = attended.reshape(tok_rows, features)
    token_part = jnp.dot(
        (attended * gate_act).astype(jnp.bfloat16), w_token_out, preferred_element_type=jnp.float32
    )
    grad_gated = jnp.dot(grad_token, w_token_out.T, preferred_element_type=jnp.float32)
    grad_attended = (grad_gated * gate_act).astype(jnp.bfloat16)
    grad_gate = (grad_gated * attended * gate_act * (1.0 - gate_act)).astype(jnp.bfloat16)
    row_delta = jnp.sum(
        (grad_attended.astype(jnp.float32) * attended).reshape(blocks_here, BLK, local_heads, DH),
        axis=-1,
    ).transpose(0, 2, 1)
    score_low, dquery, key_grad, dvalue = attend_grads(
        weights,
        weights_low,
        query_blocks,
        key_blocks,
        value_blocks,
        grad_attended.reshape(blocks_here, BLK, local_heads, DH),
        row_delta,
        scaling,
    )
    grad_pair = score_low.transpose(1, 0, 2, 3).reshape(local_heads, tok_rows, S * BLK)
    returned = jnp.concatenate(
        [
            key_grad.reshape(blocks_here, S, BLK, features),
            dvalue.reshape(blocks_here, S, BLK, features),
        ],
        axis=-1,
    )
    returned_flat = returned.reshape(blocks_here, S, BLK * 2 * features)
    outgoing = jnp.einsum(
        "bsc,bsx->cx", selector_mask.astype(jnp.float32), returned_flat, precision=ONE_HOT_PRECISION
    )
    outgoing = outgoing.reshape(2 * WIN + 1, tok_rows, 2 * features)
    collected = outgoing[WIN]
    for distance in range(-WIN, WIN + 1):
        if distance != 0:
            collected = collected + shifted(
                outgoing[distance + WIN].astype(jnp.bfloat16), "seq", distance
            ).astype(jnp.float32)
    token_grads = [
        dquery.reshape(tok_rows, features).astype(jnp.bfloat16),
        collected[:, :features].astype(jnp.bfloat16),
        collected[:, features:].astype(jnp.bfloat16),
        grad_gate,
    ]
    ext_groups = extended.reshape(windows_here + AK // AQ, AQ, 2 * atom_feat)
    slabs = jnp.concatenate(
        [ext_groups[step : step + windows_here] for step in range(group_span)], axis=1
    )
    shift_here = key_offset + halo_rows
    placer_mask = (
        jnp.arange(slab_rows, dtype=jnp.int32)[None, None, :]
        == jnp.arange(AK, dtype=jnp.int32)[None, :, None] + shift_here[:, None, None]
    )
    window_kv = jnp.einsum(
        "wrs,wsf->wrf", placer_mask.astype(jnp.bfloat16), slabs, preferred_element_type=jnp.float32
    ).astype(jnp.bfloat16)
    atom_keys = window_kv[..., :atom_feat].reshape(windows_here, AK, heads_atom, DA)
    atom_values = window_kv[..., atom_feat:].reshape(windows_here, AK, heads_atom, DA)
    atom_queries = atom_proj[0].astype(jnp.bfloat16).reshape(windows_here, AQ, heads_atom, DA)
    atom_bias_blocks = (
        atom_bias_all.reshape(heads_atom, windows_here, AQ, AK)
        .transpose(1, 0, 2, 3)
        .astype(jnp.float32)
    )
    all_valid = jnp.ones((windows_here, AK), dtype=bool)
    aweights, aweights_low, atom_attended = attend_local(
        atom_queries, atom_keys, atom_values, atom_bias_blocks, all_valid, atom_scaling
    )
    atom_attended = atom_attended.reshape(atom_rows, atom_feat)
    atom_part = jnp.dot(
        (atom_attended * atom_gate).astype(jnp.bfloat16),
        w_atom_out_all,
        preferred_element_type=jnp.float32,
    )
    agrad_gated = jnp.dot(grad_atom, w_atom_out_all.T, preferred_element_type=jnp.float32)
    agrad_attended = (agrad_gated * atom_gate).astype(jnp.bfloat16)
    agrad_gate = (agrad_gated * atom_attended * atom_gate * (1.0 - atom_gate)).astype(jnp.bfloat16)
    atom_delta = jnp.sum(
        (agrad_attended.astype(jnp.float32) * atom_attended).reshape(
            windows_here, AQ, heads_atom, DA
        ),
        axis=-1,
    ).transpose(0, 2, 1)
    ascore_low, aquery_grad, akey_grad, avalue_grad = attend_grads(
        aweights,
        aweights_low,
        atom_queries,
        atom_keys,
        atom_values,
        agrad_attended.reshape(windows_here, AQ, heads_atom, DA),
        atom_delta,
        atom_scaling,
    )
    grad_abias = ascore_low.transpose(1, 0, 2, 3).reshape(heads_atom, atom_rows, AK)
    spread_grads = jnp.concatenate(
        [
            akey_grad.reshape(windows_here, AK, atom_feat),
            avalue_grad.reshape(windows_here, AK, atom_feat),
        ],
        axis=-1,
    )
    slab_grads = jnp.einsum(
        "wrs,wrf->wsf", placer_mask.astype(jnp.float32), spread_grads, precision=ONE_HOT_PRECISION
    )
    slab_grads = slab_grads.reshape(windows_here, group_span, AQ, 2 * atom_feat)
    ext_grad = jnp.pad(slab_grads[:, 0], ((0, group_span - 1), (0, 0), (0, 0)))
    for step in range(1, group_span):
        ext_grad = ext_grad + jnp.pad(
            slab_grads[:, step], ((step, group_span - 1 - step), (0, 0), (0, 0))
        )
    ext_grad = ext_grad.reshape(atom_rows + 2 * halo_rows, 2 * atom_feat)
    rims = jnp.concatenate([ext_grad[:halo_rows], ext_grad[atom_rows + halo_rows :]], axis=0)
    edges = extended_2(rims.astype(jnp.bfloat16), (("seq", 0),), halo_rows).astype(rims.dtype)
    own_grad = ext_grad[halo_rows : halo_rows + atom_rows]
    own_grad = jnp.concatenate(
        [
            own_grad[:halo_rows] + edges[:halo_rows],
            own_grad[halo_rows : atom_rows - halo_rows],
            own_grad[atom_rows - halo_rows :] + edges[3 * halo_rows :],
        ],
        axis=0,
    )
    atom_grads = [
        aquery_grad.reshape(atom_rows, atom_feat).astype(jnp.bfloat16),
        own_grad[:, :atom_feat].astype(jnp.bfloat16),
        own_grad[:, atom_feat:].astype(jnp.bfloat16),
        agrad_gate,
    ]
    agrad_input = jnp.dot(atom_grads[0], w_atom_all[0].T, preferred_element_type=jnp.float32)
    for which in range(1, 4):
        agrad_input = agrad_input + jnp.dot(
            atom_grads[which], w_atom_all[which].T, preferred_element_type=jnp.float32
        )
    atoms_part = norm_back(atoms.astype(jnp.float32), gain_atom, agrad_input)
    cond_grad = jnp.dot(token_pick.T, agrad_input, precision=ONE_HOT_PRECISION)
    cond_term = jnp.dot(cond_grad, w_cond.astype(jnp.float32).T, precision=ONE_HOT_PRECISION)
    grad_normed = cond_term
    for which in range(4):
        grad_normed = grad_normed + jnp.dot(
            token_grads[which], w_token[which].T, preferred_element_type=jnp.float32
        )
    single_part = norm_back(single.astype(jnp.float32), gain_single, grad_normed)
    token_total, atom_total, single_total, atoms_total = head_sum(
        [token_part, atom_part, single_part, atoms_part], "head"
    )
    return (
        token_total.astype(jnp.bfloat16),
        atom_total.astype(jnp.bfloat16),
        single_total.astype(jnp.bfloat16),
        atoms_total.astype(jnp.bfloat16),
        grad_pair,
        grad_abias,
    )


def solution(mesh):
    return jax.shard_map(
        body,
        mesh=mesh,
        in_specs=(
            P("seq", None),
            P("seq", None),
            P(),
            P(),
            P(None, None, "head"),
            P("head", None),
            P(),
            P(None, None, "head"),
            P("head", None),
            P("head", "seq", None),
            P("head", "seq", None),
            P("seq", None),
            P("seq"),
            P("seq", None),
            P("seq"),
            P("seq", None),
            P("seq", None),
        ),
        out_specs=(
            P("seq", None),
            P("seq", None),
            P("seq", None),
            P("seq", None),
            P("head", "seq", None),
            P("head", "seq", None),
        ),
        check_vma=False,
    )
```

```python
import jax
import jax.numpy as jnp
from jax import lax
from jax.sharding import PartitionSpec as P

DH = 24
DA = 32
BLK = 128
S = 4
WIN = 2
AQ = 32
AK = 128


EPSILON = 1e-05
ONE_HOT_PRECISION = lax.Precision.HIGH


def shifted(block, axis, distance):
    devices = range(lax.axis_size(axis))
    route = [((i - distance) % len(devices), i) for i in devices]
    return lax.ppermute(block, axis, route)


def extended_2(block, sides, width):
    for axis, dim in sides:
        count = lax.axis_size(axis)
        forward = [(i, i + 1) for i in range(count - 1)]
        forward.append((count - 1, 0))
        backward = [(target, source) for source, target in forward]
        low = lax.ppermute(
            lax.slice_in_dim(block, block.shape[dim] - width, None, axis=dim), axis, forward
        )
        high = lax.ppermute(lax.slice_in_dim(block, 0, width, axis=dim), axis, backward)
        block = jnp.concatenate([low, block, high], axis=dim)
    return block


def head_sum(parts, axis):
    count = lax.axis_size(axis)
    if count != 4:
        return [lax.psum(p.astype(jnp.bfloat16), axis) for p in parts]
    pieces = []
    for part in parts:
        for col in range(part.shape[1] // 128):
            pieces.append(part[:, col * 128 : (col + 1) * 128])
    buf = jnp.concatenate(pieces, axis=0)
    rows = buf.shape[0]
    place = lax.axis_index(axis)
    low_bit = place % 2
    high_bit = (place // 2) % 2
    pair_near = [(i, i ^ 1) for i in range(count)]
    pair_far = [(i, i ^ 2) for i in range(count)]
    halves = buf.reshape(2, rows // 2, 128)
    keep = jnp.where(low_bit == 0, halves[0], halves[1])
    give = jnp.where(low_bit == 0, halves[1], halves[0])
    got = lax.ppermute(give.astype(jnp.bfloat16), axis, pair_near)
    summed = (keep + got.astype(jnp.float32)).reshape(2, rows // 4, 128)
    keep = jnp.where(high_bit == 0, summed[0], summed[1])
    give = jnp.where(high_bit == 0, summed[1], summed[0])
    got = lax.ppermute(give.astype(jnp.bfloat16), axis, pair_far)
    own = (keep + got.astype(jnp.float32)).astype(jnp.bfloat16)
    got = lax.ppermute(own, axis, pair_far)
    half = jnp.where(
        high_bit == 0, jnp.concatenate([own, got], axis=0), jnp.concatenate([got, own], axis=0)
    )
    got = lax.ppermute(half, axis, pair_near)
    full = jnp.where(
        low_bit == 0, jnp.concatenate([half, got], axis=0), jnp.concatenate([got, half], axis=0)
    )
    outs = []
    start = 0
    for part in parts:
        width = part.shape[1] // 128
        rows_here = part.shape[0]
        cols = [full[start + k * rows_here : start + (k + 1) * rows_here] for k in range(width)]
        start += width * rows_here
        outs.append(jnp.concatenate(cols, axis=1) if width > 1 else cols[0])
    return outs


def head_sum_small(part, axis):
    count = lax.axis_size(axis)
    low = part.astype(jnp.bfloat16)
    if count != 4:
        return lax.psum(low, axis)
    got = lax.ppermute(low, axis, [(i, i ^ 1) for i in range(count)])
    low = (low.astype(jnp.float32) + got.astype(jnp.float32)).astype(jnp.bfloat16)
    got = lax.ppermute(low, axis, [(i, i ^ 2) for i in range(count)])
    return low.astype(jnp.float32) + got.astype(jnp.float32)


def norm_rows(inputs, gains):
    row_mean = jnp.mean(inputs, axis=-1, keepdims=True)
    centred = inputs - row_mean
    variance = jnp.mean(centred * centred, axis=-1, keepdims=True)
    return centred * lax.rsqrt(variance + EPSILON) * gains


def norm_back(inputs, gains, cotangent):
    row_mean = jnp.mean(inputs, axis=-1, keepdims=True)
    centred = inputs - row_mean
    variance = jnp.mean(centred * centred, axis=-1, keepdims=True)
    inverse = lax.rsqrt(variance + EPSILON)
    standard = centred * inverse
    scaled = cotangent * gains
    return inverse * (
        scaled
        - jnp.mean(scaled, axis=-1, keepdims=True)
        - standard * jnp.mean(scaled * standard, axis=-1, keepdims=True)
    )


def attend_local(queries, key_block, value_block, bias_block, valid_keys, scaling):
    scores = (
        jnp.einsum("bqhd,bkhd->bhqk", queries, key_block, preferred_element_type=jnp.float32)
        * scaling
        + bias_block
    )
    scores = jnp.where(valid_keys[:, None, None, :], scores, -jnp.inf)
    row_max = jnp.max(scores, axis=-1, keepdims=True)
    exponent = jnp.exp(scores - row_max)
    weights = exponent / jnp.sum(exponent, axis=-1, keepdims=True)
    weights_low = weights.astype(jnp.bfloat16)
    attended = jnp.einsum(
        "bhqk,bkhd->bqhd", weights_low, value_block, preferred_element_type=jnp.float32
    )
    return (weights, weights_low, attended)


def attend_grads(
    weights, weights_low, queries, key_block, value_block, grad_out, row_delta, scaling
):
    weight_grad = jnp.einsum(
        "bqhd,bkhd->bhqk", grad_out, value_block, preferred_element_type=jnp.float32
    )
    dscore = weights * (weight_grad - row_delta[..., None])
    dscore_low = dscore.astype(jnp.bfloat16)
    dquery = (
        jnp.einsum("bhqk,bkhd->bqhd", dscore_low, key_block, preferred_element_type=jnp.float32)
        * scaling
    )
    key_grad = (
        jnp.einsum("bhqk,bqhd->bkhd", dscore_low, queries, preferred_element_type=jnp.float32)
        * scaling
    )
    dvalue = jnp.einsum(
        "bhqk,bqhd->bkhd", weights_low, grad_out, preferred_element_type=jnp.float32
    )
    return (dscore_low, dquery, key_grad, dvalue)


def body(
    single,
    atoms,
    gain_single,
    gain_atom,
    w_token,
    w_token_out,
    w_cond,
    w_atom,
    w_atom_out,
    pair_bias,
    atom_bias,
    used_blocks,
    used_count,
    atom_counts,
    key_offset,
    grad_token,
    grad_atom,
):
    device = lax.axis_index("seq")
    shards = lax.axis_size("seq")
    tok_rows = single.shape[0]
    blocks_here = tok_rows // BLK
    local_heads = w_token.shape[2] // DH
    features = local_heads * DH
    scaling = DH ** (-0.5)
    normed_low = norm_rows(single.astype(jnp.float32), gain_single).astype(jnp.bfloat16)
    projected = [
        jnp.dot(normed_low, w_token[which], preferred_element_type=jnp.float32)
        for which in range(4)
    ]
    queries = projected[0].astype(jnp.bfloat16)
    gate_act = jax.nn.sigmoid(projected[3])
    key_value = jnp.concatenate(
        [projected[1].astype(jnp.bfloat16), projected[2].astype(jnp.bfloat16)], axis=1
    )
    w_atom_all, w_atom_out_all, atom_bias_all = (w_atom, w_atom_out, atom_bias)
    atom_rows = atoms.shape[0]
    heads_atom = w_atom_all.shape[2] // DA
    atom_feat = heads_atom * DA
    halo_rows = AK // 2
    windows_here = atom_rows // AQ
    group_span = AK // AQ + 1
    slab_rows = group_span * AQ
    atom_scaling = DA ** (-0.5)
    normed_atoms = norm_rows(atoms.astype(jnp.float32), gain_atom)
    counts = atom_counts[0]
    ends = jnp.cumsum(counts)
    atom_place = jnp.arange(atom_rows, dtype=jnp.int32)
    token_local = jnp.sum((ends[None, :] <= atom_place[:, None]).astype(jnp.int32), axis=1)
    token_pick = (token_local[:, None] == jnp.arange(tok_rows, dtype=jnp.int32)[None, :]).astype(
        jnp.float32
    )
    condition = jnp.dot(normed_low, w_cond, preferred_element_type=jnp.float32)
    atom_input = (normed_atoms + jnp.dot(token_pick, condition, precision=ONE_HOT_PRECISION)).astype(
        jnp.bfloat16
    )
    atom_proj = [
        jnp.dot(atom_input, w_atom_all[which], preferred_element_type=jnp.float32)
        for which in range(4)
    ]
    atom_gate = jax.nn.sigmoid(atom_proj[3])
    atom_kv = jnp.concatenate(
        [atom_proj[1].astype(jnp.bfloat16), atom_proj[2].astype(jnp.bfloat16)], axis=1
    )
    extended = extended_2(atom_kv, (("seq", 0),), halo_rows)
    key_value, extended = lax.optimization_barrier((key_value, extended))
    owner_dev = used_blocks // blocks_here
    relative = jnp.mod(owner_dev - device, shards)
    relative = jnp.where(relative > shards // 2, relative - shards, relative)
    pieces = [key_value for distance in range(-WIN, WIN + 1)]
    for distance in range(-WIN, WIN + 1):
        if distance != 0:
            pieces[distance + WIN] = shifted(key_value, "seq", -distance)
    window = jnp.stack(pieces)
    candidates = (2 * WIN + 1) * blocks_here
    window_flat = window.reshape(candidates, BLK * 2 * features)
    picked = (relative + WIN) * blocks_here + used_blocks % blocks_here
    selector_mask = picked[:, :, None] == jnp.arange(candidates, dtype=jnp.int32)[None, None, :]
    selector = selector_mask.astype(jnp.bfloat16)
    stashed = jnp.einsum(
        "bsc,cx->bsx", selector, window_flat, preferred_element_type=jnp.float32
    ).astype(jnp.bfloat16)
    stashed = stashed.reshape(blocks_here, S, BLK, 2 * features)
    key_blocks = stashed[..., :features].reshape(blocks_here, S * BLK, local_heads, DH)
    value_blocks = stashed[..., features:].reshape(blocks_here, S * BLK, local_heads, DH)
    query_blocks = queries.reshape(blocks_here, BLK, local_heads, DH)
    bias_blocks = (
        pair_bias.reshape(local_heads, blocks_here, BLK, S * BLK)
        .transpose(1, 0, 2, 3)
        .astype(jnp.float32)
    )
    valid_keys = jnp.repeat(
        jnp.arange(S, dtype=jnp.int32)[None, :] < used_count[:, None], BLK, axis=1
    )
    weights, weights_low, attended = attend_local(
        query_blocks, key_blocks, value_blocks, bias_blocks, valid_keys, scaling
    )
    attended = attended.reshape(tok_rows, features)
    token_part = jnp.dot(
        (attended * gate_act).astype(jnp.bfloat16), w_token_out, preferred_element_type=jnp.float32
    )
    grad_gated = jnp.dot(grad_token, w_token_out.T, preferred_element_type=jnp.float32)
    grad_attended = (grad_gated * gate_act).astype(jnp.bfloat16)
    grad_gate = (grad_gated * attended * gate_act * (1.0 - gate_act)).astype(jnp.bfloat16)
    row_delta = jnp.sum(
        (grad_attended.astype(jnp.float32) * attended).reshape(blocks_here, BLK, local_heads, DH),
        axis=-1,
    ).transpose(0, 2, 1)
    score_low, dquery, key_grad, dvalue = attend_grads(
        weights,
        weights_low,
        query_blocks,
        key_blocks,
        value_blocks,
        grad_attended.reshape(blocks_here, BLK, local_heads, DH),
        row_delta,
        scaling,
    )
    grad_pair = score_low.transpose(1, 0, 2, 3).reshape(local_heads, tok_rows, S * BLK)
    returned = jnp.concatenate(
        [
            key_grad.reshape(blocks_here, S, BLK, features),
            dvalue.reshape(blocks_here, S, BLK, features),
        ],
        axis=-1,
    )
    returned_flat = returned.reshape(blocks_here, S, BLK * 2 * features)
    outgoing = jnp.einsum(
        "bsc,bsx->cx", selector_mask.astype(jnp.float32), returned_flat, precision=ONE_HOT_PRECISION
    )
    outgoing = outgoing.reshape(2 * WIN + 1, tok_rows, 2 * features)
    collected = outgoing[WIN]
    for distance in range(-WIN, WIN + 1):
        if distance != 0:
            collected = collected + shifted(
                outgoing[distance + WIN].astype(jnp.bfloat16), "seq", distance
            ).astype(jnp.float32)
    token_grads = [
        dquery.reshape(tok_rows, features).astype(jnp.bfloat16),
        collected[:, :features].astype(jnp.bfloat16),
        collected[:, features:].astype(jnp.bfloat16),
        grad_gate,
    ]
    ext_groups = extended.reshape(windows_here + AK // AQ, AQ, 2 * atom_feat)
    slabs = jnp.concatenate(
        [ext_groups[step : step + windows_here] for step in range(group_span)], axis=1
    )
    shift_here = key_offset + halo_rows
    placer_mask = (
        jnp.arange(slab_rows, dtype=jnp.int32)[None, None, :]
        == jnp.arange(AK, dtype=jnp.int32)[None, :, None] + shift_here[:, None, None]
    )
    window_kv = jnp.einsum(
        "wrs,wsf->wrf", placer_mask.astype(jnp.bfloat16), slabs, preferred_element_type=jnp.float32
    ).astype(jnp.bfloat16)
    atom_keys = window_kv[..., :atom_feat].reshape(windows_here, AK, heads_atom, DA)
    atom_values = window_kv[..., atom_feat:].reshape(windows_here, AK, heads_atom, DA)
    atom_queries = atom_proj[0].astype(jnp.bfloat16).reshape(windows_here, AQ, heads_atom, DA)
    atom_bias_blocks = (
        atom_bias_all.reshape(heads_atom, windows_here, AQ, AK)
        .transpose(1, 0, 2, 3)
        .astype(jnp.float32)
    )
    all_valid = jnp.ones((windows_here, AK), dtype=bool)
    aweights, aweights_low, atom_attended = attend_local(
        atom_queries, atom_keys, atom_values, atom_bias_blocks, all_valid, atom_scaling
    )
    atom_attended = atom_attended.reshape(atom_rows, atom_feat)
    atom_part = jnp.dot(
        (atom_attended * atom_gate).astype(jnp.bfloat16),
        w_atom_out_all,
        preferred_element_type=jnp.float32,
    )
    agrad_gated = jnp.dot(grad_atom, w_atom_out_all.T, preferred_element_type=jnp.float32)
    agrad_attended = (agrad_gated * atom_gate).astype(jnp.bfloat16)
    agrad_gate = (agrad_gated * atom_attended * atom_gate * (1.0 - atom_gate)).astype(jnp.bfloat16)
    atom_delta = jnp.sum(
        (agrad_attended.astype(jnp.float32) * atom_attended).reshape(
            windows_here, AQ, heads_atom, DA
        ),
        axis=-1,
    ).transpose(0, 2, 1)
    ascore_low, aquery_grad, akey_grad, avalue_grad = attend_grads(
        aweights,
        aweights_low,
        atom_queries,
        atom_keys,
        atom_values,
        agrad_attended.reshape(windows_here, AQ, heads_atom, DA),
        atom_delta,
        atom_scaling,
    )
    grad_abias = ascore_low.transpose(1, 0, 2, 3).reshape(heads_atom, atom_rows, AK)
    spread_grads = jnp.concatenate(
        [
            akey_grad.reshape(windows_here, AK, atom_feat),
            avalue_grad.reshape(windows_here, AK, atom_feat),
        ],
        axis=-1,
    )
    slab_grads = jnp.einsum(
        "wrs,wrf->wsf", placer_mask.astype(jnp.float32), spread_grads, precision=ONE_HOT_PRECISION
    )
    slab_grads = slab_grads.reshape(windows_here, group_span, AQ, 2 * atom_feat)
    ext_grad = jnp.pad(slab_grads[:, 0], ((0, group_span - 1), (0, 0), (0, 0)))
    for step in range(1, group_span):
        ext_grad = ext_grad + jnp.pad(
            slab_grads[:, step], ((step, group_span - 1 - step), (0, 0), (0, 0))
        )
    ext_grad = ext_grad.reshape(atom_rows + 2 * halo_rows, 2 * atom_feat)
    rims = jnp.concatenate([ext_grad[:halo_rows], ext_grad[atom_rows + halo_rows :]], axis=0)
    edges = extended_2(rims.astype(jnp.bfloat16), (("seq", 0),), halo_rows).astype(rims.dtype)
    own_grad = ext_grad[halo_rows : halo_rows + atom_rows]
    own_grad = jnp.concatenate(
        [
            own_grad[:halo_rows] + edges[:halo_rows],
            own_grad[halo_rows : atom_rows - halo_rows],
            own_grad[atom_rows - halo_rows :] + edges[3 * halo_rows :],
        ],
        axis=0,
    )
    atom_grads = [
        aquery_grad.reshape(atom_rows, atom_feat).astype(jnp.bfloat16),
        own_grad[:, :atom_feat].astype(jnp.bfloat16),
        own_grad[:, atom_feat:].astype(jnp.bfloat16),
        agrad_gate,
    ]
    agrad_input = jnp.dot(atom_grads[0], w_atom_all[0].T, preferred_element_type=jnp.float32)
    for which in range(1, 4):
        agrad_input = agrad_input + jnp.dot(
            atom_grads[which], w_atom_all[which].T, preferred_element_type=jnp.float32
        )
    atoms_part = norm_back(atoms.astype(jnp.float32), gain_atom, agrad_input)
    cond_grad = jnp.dot(token_pick.T, agrad_input, precision=ONE_HOT_PRECISION)
    cond_term = jnp.dot(cond_grad, w_cond.astype(jnp.float32).T, precision=ONE_HOT_PRECISION)
    grad_normed = cond_term
    for which in range(4):
        grad_normed = grad_normed + jnp.dot(
            token_grads[which], w_token[which].T, preferred_element_type=jnp.float32
        )
    single_part = norm_back(single.astype(jnp.float32), gain_single, grad_normed)
    token_total, atom_total, atoms_total = head_sum([token_part, atom_part, atoms_part], "head")
    single_total = head_sum_small(single_part, "head")
    return (
        token_total.astype(jnp.bfloat16),
        atom_total.astype(jnp.bfloat16),
        single_total.astype(jnp.bfloat16),
        atoms_total.astype(jnp.bfloat16),
        grad_pair,
        grad_abias,
    )


def solution(mesh):
    return jax.shard_map(
        body,
        mesh=mesh,
        in_specs=(
            P("seq", None),
            P("seq", None),
            P(),
            P(),
            P(None, None, "head"),
            P("head", None),
            P(),
            P(None, None, "head"),
            P("head", None),
            P("head", "seq", None),
            P("head", "seq", None),
            P("seq", None),
            P("seq"),
            P("seq", None),
            P("seq"),
            P("seq", None),
            P("seq", None),
        ),
        out_specs=(
            P("seq", None),
            P("seq", None),
            P("seq", None),
            P("seq", None),
            P("head", "seq", None),
            P("head", "seq", None),
        ),
        check_vma=False,
    )
```

```python
import jax
import jax.numpy as jnp
from jax import lax
from jax.sharding import PartitionSpec as P

DH = 24
DA = 32
BLK = 128
S = 4
WIN = 2
AQ = 32
AK = 128


EPSILON = 1e-05
ONE_HOT_PRECISION = lax.Precision.HIGH


def shifted(block, axis, distance):
    devices = range(lax.axis_size(axis))
    route = [((i - distance) % len(devices), i) for i in devices]
    return lax.ppermute(block, axis, route)


def extended_2(block, sides, width):
    for axis, dim in sides:
        count = lax.axis_size(axis)
        forward = [(i, i + 1) for i in range(count - 1)]
        forward.append((count - 1, 0))
        backward = [(target, source) for source, target in forward]
        low = lax.ppermute(
            lax.slice_in_dim(block, block.shape[dim] - width, None, axis=dim), axis, forward
        )
        high = lax.ppermute(lax.slice_in_dim(block, 0, width, axis=dim), axis, backward)
        block = jnp.concatenate([low, block, high], axis=dim)
    return block


def head_sum(parts, axis):
    count = lax.axis_size(axis)
    if count != 4:
        return [lax.psum(p.astype(jnp.bfloat16), axis) for p in parts]
    pieces = []
    for part in parts:
        for col in range(part.shape[1] // 128):
            pieces.append(part[:, col * 128 : (col + 1) * 128])
    buf = jnp.concatenate(pieces, axis=0)
    rows = buf.shape[0]
    place = lax.axis_index(axis)
    low_bit = place % 2
    high_bit = (place // 2) % 2
    pair_near = [(i, i ^ 1) for i in range(count)]
    pair_far = [(i, i ^ 2) for i in range(count)]
    halves = buf.reshape(2, rows // 2, 128)
    keep = jnp.where(low_bit == 0, halves[0], halves[1])
    give = jnp.where(low_bit == 0, halves[1], halves[0])
    got = lax.ppermute(give.astype(jnp.bfloat16), axis, pair_near)
    summed = (keep + got.astype(jnp.float32)).reshape(2, rows // 4, 128)
    keep = jnp.where(high_bit == 0, summed[0], summed[1])
    give = jnp.where(high_bit == 0, summed[1], summed[0])
    got = lax.ppermute(give.astype(jnp.bfloat16), axis, pair_far)
    own = (keep + got.astype(jnp.float32)).astype(jnp.bfloat16)
    got = lax.ppermute(own, axis, pair_far)
    half = jnp.where(
        high_bit == 0, jnp.concatenate([own, got], axis=0), jnp.concatenate([got, own], axis=0)
    )
    got = lax.ppermute(half, axis, pair_near)
    full = jnp.where(
        low_bit == 0, jnp.concatenate([half, got], axis=0), jnp.concatenate([got, half], axis=0)
    )
    outs = []
    start = 0
    for part in parts:
        width = part.shape[1] // 128
        rows_here = part.shape[0]
        cols = [full[start + k * rows_here : start + (k + 1) * rows_here] for k in range(width)]
        start += width * rows_here
        outs.append(jnp.concatenate(cols, axis=1) if width > 1 else cols[0])
    return outs


def norm_rows(inputs, gains):
    row_mean = jnp.mean(inputs, axis=-1, keepdims=True)
    centred = inputs - row_mean
    variance = jnp.mean(centred * centred, axis=-1, keepdims=True)
    return centred * lax.rsqrt(variance + EPSILON) * gains


def norm_back(inputs, gains, cotangent):
    row_mean = jnp.mean(inputs, axis=-1, keepdims=True)
    centred = inputs - row_mean
    variance = jnp.mean(centred * centred, axis=-1, keepdims=True)
    inverse = lax.rsqrt(variance + EPSILON)
    standard = centred * inverse
    scaled = cotangent * gains
    return inverse * (
        scaled
        - jnp.mean(scaled, axis=-1, keepdims=True)
        - standard * jnp.mean(scaled * standard, axis=-1, keepdims=True)
    )


def attend_local(queries, key_block, value_block, bias_block, valid_keys, scaling):
    scores = (
        jnp.einsum("bqhd,bkhd->bhqk", queries, key_block, preferred_element_type=jnp.float32)
        * scaling
        + bias_block
    )
    scores = jnp.where(valid_keys[:, None, None, :], scores, -jnp.inf)
    row_max = jnp.max(scores, axis=-1, keepdims=True)
    exponent = jnp.exp(scores - row_max)
    weights = exponent / jnp.sum(exponent, axis=-1, keepdims=True)
    weights_low = weights.astype(jnp.bfloat16)
    attended = jnp.einsum(
        "bhqk,bkhd->bqhd", weights_low, value_block, preferred_element_type=jnp.float32
    )
    return (weights, weights_low, attended)


def attend_grads(
    weights, weights_low, queries, key_block, value_block, grad_out, row_delta, scaling
):
    weight_grad = jnp.einsum(
        "bqhd,bkhd->bhqk", grad_out, value_block, preferred_element_type=jnp.float32
    )
    dscore = weights * (weight_grad - row_delta[..., None])
    dscore_low = dscore.astype(jnp.bfloat16)
    dquery = (
        jnp.einsum("bhqk,bkhd->bqhd", dscore_low, key_block, preferred_element_type=jnp.float32)
        * scaling
    )
    key_grad = (
        jnp.einsum("bhqk,bqhd->bkhd", dscore_low, queries, preferred_element_type=jnp.float32)
        * scaling
    )
    dvalue = jnp.einsum(
        "bhqk,bqhd->bkhd", weights_low, grad_out, preferred_element_type=jnp.float32
    )
    return (dscore_low, dquery, key_grad, dvalue)


def body(
    single,
    atoms,
    gain_single,
    gain_atom,
    w_token,
    w_token_out,
    w_cond,
    w_atom,
    w_atom_out,
    pair_bias,
    atom_bias,
    used_blocks,
    used_count,
    atom_counts,
    key_offset,
    grad_token,
    grad_atom,
):
    device = lax.axis_index("seq")
    shards = lax.axis_size("seq")
    tok_rows = single.shape[0]
    blocks_here = tok_rows // BLK
    local_heads = w_token.shape[2] // DH
    features = local_heads * DH
    scaling = DH ** (-0.5)
    normed_low = norm_rows(single.astype(jnp.float32), gain_single).astype(jnp.bfloat16)
    projected = [
        jnp.dot(normed_low, w_token[which], preferred_element_type=jnp.float32)
        for which in range(4)
    ]
    queries = projected[0].astype(jnp.bfloat16)
    gate_act = jax.nn.sigmoid(projected[3])
    key_value = jnp.concatenate(
        [projected[1].astype(jnp.bfloat16), projected[2].astype(jnp.bfloat16)], axis=1
    )
    w_atom_all, w_atom_out_all, atom_bias_all = (w_atom, w_atom_out, atom_bias)
    atom_rows = atoms.shape[0]
    heads_atom = w_atom_all.shape[2] // DA
    atom_feat = heads_atom * DA
    halo_rows = AK // 2
    windows_here = atom_rows // AQ
    group_span = AK // AQ + 1
    slab_rows = group_span * AQ
    atom_scaling = DA ** (-0.5)
    normed_atoms = norm_rows(atoms.astype(jnp.float32), gain_atom)
    counts = atom_counts[0]
    ends = jnp.cumsum(counts)
    atom_place = jnp.arange(atom_rows, dtype=jnp.int32)
    token_local = jnp.sum((ends[None, :] <= atom_place[:, None]).astype(jnp.int32), axis=1)
    token_pick = (token_local[:, None] == jnp.arange(tok_rows, dtype=jnp.int32)[None, :]).astype(
        jnp.float32
    )
    condition = jnp.dot(normed_low, w_cond, preferred_element_type=jnp.float32)
    atom_input = (normed_atoms + jnp.take(condition, token_local, axis=0)).astype(
        jnp.bfloat16
    )
    atom_proj = [
        jnp.dot(atom_input, w_atom_all[which], preferred_element_type=jnp.float32)
        for which in range(4)
    ]
    atom_gate = jax.nn.sigmoid(atom_proj[3])
    atom_kv = jnp.concatenate(
        [atom_proj[1].astype(jnp.bfloat16), atom_proj[2].astype(jnp.bfloat16)], axis=1
    )
    extended = extended_2(atom_kv, (("seq", 0),), halo_rows)
    key_value, extended = lax.optimization_barrier((key_value, extended))
    owner_dev = used_blocks // blocks_here
    relative = jnp.mod(owner_dev - device, shards)
    relative = jnp.where(relative > shards // 2, relative - shards, relative)
    pieces = [key_value for distance in range(-WIN, WIN + 1)]
    for distance in range(-WIN, WIN + 1):
        if distance != 0:
            pieces[distance + WIN] = shifted(key_value, "seq", -distance)
    window = jnp.stack(pieces)
    candidates = (2 * WIN + 1) * blocks_here
    window_flat = window.reshape(candidates, BLK * 2 * features)
    picked = (relative + WIN) * blocks_here + used_blocks % blocks_here
    selector_mask = picked[:, :, None] == jnp.arange(candidates, dtype=jnp.int32)[None, None, :]
    selector = selector_mask.astype(jnp.bfloat16)
    stashed = jnp.einsum(
        "bsc,cx->bsx", selector, window_flat, preferred_element_type=jnp.float32
    ).astype(jnp.bfloat16)
    stashed = stashed.reshape(blocks_here, S, BLK, 2 * features)
    key_blocks = stashed[..., :features].reshape(blocks_here, S * BLK, local_heads, DH)
    value_blocks = stashed[..., features:].reshape(blocks_here, S * BLK, local_heads, DH)
    query_blocks = queries.reshape(blocks_here, BLK, local_heads, DH)
    bias_blocks = (
        pair_bias.reshape(local_heads, blocks_here, BLK, S * BLK)
        .transpose(1, 0, 2, 3)
        .astype(jnp.float32)
    )
    valid_keys = jnp.repeat(
        jnp.arange(S, dtype=jnp.int32)[None, :] < used_count[:, None], BLK, axis=1
    )
    weights, weights_low, attended = attend_local(
        query_blocks, key_blocks, value_blocks, bias_blocks, valid_keys, scaling
    )
    attended = attended.reshape(tok_rows, features)
    token_part = jnp.dot(
        (attended * gate_act).astype(jnp.bfloat16), w_token_out, preferred_element_type=jnp.float32
    )
    grad_gated = jnp.dot(grad_token, w_token_out.T, preferred_element_type=jnp.float32)
    grad_attended = (grad_gated * gate_act).astype(jnp.bfloat16)
    grad_gate = (grad_gated * attended * gate_act * (1.0 - gate_act)).astype(jnp.bfloat16)
    row_delta = jnp.sum(
        (grad_attended.astype(jnp.float32) * attended).reshape(blocks_here, BLK, local_heads, DH),
        axis=-1,
    ).transpose(0, 2, 1)
    score_low, dquery, key_grad, dvalue = attend_grads(
        weights,
        weights_low,
        query_blocks,
        key_blocks,
        value_blocks,
        grad_attended.reshape(blocks_here, BLK, local_heads, DH),
        row_delta,
        scaling,
    )
    grad_pair = score_low.transpose(1, 0, 2, 3).reshape(local_heads, tok_rows, S * BLK)
    returned = jnp.concatenate(
        [
            key_grad.reshape(blocks_here, S, BLK, features),
            dvalue.reshape(blocks_here, S, BLK, features),
        ],
        axis=-1,
    )
    returned_flat = returned.reshape(blocks_here, S, BLK * 2 * features)
    outgoing = jnp.einsum(
        "bsc,bsx->cx", selector_mask.astype(jnp.float32), returned_flat, precision=ONE_HOT_PRECISION
    )
    outgoing = outgoing.reshape(2 * WIN + 1, tok_rows, 2 * features)
    collected = outgoing[WIN]
    for distance in range(-WIN, WIN + 1):
        if distance != 0:
            collected = collected + shifted(
                outgoing[distance + WIN].astype(jnp.bfloat16), "seq", distance
            ).astype(jnp.float32)
    token_grads = [
        dquery.reshape(tok_rows, features).astype(jnp.bfloat16),
        collected[:, :features].astype(jnp.bfloat16),
        collected[:, features:].astype(jnp.bfloat16),
        grad_gate,
    ]
    ext_groups = extended.reshape(windows_here + AK // AQ, AQ, 2 * atom_feat)
    slabs = jnp.concatenate(
        [ext_groups[step : step + windows_here] for step in range(group_span)], axis=1
    )
    shift_here = key_offset + halo_rows
    placer_mask = (
        jnp.arange(slab_rows, dtype=jnp.int32)[None, None, :]
        == jnp.arange(AK, dtype=jnp.int32)[None, :, None] + shift_here[:, None, None]
    )
    window_kv = jnp.einsum(
        "wrs,wsf->wrf", placer_mask.astype(jnp.bfloat16), slabs, preferred_element_type=jnp.float32
    ).astype(jnp.bfloat16)
    atom_keys = window_kv[..., :atom_feat].reshape(windows_here, AK, heads_atom, DA)
    atom_values = window_kv[..., atom_feat:].reshape(windows_here, AK, heads_atom, DA)
    atom_queries = atom_proj[0].astype(jnp.bfloat16).reshape(windows_here, AQ, heads_atom, DA)
    atom_bias_blocks = (
        atom_bias_all.reshape(heads_atom, windows_here, AQ, AK)
        .transpose(1, 0, 2, 3)
        .astype(jnp.float32)
    )
    all_valid = jnp.ones((windows_here, AK), dtype=bool)
    aweights, aweights_low, atom_attended = attend_local(
        atom_queries, atom_keys, atom_values, atom_bias_blocks, all_valid, atom_scaling
    )
    atom_attended = atom_attended.reshape(atom_rows, atom_feat)
    atom_part = jnp.dot(
        (atom_attended * atom_gate).astype(jnp.bfloat16),
        w_atom_out_all,
        preferred_element_type=jnp.float32,
    )
    agrad_gated = jnp.dot(grad_atom, w_atom_out_all.T, preferred_element_type=jnp.float32)
    agrad_attended = (agrad_gated * atom_gate).astype(jnp.bfloat16)
    agrad_gate = (agrad_gated * atom_attended * atom_gate * (1.0 - atom_gate)).astype(jnp.bfloat16)
    atom_delta = jnp.sum(
        (agrad_attended.astype(jnp.float32) * atom_attended).reshape(
            windows_here, AQ, heads_atom, DA
        ),
        axis=-1,
    ).transpose(0, 2, 1)
    ascore_low, aquery_grad, akey_grad, avalue_grad = attend_grads(
        aweights,
        aweights_low,
        atom_queries,
        atom_keys,
        atom_values,
        agrad_attended.reshape(windows_here, AQ, heads_atom, DA),
        atom_delta,
        atom_scaling,
    )
    grad_abias = ascore_low.transpose(1, 0, 2, 3).reshape(heads_atom, atom_rows, AK)
    spread_grads = jnp.concatenate(
        [
            akey_grad.reshape(windows_here, AK, atom_feat),
            avalue_grad.reshape(windows_here, AK, atom_feat),
        ],
        axis=-1,
    )
    slab_grads = jnp.einsum(
        "wrs,wrf->wsf", placer_mask.astype(jnp.float32), spread_grads, precision=ONE_HOT_PRECISION
    )
    slab_grads = slab_grads.reshape(windows_here, group_span, AQ, 2 * atom_feat)
    ext_grad = jnp.pad(slab_grads[:, 0], ((0, group_span - 1), (0, 0), (0, 0)))
    for step in range(1, group_span):
        ext_grad = ext_grad + jnp.pad(
            slab_grads[:, step], ((step, group_span - 1 - step), (0, 0), (0, 0))
        )
    ext_grad = ext_grad.reshape(atom_rows + 2 * halo_rows, 2 * atom_feat)
    rims = jnp.concatenate([ext_grad[:halo_rows], ext_grad[atom_rows + halo_rows :]], axis=0)
    edges = extended_2(rims.astype(jnp.bfloat16), (("seq", 0),), halo_rows).astype(rims.dtype)
    own_grad = ext_grad[halo_rows : halo_rows + atom_rows]
    own_grad = jnp.concatenate(
        [
            own_grad[:halo_rows] + edges[:halo_rows],
            own_grad[halo_rows : atom_rows - halo_rows],
            own_grad[atom_rows - halo_rows :] + edges[3 * halo_rows :],
        ],
        axis=0,
    )
    atom_grads = [
        aquery_grad.reshape(atom_rows, atom_feat).astype(jnp.bfloat16),
        own_grad[:, :atom_feat].astype(jnp.bfloat16),
        own_grad[:, atom_feat:].astype(jnp.bfloat16),
        agrad_gate,
    ]
    agrad_input = jnp.dot(atom_grads[0], w_atom_all[0].T, preferred_element_type=jnp.float32)
    for which in range(1, 4):
        agrad_input = agrad_input + jnp.dot(
            atom_grads[which], w_atom_all[which].T, preferred_element_type=jnp.float32
        )
    atoms_part = norm_back(atoms.astype(jnp.float32), gain_atom, agrad_input)
    cond_grad = jnp.dot(token_pick.T, agrad_input, precision=ONE_HOT_PRECISION)
    cond_term = jnp.dot(cond_grad, w_cond.astype(jnp.float32).T, precision=ONE_HOT_PRECISION)
    grad_normed = cond_term
    for which in range(4):
        grad_normed = grad_normed + jnp.dot(
            token_grads[which], w_token[which].T, preferred_element_type=jnp.float32
        )
    single_part = norm_back(single.astype(jnp.float32), gain_single, grad_normed)
    token_total, atom_total, single_total, atoms_total = head_sum(
        [token_part, atom_part, single_part, atoms_part], "head"
    )
    return (
        token_total.astype(jnp.bfloat16),
        atom_total.astype(jnp.bfloat16),
        single_total.astype(jnp.bfloat16),
        atoms_total.astype(jnp.bfloat16),
        grad_pair,
        grad_abias,
    )


def solution(mesh):
    return jax.shard_map(
        body,
        mesh=mesh,
        in_specs=(
            P("seq", None),
            P("seq", None),
            P(),
            P(),
            P(None, None, "head"),
            P("head", None),
            P(),
            P(None, None, "head"),
            P("head", None),
            P("head", "seq", None),
            P("head", "seq", None),
            P("seq", None),
            P("seq"),
            P("seq", None),
            P("seq"),
            P("seq", None),
            P("seq", None),
        ),
        out_specs=(
            P("seq", None),
            P("seq", None),
            P("seq", None),
            P("seq", None),
            P("head", "seq", None),
            P("head", "seq", None),
        ),
        check_vma=False,
    )
```

```python
import jax
import jax.numpy as jnp
from jax import lax
from jax.sharding import PartitionSpec as P

DH = 24
DA = 32
BLK = 128
S = 4
WIN = 2
AQ = 32
AK = 128


EPSILON = 1e-05
ONE_HOT_PRECISION = lax.Precision.HIGH


def shifted(block, axis, distance):
    devices = range(lax.axis_size(axis))
    route = [((i - distance) % len(devices), i) for i in devices]
    return lax.ppermute(block, axis, route)


def extended_2(block, sides, width):
    for axis, dim in sides:
        count = lax.axis_size(axis)
        forward = [(i, i + 1) for i in range(count - 1)]
        forward.append((count - 1, 0))
        backward = [(target, source) for source, target in forward]
        low = lax.ppermute(
            lax.slice_in_dim(block, block.shape[dim] - width, None, axis=dim), axis, forward
        )
        high = lax.ppermute(lax.slice_in_dim(block, 0, width, axis=dim), axis, backward)
        block = jnp.concatenate([low, block, high], axis=dim)
    return block


def head_sum(parts, axis):
    count = lax.axis_size(axis)
    if count != 4:
        return [lax.psum(p.astype(jnp.bfloat16), axis) for p in parts]
    pieces = []
    for part in parts:
        for col in range(part.shape[1] // 128):
            pieces.append(part[:, col * 128 : (col + 1) * 128])
    buf = jnp.concatenate(pieces, axis=0).astype(jnp.bfloat16)
    rows = buf.shape[0]
    place = lax.axis_index(axis)
    low_bit = place % 2
    high_bit = (place // 2) % 2
    pair_near = [(i, i ^ 1) for i in range(count)]
    pair_far = [(i, i ^ 2) for i in range(count)]
    halves = buf.reshape(2, rows // 2, 128)
    keep = jnp.where(low_bit == 0, halves[0], halves[1])
    give = jnp.where(low_bit == 0, halves[1], halves[0])
    got = lax.ppermute(give.astype(jnp.bfloat16), axis, pair_near)
    summed = (keep.astype(jnp.float32) + got.astype(jnp.float32)).reshape(2, rows // 4, 128)
    keep = jnp.where(high_bit == 0, summed[0], summed[1])
    give = jnp.where(high_bit == 0, summed[1], summed[0])
    got = lax.ppermute(give.astype(jnp.bfloat16), axis, pair_far)
    own = (keep + got.astype(jnp.float32)).astype(jnp.bfloat16)
    got = lax.ppermute(own, axis, pair_far)
    half = jnp.where(
        high_bit == 0, jnp.concatenate([own, got], axis=0), jnp.concatenate([got, own], axis=0)
    )
    got = lax.ppermute(half, axis, pair_near)
    full = jnp.where(
        low_bit == 0, jnp.concatenate([half, got], axis=0), jnp.concatenate([got, half], axis=0)
    )
    outs = []
    start = 0
    for part in parts:
        width = part.shape[1] // 128
        rows_here = part.shape[0]
        cols = [full[start + k * rows_here : start + (k + 1) * rows_here] for k in range(width)]
        start += width * rows_here
        outs.append(jnp.concatenate(cols, axis=1) if width > 1 else cols[0])
    return outs


def norm_rows(inputs, gains):
    row_mean = jnp.mean(inputs, axis=-1, keepdims=True)
    centred = inputs - row_mean
    variance = jnp.mean(centred * centred, axis=-1, keepdims=True)
    return centred * lax.rsqrt(variance + EPSILON) * gains


def norm_back(inputs, gains, cotangent):
    row_mean = jnp.mean(inputs, axis=-1, keepdims=True)
    centred = inputs - row_mean
    variance = jnp.mean(centred * centred, axis=-1, keepdims=True)
    inverse = lax.rsqrt(variance + EPSILON)
    standard = centred * inverse
    scaled = cotangent * gains
    return inverse * (
        scaled
        - jnp.mean(scaled, axis=-1, keepdims=True)
        - standard * jnp.mean(scaled * standard, axis=-1, keepdims=True)
    )


def attend_local(queries, key_block, value_block, bias_block, valid_keys, scaling):
    scores = (
        jnp.einsum("bqhd,bkhd->bhqk", queries, key_block, preferred_element_type=jnp.float32)
        * scaling
        + bias_block
    )
    scores = jnp.where(valid_keys[:, None, None, :], scores, -jnp.inf)
    row_max = jnp.max(scores, axis=-1, keepdims=True)
    exponent = jnp.exp(scores - row_max)
    weights = exponent / jnp.sum(exponent, axis=-1, keepdims=True)
    weights_low = weights.astype(jnp.bfloat16)
    attended = jnp.einsum(
        "bhqk,bkhd->bqhd", weights_low, value_block, preferred_element_type=jnp.float32
    )
    return (weights, weights_low, attended)


def attend_grads(
    weights, weights_low, queries, key_block, value_block, grad_out, row_delta, scaling
):
    weight_grad = jnp.einsum(
        "bqhd,bkhd->bhqk", grad_out, value_block, preferred_element_type=jnp.float32
    )
    dscore = weights * (weight_grad - row_delta[..., None])
    dscore_low = dscore.astype(jnp.bfloat16)
    dquery = (
        jnp.einsum("bhqk,bkhd->bqhd", dscore_low, key_block, preferred_element_type=jnp.float32)
        * scaling
    )
    key_grad = (
        jnp.einsum("bhqk,bqhd->bkhd", dscore_low, queries, preferred_element_type=jnp.float32)
        * scaling
    )
    dvalue = jnp.einsum(
        "bhqk,bqhd->bkhd", weights_low, grad_out, preferred_element_type=jnp.float32
    )
    return (dscore_low, dquery, key_grad, dvalue)


def body(
    single,
    atoms,
    gain_single,
    gain_atom,
    w_token,
    w_token_out,
    w_cond,
    w_atom,
    w_atom_out,
    pair_bias,
    atom_bias,
    used_blocks,
    used_count,
    atom_counts,
    key_offset,
    grad_token,
    grad_atom,
):
    device = lax.axis_index("seq")
    shards = lax.axis_size("seq")
    tok_rows = single.shape[0]
    blocks_here = tok_rows // BLK
    local_heads = w_token.shape[2] // DH
    features = local_heads * DH
    scaling = DH ** (-0.5)
    normed_low = norm_rows(single.astype(jnp.float32), gain_single).astype(jnp.bfloat16)
    projected = [
        jnp.dot(normed_low, w_token[which], preferred_element_type=jnp.float32)
        for which in range(4)
    ]
    queries = projected[0].astype(jnp.bfloat16)
    gate_act = jax.nn.sigmoid(projected[3])
    key_value = jnp.concatenate(
        [projected[1].astype(jnp.bfloat16), projected[2].astype(jnp.bfloat16)], axis=1
    )
    w_atom_all, w_atom_out_all, atom_bias_all = (w_atom, w_atom_out, atom_bias)
    atom_rows = atoms.shape[0]
    heads_atom = w_atom_all.shape[2] // DA
    atom_feat = heads_atom * DA
    halo_rows = AK // 2
    windows_here = atom_rows // AQ
    group_span = AK // AQ + 1
    slab_rows = group_span * AQ
    atom_scaling = DA ** (-0.5)
    normed_atoms = norm_rows(atoms.astype(jnp.float32), gain_atom)
    counts = atom_counts[0]
    ends = jnp.cumsum(counts)
    atom_place = jnp.arange(atom_rows, dtype=jnp.int32)
    token_local = jnp.sum((ends[None, :] <= atom_place[:, None]).astype(jnp.int32), axis=1)
    token_pick = (token_local[:, None] == jnp.arange(tok_rows, dtype=jnp.int32)[None, :]).astype(
        jnp.float32
    )
    condition = jnp.dot(normed_low, w_cond, preferred_element_type=jnp.float32)
    atom_input = (normed_atoms + jnp.dot(token_pick, condition, precision=ONE_HOT_PRECISION)).astype(
        jnp.bfloat16
    )
    atom_proj = [
        jnp.dot(atom_input, w_atom_all[which], preferred_element_type=jnp.float32)
        for which in range(4)
    ]
    atom_gate = jax.nn.sigmoid(atom_proj[3])
    atom_kv = jnp.concatenate(
        [atom_proj[1].astype(jnp.bfloat16), atom_proj[2].astype(jnp.bfloat16)], axis=1
    )
    extended = extended_2(atom_kv, (("seq", 0),), halo_rows)
    key_value, extended = lax.optimization_barrier((key_value, extended))
    owner_dev = used_blocks // blocks_here
    relative = jnp.mod(owner_dev - device, shards)
    relative = jnp.where(relative > shards // 2, relative - shards, relative)
    pieces = [key_value for distance in range(-WIN, WIN + 1)]
    for distance in range(-WIN, WIN + 1):
        if distance != 0:
            pieces[distance + WIN] = shifted(key_value, "seq", -distance)
    window = jnp.stack(pieces)
    candidates = (2 * WIN + 1) * blocks_here
    window_flat = window.reshape(candidates, BLK * 2 * features)
    picked = (relative + WIN) * blocks_here + used_blocks % blocks_here
    selector_mask = picked[:, :, None] == jnp.arange(candidates, dtype=jnp.int32)[None, None, :]
    selector = selector_mask.astype(jnp.bfloat16)
    stashed = jnp.einsum(
        "bsc,cx->bsx", selector, window_flat, preferred_element_type=jnp.float32
    ).astype(jnp.bfloat16)
    stashed = stashed.reshape(blocks_here, S, BLK, 2 * features)
    key_blocks = stashed[..., :features].reshape(blocks_here, S * BLK, local_heads, DH)
    value_blocks = stashed[..., features:].reshape(blocks_here, S * BLK, local_heads, DH)
    query_blocks = queries.reshape(blocks_here, BLK, local_heads, DH)
    bias_blocks = (
        pair_bias.reshape(local_heads, blocks_here, BLK, S * BLK)
        .transpose(1, 0, 2, 3)
        .astype(jnp.float32)
    )
    valid_keys = jnp.repeat(
        jnp.arange(S, dtype=jnp.int32)[None, :] < used_count[:, None], BLK, axis=1
    )
    weights, weights_low, attended = attend_local(
        query_blocks, key_blocks, value_blocks, bias_blocks, valid_keys, scaling
    )
    attended = attended.reshape(tok_rows, features)
    token_part = jnp.dot(
        (attended * gate_act).astype(jnp.bfloat16), w_token_out, preferred_element_type=jnp.float32
    )
    grad_gated = jnp.dot(grad_token, w_token_out.T, preferred_element_type=jnp.float32)
    grad_attended = (grad_gated * gate_act).astype(jnp.bfloat16)
    grad_gate = (grad_gated * attended * gate_act * (1.0 - gate_act)).astype(jnp.bfloat16)
    row_delta = jnp.sum(
        (grad_attended.astype(jnp.float32) * attended).reshape(blocks_here, BLK, local_heads, DH),
        axis=-1,
    ).transpose(0, 2, 1)
    score_low, dquery, key_grad, dvalue = attend_grads(
        weights,
        weights_low,
        query_blocks,
        key_blocks,
        value_blocks,
        grad_attended.reshape(blocks_here, BLK, local_heads, DH),
        row_delta,
        scaling,
    )
    grad_pair = score_low.transpose(1, 0, 2, 3).reshape(local_heads, tok_rows, S * BLK)
    returned = jnp.concatenate(
        [
            key_grad.reshape(blocks_here, S, BLK, features),
            dvalue.reshape(blocks_here, S, BLK, features),
        ],
        axis=-1,
    )
    returned_flat = returned.reshape(blocks_here, S, BLK * 2 * features)
    outgoing = jnp.einsum(
        "bsc,bsx->cx", selector_mask.astype(jnp.float32), returned_flat, precision=ONE_HOT_PRECISION
    )
    outgoing = outgoing.reshape(2 * WIN + 1, tok_rows, 2 * features)
    collected = outgoing[WIN]
    for distance in range(-WIN, WIN + 1):
        if distance != 0:
            collected = collected + shifted(
                outgoing[distance + WIN].astype(jnp.bfloat16), "seq", distance
            ).astype(jnp.float32)
    token_grads = [
        dquery.reshape(tok_rows, features).astype(jnp.bfloat16),
        collected[:, :features].astype(jnp.bfloat16),
        collected[:, features:].astype(jnp.bfloat16),
        grad_gate,
    ]
    ext_groups = extended.reshape(windows_here + AK // AQ, AQ, 2 * atom_feat)
    slabs = jnp.concatenate(
        [ext_groups[step : step + windows_here] for step in range(group_span)], axis=1
    )
    shift_here = key_offset + halo_rows
    placer_mask = (
        jnp.arange(slab_rows, dtype=jnp.int32)[None, None, :]
        == jnp.arange(AK, dtype=jnp.int32)[None, :, None] + shift_here[:, None, None]
    )
    window_kv = jnp.einsum(
        "wrs,wsf->wrf", placer_mask.astype(jnp.bfloat16), slabs, preferred_element_type=jnp.float32
    ).astype(jnp.bfloat16)
    atom_keys = window_kv[..., :atom_feat].reshape(windows_here, AK, heads_atom, DA)
    atom_values = window_kv[..., atom_feat:].reshape(windows_here, AK, heads_atom, DA)
    atom_queries = atom_proj[0].astype(jnp.bfloat16).reshape(windows_here, AQ, heads_atom, DA)
    atom_bias_blocks = (
        atom_bias_all.reshape(heads_atom, windows_here, AQ, AK)
        .transpose(1, 0, 2, 3)
        .astype(jnp.float32)
    )
    all_valid = jnp.ones((windows_here, AK), dtype=bool)
    aweights, aweights_low, atom_attended = attend_local(
        atom_queries, atom_keys, atom_values, atom_bias_blocks, all_valid, atom_scaling
    )
    atom_attended = atom_attended.reshape(atom_rows, atom_feat)
    atom_part = jnp.dot(
        (atom_attended * atom_gate).astype(jnp.bfloat16),
        w_atom_out_all,
        preferred_element_type=jnp.float32,
    )
    agrad_gated = jnp.dot(grad_atom, w_atom_out_all.T, preferred_element_type=jnp.float32)
    agrad_attended = (agrad_gated * atom_gate).astype(jnp.bfloat16)
    agrad_gate = (agrad_gated * atom_attended * atom_gate * (1.0 - atom_gate)).astype(jnp.bfloat16)
    atom_delta = jnp.sum(
        (agrad_attended.astype(jnp.float32) * atom_attended).reshape(
            windows_here, AQ, heads_atom, DA
        ),
        axis=-1,
    ).transpose(0, 2, 1)
    ascore_low, aquery_grad, akey_grad, avalue_grad = attend_grads(
        aweights,
        aweights_low,
        atom_queries,
        atom_keys,
        atom_values,
        agrad_attended.reshape(windows_here, AQ, heads_atom, DA),
        atom_delta,
        atom_scaling,
    )
    grad_abias = ascore_low.transpose(1, 0, 2, 3).reshape(heads_atom, atom_rows, AK)
    spread_grads = jnp.concatenate(
        [
            akey_grad.reshape(windows_here, AK, atom_feat),
            avalue_grad.reshape(windows_here, AK, atom_feat),
        ],
        axis=-1,
    )
    slab_grads = jnp.einsum(
        "wrs,wrf->wsf", placer_mask.astype(jnp.float32), spread_grads, precision=ONE_HOT_PRECISION
    )
    slab_grads = slab_grads.reshape(windows_here, group_span, AQ, 2 * atom_feat)
    ext_grad = jnp.pad(slab_grads[:, 0], ((0, group_span - 1), (0, 0), (0, 0)))
    for step in range(1, group_span):
        ext_grad = ext_grad + jnp.pad(
            slab_grads[:, step], ((step, group_span - 1 - step), (0, 0), (0, 0))
        )
    ext_grad = ext_grad.reshape(atom_rows + 2 * halo_rows, 2 * atom_feat)
    rims = jnp.concatenate([ext_grad[:halo_rows], ext_grad[atom_rows + halo_rows :]], axis=0)
    edges = extended_2(rims.astype(jnp.bfloat16), (("seq", 0),), halo_rows).astype(rims.dtype)
    own_grad = ext_grad[halo_rows : halo_rows + atom_rows]
    own_grad = jnp.concatenate(
        [
            own_grad[:halo_rows] + edges[:halo_rows],
            own_grad[halo_rows : atom_rows - halo_rows],
            own_grad[atom_rows - halo_rows :] + edges[3 * halo_rows :],
        ],
        axis=0,
    )
    atom_grads = [
        aquery_grad.reshape(atom_rows, atom_feat).astype(jnp.bfloat16),
        own_grad[:, :atom_feat].astype(jnp.bfloat16),
        own_grad[:, atom_feat:].astype(jnp.bfloat16),
        agrad_gate,
    ]
    agrad_input = jnp.dot(atom_grads[0], w_atom_all[0].T, preferred_element_type=jnp.float32)
    for which in range(1, 4):
        agrad_input = agrad_input + jnp.dot(
            atom_grads[which], w_atom_all[which].T, preferred_element_type=jnp.float32
        )
    atoms_part = norm_back(atoms.astype(jnp.float32), gain_atom, agrad_input)
    cond_grad = jnp.dot(token_pick.T, agrad_input, precision=ONE_HOT_PRECISION)
    cond_term = jnp.dot(cond_grad, w_cond.astype(jnp.float32).T, precision=ONE_HOT_PRECISION)
    grad_normed = cond_term
    for which in range(4):
        grad_normed = grad_normed + jnp.dot(
            token_grads[which], w_token[which].T, preferred_element_type=jnp.float32
        )
    single_part = norm_back(single.astype(jnp.float32), gain_single, grad_normed)
    token_total, atom_total, single_total, atoms_total = head_sum(
        [token_part, atom_part, single_part, atoms_part], "head"
    )
    return (
        token_total.astype(jnp.bfloat16),
        atom_total.astype(jnp.bfloat16),
        single_total.astype(jnp.bfloat16),
        atoms_total.astype(jnp.bfloat16),
        grad_pair,
        grad_abias,
    )


def solution(mesh):
    return jax.shard_map(
        body,
        mesh=mesh,
        in_specs=(
            P("seq", None),
            P("seq", None),
            P(),
            P(),
            P(None, None, "head"),
            P("head", None),
            P(),
            P(None, None, "head"),
            P("head", None),
            P("head", "seq", None),
            P("head", "seq", None),
            P("seq", None),
            P("seq"),
            P("seq", None),
            P("seq"),
            P("seq", None),
            P("seq", None),
        ),
        out_specs=(
            P("seq", None),
            P("seq", None),
            P("seq", None),
            P("seq", None),
            P("head", "seq", None),
            P("head", "seq", None),
        ),
        check_vma=False,
    )
```
